32 devices in a mesh: groups: 2 (over y), tiles: 4 (over z), bins: 2 (over x), vert: 2 (over core).
Axes of the slice: x: 2, y: 2, z: 4, core: 2. Of those that a mesh axis runs over, the one named last changes fastest.
Arguments:
- bin_mass: float32 [264, 32, 16, 128], P('bins', ('groups', 'tiles'), 'vert'), parts along dimension 1, may hold values from 0.25 to 4
- wind_east: float32 [32, 16, 128], P(('groups', 'tiles'), 'vert'), parts along dimension 0, may hold values from -0.7 to 0.7
- wind_north: float32 [32, 16, 128], P(('groups', 'tiles'), 'vert'), parts along dimension 0, may hold values from -0.3 to 0.3
- supersaturation: float32 [32, 16, 128], P(('groups', 'tiles'), 'vert'), parts along dimension 0, may hold values from -4 to 4
- potential_temp: float32 [32, 16, 128], P(('groups', 'tiles'), 'vert'), parts along dimension 0, may hold values from -6 to 6
- terrain_height: int32 [32, 128], P(('groups', 'tiles')), parts along dimension 0, may hold values from 0 to 3
- fall_speed: float32 [264], P('bins'), may hold values from 0.05 to 0.9
- growth_rate: float32 [264], P('bins'), may hold values from 0.05 to 0.5
- latent_factor: float32 [264], P('bins'), may hold values from 0.3 to 3
- bin_order: int32 [264], replicated, may hold values from 0 to 263, each once
- kernel_index: int32 [8, 8], replicated, may hold values from 0 to 3
- collision_kernels: bfloat16 [4, 33, 33], replicated, may hold values from -0.375 to 0.375
Outputs:
- mass_next: float32 [264, 32, 16, 128], P('bins', ('groups', 'tiles'), 'vert'), parts along dimension 1
- temp_next: float32 [32, 16, 128], P(('groups', 'tiles'), 'vert'), parts along dimension 0
- vapor_next: float32 [32, 16, 128], P(('groups', 'tiles'), 'vert'), parts along dimension 0
The draws below stay inside these ranges and needn't reach their ends.
There are 2 independent parts, one for each index of `groups`. The reference program is written for one: setup_inputs(seed, part) draws one part's arguments, and reference() takes and returns one part's arrays. A program takes and returns all parts, laid end to end along the dimension named above; an argument that names none is the same for every part. Nothing has to cross between parts.
Inputs may be any that keep to these rules, and one draw needn't show every extreme that they name: `bin_order`: each bin number appears once.
All inputs are finite; a program needn't handle non-finite values.
Results may differ from the reference program's by a relative error of at most 0.0021.
Values may be sent and summed in bfloat16 or wider, within the bound.
No kernel may reach another device: no remote copies, remote signals or barrier semaphores. Data moves between devices by JAX's collectives and lax.ppermute only.
A program may use at most 64 MiB of HBM per device.

```python
import math
import jax
import jax.numpy as jnp
from jax import lax

NB = 33
CLASSES = 8
NK = 4
SUB = 8
NY = 128
BINS = 264
NX = 16
NZ = 16


def draw_wind_east(key, part):
    key_sign = jax.random.fold_in(key, 11)
    key_flip = jax.random.fold_in(key, 12)
    key_magnitude = jax.random.fold_in(key, 13)
    column_bits = jax.random.randint(key_sign, (NZ, NY), 0, 2)
    column_sign = (1 - 2 * column_bits).astype(jnp.float32)
    flip_draw = jax.random.randint(key_flip, (NX,), 0, 8)
    parity = jnp.cumsum((flip_draw == 0).astype(jnp.int32)) % 2
    row_sign = (1 - 2 * parity).astype(jnp.float32)
    magnitude = jax.random.uniform(key_magnitude, (NX, NZ, NY), jnp.float32, 0.35, 0.7)
    return magnitude * row_sign[:, None, None] * column_sign[None, :, :]


def with_ends(entries, stream_key, smallest, largest):
    longest = entries.shape.index(max(entries.shape))
    spots = []
    for shift in (0, 1):
        where = [jax.random.randint(jax.random.fold_in(stream_key, axis), (), 0, length) for axis, length in enumerate(entries.shape)]
        where[longest] = (where[longest] + shift) % entries.shape[longest]
        spots.append(tuple(where))
    return entries.at[spots[0]].set(smallest).at[spots[1]].set(largest)


def block_scale(rng, dims, shards, least, high):
    level, own = 1.0, jax.random.fold_in(rng, 6)
    for position, blocks in shards:
        steps = jnp.exp(jax.random.uniform(jax.random.fold_in(own, position), (blocks,), jnp.float32, least / len(shards), high / len(shards)))
        level = level * jnp.repeat(steps, dims[position] // blocks).reshape([-1 if axis == position else 1 for axis in range(len(dims))])
    return level


def gaussian(key, shape, spread, bound, split=(), kind=jnp.bfloat16):
    values = spread * jax.random.normal(key, shape, jnp.float32)
    if split:
        values = values * block_scale(key, shape, split, -0.22, 0.18)
    return jnp.clip(values, -bound, bound).astype(kind)


def setup_inputs(seed: int = 0, part: int = 0) -> dict:
    keys = jax.random.split(jax.random.key(seed), 13)
    own_keys = jax.random.split(jax.random.fold_in(keys[12], part), 13)
    bin_mass = jnp.clip(jnp.exp(math.log(4.0) - 2.7725887 * jax.random.uniform(own_keys[0], (BINS, NX, NZ, NY), jnp.float32) ** block_scale(own_keys[0], (BINS, NX, NZ, NY), ((0, 2), (1, 4), (2, 2)), -0.2, 0.2)), 0.25, 4.0)
    wind_east = draw_wind_east(jax.random.fold_in(jax.random.fold_in(keys[12], part), 71), part)
    wind_north = jnp.clip(jax.random.uniform(own_keys[2], (NX, NZ, NY), jnp.float32, -0.3, 0.3) * block_scale(own_keys[2], (NX, NZ, NY), ((0, 4), (1, 2)), -0.4, 0.0), -0.3, 0.3)
    supersaturation = gaussian(own_keys[3], (NX, NZ, NY), 1.0, 4.0, ((0, 4), (1, 2)), jnp.float32)
    potential_temp = gaussian(own_keys[4], (NX, NZ, NY), 1.0, 6.0, ((0, 4), (1, 2)), jnp.float32)
    terrain_height = with_ends(jax.random.randint(own_keys[5], (NX, NY), 0, 4), jax.random.fold_in(own_keys[5], 1), 0, 3).astype(jnp.int32)
    fall_speed = jnp.clip(jnp.exp(math.log(0.9) - 2.8903717 * jax.random.uniform(keys[6], (BINS,), jnp.float32) ** block_scale(keys[6], (BINS,), ((0, 2),), -0.2, 0.2)), 0.05, 0.9)
    growth_rate = jnp.clip(jnp.exp(math.log(0.5) - 2.3025851 * jax.random.uniform(keys[7], (BINS,), jnp.float32) ** block_scale(keys[7], (BINS,), ((0, 2),), -0.2, 0.2)), 0.05, 0.5)
    latent_factor = jnp.clip(jnp.exp(math.log(3.0) - 2.3025851 * jax.random.uniform(keys[8], (BINS,), jnp.float32) ** block_scale(keys[8], (BINS,), ((0, 2),), -0.2, 0.2)), 0.3, 3.0)
    bin_order = jax.random.permutation(keys[9], BINS).astype(jnp.int32)
    kernel_index = with_ends(jax.random.randint(keys[10], (CLASSES, CLASSES), 0, NK), jax.random.fold_in(keys[10], 1), 0, NK - 1).astype(jnp.int32)
    collision_kernels = gaussian(keys[11], (NK, NB, NB), BINS ** -0.5, 0.375)
    return {"bin_mass": bin_mass, "wind_east": wind_east, "wind_north": wind_north, "supersaturation": supersaturation, "potential_temp": potential_temp, "terrain_height": terrain_height, "fall_speed": fall_speed, "growth_rate": growth_rate, "latent_factor": latent_factor, "bin_order": bin_order, "kernel_index": kernel_index, "collision_kernels": collision_kernels}


collision_rate = 0.001
condense_rate = 0.02
heating_gain = 0.03
growth_gain = 0.5


def tendency(center_cells, left_cells, right_cells, wind_x, wind_y):
    south_cells = jnp.roll(center_cells, 1, axis=3)
    north_cells = jnp.roll(center_cells, -1, axis=3)
    along_x = jnp.maximum(wind_x, 0.0) * (center_cells - left_cells) + jnp.minimum(wind_x, 0.0) * (right_cells - center_cells)
    along_y = jnp.maximum(wind_y, 0.0) * (center_cells - south_cells) + jnp.minimum(wind_y, 0.0) * (north_cells - center_cells)
    return -along_x - along_y


def coupling_table(bin_order, kernel_index, collision_kernels):
    bin_class = bin_order // NB
    bin_within = bin_order % NB
    chosen = kernel_index[bin_class[:, None], bin_class[None, :]]
    coupling = collision_kernels[chosen, bin_within[:, None], bin_within[None, :]]
    same_class = (bin_class[:, None] == bin_class[None, :]).astype(jnp.bfloat16)
    return jnp.concatenate([coupling, same_class], axis=0)


def reference(bin_mass, wind_east, wind_north, supersaturation, potential_temp, terrain_height, fall_speed, growth_rate, latent_factor, bin_order, kernel_index, collision_kernels):
    levels = lax.iota(jnp.int32, NZ)
    open_cells = (levels[None, :, None] >= terrain_height[:, None, :]).astype(jnp.float32)
    wind_x = wind_east * open_cells
    wind_y = wind_north * open_cells
    section_field = bin_mass
    for weight_now in (1.0 / 3.0, 0.5, 1.0):
        extended = jnp.pad(section_field, ((0, 0), (1, 1), (0, 0), (0, 0)))
        section_field = bin_mass + weight_now * tendency(extended[:, 1:-1], extended[:, :-2], extended[:, 2:], wind_x, wind_y)
    from_above = jnp.concatenate([section_field[:, :, 1:], jnp.zeros_like(section_field[:, :, :1])], axis=2)
    speed = fall_speed[:, None, None, None]
    settled = (1.0 - speed) * section_field + speed * from_above
    growth = growth_rate[:, None, None, None]
    uptake = jnp.sum(growth * settled, axis=0)
    heating = jnp.sum(latent_factor[:, None, None, None] * growth * settled, axis=0)
    midway = supersaturation * jnp.exp(-0.5 * condense_rate * uptake)
    grown = settled * (1.0 + growth_gain * growth * midway)
    temp_next = potential_temp + heating_gain * midway * heating
    vapor_next = supersaturation * jnp.exp(-condense_rate * uptake)
    table = coupling_table(bin_order, kernel_index, collision_kernels)
    start = lax.optimization_barrier(grown.astype(jnp.bfloat16))
    planes = jnp.moveaxis(start, 1, 0).reshape(NX, BINS, NZ * NY)

    def collide(plane):
        first = plane.astype(jnp.float32)
        iterate = first
        for substep in range(SUB):
            products = jnp.dot(table, iterate.astype(jnp.bfloat16), preferred_element_type=jnp.float32)
            iterate = iterate + collision_rate * products[BINS:] * products[:BINS]
        return (iterate - first).astype(jnp.bfloat16)

    changes = lax.map(collide, planes)
    change = jnp.moveaxis(changes.reshape(NX, BINS, NZ, NY), 0, 1)
    change = lax.optimization_barrier(change).astype(jnp.float32)
    mass_next = (grown + change) * open_cells
    return (mass_next, temp_next, vapor_next)
```

```python
import jax
import jax.numpy as jnp
from jax import lax
from jax.sharding import PartitionSpec as P

SUB = 8


collision_rate = 0.001
condense_rate = 0.02
heating_gain = 0.03
growth_gain = 0.5
highest = lax.Precision.HIGHEST


def extended_2(array, sides, width):
    for axis, dim in sides:
        size, length = (lax.axis_size(axis), array.shape[dim])
        up = [(i, (i + 1) % size) for i in range(size - 1)]
        down = [(j, i) for i, j in up]
        last = lax.slice_in_dim(array, length - width, length, axis=dim)
        first = lax.slice_in_dim(array, 0, width, axis=dim)
        before = lax.ppermute(last, axis, up)
        after = lax.ppermute(first, axis, down)
        array = jnp.concatenate([before, array, after], axis=dim)
    return array


def shifted(block, axis, distance):
    devices = range(lax.axis_size(axis))
    route = [(i - distance, i) for i in devices if i - distance in devices]
    return lax.ppermute(block, axis, route)


def tendency(center_cells, left_cells, right_cells, wind_x, wind_y):
    south_cells = jnp.roll(center_cells, 1, axis=3)
    north_cells = jnp.roll(center_cells, -1, axis=3)
    along_x = jnp.maximum(wind_x, 0.0) * (center_cells - left_cells) + jnp.minimum(wind_x, 0.0) * (
        right_cells - center_cells
    )
    along_y = jnp.maximum(wind_y, 0.0) * (center_cells - south_cells) + jnp.minimum(wind_y, 0.0) * (
        north_cells - center_cells
    )
    return -along_x - along_y


def coupling_table(bin_order, kernel_index, collision_kernels):
    class_count = kernel_index.shape[0]
    table_count = collision_kernels.shape[0]
    class_bins = collision_kernels.shape[1]
    bin_class = bin_order // class_bins
    bin_within = bin_order % class_bins
    kernel_pick = (kernel_index[:, :, None] == lax.iota(jnp.int32, table_count)).astype(jnp.float32)
    block_table = jnp.einsum(
        "ack,kmn->acmn", kernel_pick, collision_kernels.astype(jnp.float32), precision=highest
    )
    class_hot = (bin_class[:, None] == lax.iota(jnp.int32, class_count)).astype(jnp.float32)
    within_hot = (bin_within[:, None] == lax.iota(jnp.int32, class_bins)).astype(jnp.float32)
    row_table = jnp.einsum("bm,acmn->bacn", within_hot, block_table, precision=highest)
    row_table = jnp.einsum("ba,bacn->bcn", class_hot, row_table, precision=highest)
    coupling = jnp.einsum("bcn,dc,dn->bd", row_table, class_hot, within_hot, precision=highest)
    same_class = jnp.dot(class_hot, class_hot.T, precision=highest)
    return jnp.concatenate([coupling, same_class], axis=0).astype(jnp.bfloat16)


def collide(table, first):
    all_bins = table.shape[1]
    iterate = first
    for substep in range(SUB):
        products = jnp.dot(table, iterate.astype(jnp.bfloat16), preferred_element_type=jnp.float32)
        iterate = iterate + collision_rate * products[all_bins:] * products[:all_bins]
    return (iterate - first).astype(jnp.bfloat16)


def spread_collision(grown, bin_order, kernel_index, collision_kernels):
    local_bins, width_x, width_z, width_y = grown.shape
    table = coupling_table(bin_order, kernel_index, collision_kernels)
    all_bins = table.shape[1]
    start = grown.astype(jnp.bfloat16).reshape(local_bins, width_x, width_z * width_y)
    cell_block = lax.all_to_all(start, "bins", split_axis=2, concat_axis=0, tiled=True)
    block_shape = cell_block.shape
    first = cell_block.reshape(all_bins, -1).astype(jnp.float32)
    change = collide(table, first).reshape(block_shape)
    change = lax.all_to_all(change, "bins", split_axis=0, concat_axis=2, tiled=True)
    return change.reshape(local_bins, width_x, width_z, width_y).astype(jnp.float32)


def paired_collision(grown, bin_order, kernel_index, collision_kernels):
    local_bins, width_x, width_z, width_y = grown.shape
    swap = [(0, 1), (1, 0)]
    me = lax.axis_index("bins")
    order = lax.dynamic_slice_in_dim(
        jnp.concatenate([bin_order, bin_order]), me * local_bins, 2 * local_bins
    )
    table = coupling_table(order, kernel_index, collision_kernels)
    halves = grown.astype(jnp.bfloat16).reshape(local_bins, 2, width_x // 2, width_z, width_y)
    own = lax.dynamic_index_in_dim(halves, me, axis=1, keepdims=False)
    away = lax.dynamic_index_in_dim(halves, 1 - me, axis=1, keepdims=False)
    arrived = lax.ppermute(away, "bins", swap)
    first = jnp.concatenate([own, arrived], axis=0).reshape(2 * local_bins, -1).astype(jnp.float32)
    change = collide(table, first).reshape(2 * local_bins, width_x // 2, width_z, width_y)
    back = lax.ppermute(change[local_bins:], "bins", swap)
    pair = jnp.stack([change[:local_bins], back], axis=1)
    pair = jnp.where(me == 0, pair, pair[:, ::-1])
    return pair.reshape(local_bins, width_x, width_z, width_y).astype(jnp.float32)


def body(
    bin_mass,
    wind_east,
    wind_north,
    supersaturation,
    potential_temp,
    terrain_height,
    fall_speed,
    growth_rate,
    latent_factor,
    bin_order,
    kernel_index,
    collision_kernels,
):
    local_bins, width_x, width_z, width_y = bin_mass.shape
    levels = lax.axis_index("vert") * width_z + lax.iota(jnp.int32, width_z)
    open_cells = (levels[None, :, None] >= terrain_height[:, None, :]).astype(jnp.float32)
    wind_x = wind_east * open_cells
    wind_y = wind_north * open_cells
    section_weights = (1.0 / 3.0, 0.5, 1.0)
    section_field = bin_mass
    for weight_now in section_weights:
        extended = extended_2(section_field, (("tiles", 1),), 1)
        section_field = bin_mass + weight_now * tendency(
            extended[:, 1:-1], extended[:, :-2], extended[:, 2:], wind_x, wind_y
        )
    rim_above = shifted(section_field[:, :, :1, :], "vert", -1)
    from_above = jnp.concatenate([section_field[:, :, 1:], rim_above], axis=2)
    speed = fall_speed[:, None, None, None]
    settled = (1.0 - speed) * section_field + speed * from_above
    growth = growth_rate[:, None, None, None]
    partial = (
        jnp.sum(growth * settled, axis=0),
        jnp.sum(latent_factor[:, None, None, None] * growth * settled, axis=0),
    )
    bin_devices = lax.axis_size("bins")
    if bin_devices == 2:
        swap = [(0, 1), (1, 0)]
        other = lax.ppermute(jnp.stack(partial), "bins", swap)
        uptake, heating = partial[0] + other[0], partial[1] + other[1]
    else:
        uptake, heating = lax.psum(partial, "bins")
    midway = supersaturation * jnp.exp(-0.5 * condense_rate * uptake)
    grown = settled * (1.0 + growth_gain * growth * midway)
    temp_next = potential_temp + heating_gain * midway * heating
    vapor_next = supersaturation * jnp.exp(-condense_rate * uptake)
    if bin_devices == 2 and width_x % 2 == 0:
        change = paired_collision(grown, bin_order, kernel_index, collision_kernels)
    else:
        change = spread_collision(grown, bin_order, kernel_index, collision_kernels)
    mass_next = (grown + change) * open_cells
    return (mass_next, temp_next, vapor_next)


def solution(mesh):
    return jax.shard_map(
        body,
        mesh=mesh,
        in_specs=(
            P("bins", ("groups", "tiles"), "vert", None),
            P(("groups", "tiles"), "vert", None),
            P(("groups", "tiles"), "vert", None),
            P(("groups", "tiles"), "vert", None),
            P(("groups", "tiles"), "vert", None),
            P(("groups", "tiles"), None),
            P("bins"),
            P("bins"),
            P("bins"),
            P(),
            P(),
            P(),
        ),
        out_specs=(
            P("bins", ("groups", "tiles"), "vert", None),
            P(("groups", "tiles"), "vert", None),
            P(("groups", "tiles"), "vert", None),
        ),
        check_vma=False,
    )
```

```python
import jax
import jax.numpy as jnp
from jax import lax
from jax.sharding import PartitionSpec as P

SUB = 8


collision_rate = 0.001
condense_rate = 0.02
heating_gain = 0.03
growth_gain = 0.5
highest = lax.Precision.HIGHEST


def extended_2(array, sides, width):
    for axis, dim in sides:
        size, length = (lax.axis_size(axis), array.shape[dim])
        up = [(i, (i + 1) % size) for i in range(size - 1)]
        down = [(j, i) for i, j in up]
        last = lax.slice_in_dim(array, length - width, length, axis=dim)
        first = lax.slice_in_dim(array, 0, width, axis=dim)
        before = lax.ppermute(last, axis, up)
        after = lax.ppermute(first, axis, down)
        array = jnp.concatenate([before, array, after], axis=dim)
    return array


def advect_wide(bin_mass, wind_x, wind_y, section_weights):
    local_bins, width_x = bin_mass.shape[:2]
    depth = len(section_weights)
    tiles = lax.axis_size("tiles")
    up = [(i, i + 1) for i in range(tiles - 1)]
    down = [(j, i) for i, j in up]

    def rim(lo, hi):
        return jnp.concatenate(
            [bin_mass[:, lo:hi], wind_x[None, lo:hi], wind_y[None, lo:hi]], axis=0
        )

    before = lax.ppermute(rim(width_x - depth, width_x), "tiles", up)
    after = lax.ppermute(rim(0, depth), "tiles", down)
    field = jnp.concatenate([before[:local_bins], bin_mass, after[:local_bins]], axis=1)
    wx = jnp.concatenate([before[local_bins], wind_x, after[local_bins]], axis=0)
    wy = jnp.concatenate([before[local_bins + 1], wind_y, after[local_bins + 1]], axis=0)
    section = field
    for stage, weight_now in enumerate(section_weights, start=1):
        span = width_x + 2 * (depth - stage)
        section = field[:, stage : stage + span] + weight_now * tendency(
            section[:, 1 : 1 + span],
            section[:, 0:span],
            section[:, 2 : 2 + span],
            wx[stage : stage + span],
            wy[stage : stage + span],
        )
    return section


def shifted(block, axis, distance):
    devices = range(lax.axis_size(axis))
    route = [(i - distance, i) for i in devices if i - distance in devices]
    return lax.ppermute(block, axis, route)


def tendency(center_cells, left_cells, right_cells, wind_x, wind_y):
    south_cells = jnp.roll(center_cells, 1, axis=3)
    north_cells = jnp.roll(center_cells, -1, axis=3)
    along_x = jnp.maximum(wind_x, 0.0) * (center_cells - left_cells) + jnp.minimum(wind_x, 0.0) * (
        right_cells - center_cells
    )
    along_y = jnp.maximum(wind_y, 0.0) * (center_cells - south_cells) + jnp.minimum(wind_y, 0.0) * (
        north_cells - center_cells
    )
    return -along_x - along_y


def coupling_table(bin_order, kernel_index, collision_kernels):
    class_count = kernel_index.shape[0]
    table_count = collision_kernels.shape[0]
    class_bins = collision_kernels.shape[1]
    bin_class = bin_order // class_bins
    bin_within = bin_order % class_bins
    kernel_pick = (kernel_index[:, :, None] == lax.iota(jnp.int32, table_count)).astype(jnp.float32)
    block_table = jnp.einsum(
        "ack,kmn->acmn", kernel_pick, collision_kernels.astype(jnp.float32), precision=highest
    )
    class_hot = (bin_class[:, None] == lax.iota(jnp.int32, class_count)).astype(jnp.float32)
    within_hot = (bin_within[:, None] == lax.iota(jnp.int32, class_bins)).astype(jnp.float32)
    row_table = jnp.einsum("bm,acmn->bacn", within_hot, block_table, precision=highest)
    row_table = jnp.einsum("ba,bacn->bcn", class_hot, row_table, precision=highest)
    coupling = jnp.einsum("bcn,dc,dn->bd", row_table, class_hot, within_hot, precision=highest)
    same_class = jnp.dot(class_hot, class_hot.T, precision=highest)
    return jnp.concatenate([coupling, same_class], axis=0).astype(jnp.bfloat16)


def collide(table, first):
    all_bins = table.shape[1]
    iterate = first
    for substep in range(SUB):
        products = jnp.dot(table, iterate.astype(jnp.bfloat16), preferred_element_type=jnp.float32)
        iterate = iterate + collision_rate * products[all_bins:] * products[:all_bins]
    return (iterate - first).astype(jnp.bfloat16)


def spread_collision(grown, bin_order, kernel_index, collision_kernels):
    local_bins, width_x, width_z, width_y = grown.shape
    table = coupling_table(bin_order, kernel_index, collision_kernels)
    all_bins = table.shape[1]
    start = grown.astype(jnp.bfloat16).reshape(local_bins, width_x, width_z * width_y)
    cell_block = lax.all_to_all(start, "bins", split_axis=2, concat_axis=0, tiled=True)
    block_shape = cell_block.shape
    first = cell_block.reshape(all_bins, -1).astype(jnp.float32)
    change = collide(table, first).reshape(block_shape)
    change = lax.all_to_all(change, "bins", split_axis=0, concat_axis=2, tiled=True)
    return change.reshape(local_bins, width_x, width_z, width_y).astype(jnp.float32)


def paired_collision(grown, bin_order, kernel_index, collision_kernels):
    local_bins, width_x, width_z, width_y = grown.shape
    swap = [(0, 1), (1, 0)]
    me = lax.axis_index("bins")
    order = lax.dynamic_slice_in_dim(
        jnp.concatenate([bin_order, bin_order]), me * local_bins, 2 * local_bins
    )
    table = coupling_table(order, kernel_index, collision_kernels)
    halves = grown.astype(jnp.bfloat16).reshape(local_bins, 2, width_x // 2, width_z, width_y)
    own = lax.dynamic_index_in_dim(halves, me, axis=1, keepdims=False)
    away = lax.dynamic_index_in_dim(halves, 1 - me, axis=1, keepdims=False)
    arrived = lax.ppermute(away, "bins", swap)
    first = jnp.concatenate([own, arrived], axis=0).reshape(2 * local_bins, -1).astype(jnp.float32)
    change = collide(table, first).reshape(2 * local_bins, width_x // 2, width_z, width_y)
    back = lax.ppermute(change[local_bins:], "bins", swap)
    pair = jnp.stack([change[:local_bins], back], axis=1)
    pair = jnp.where(me == 0, pair, pair[:, ::-1])
    return pair.reshape(local_bins, width_x, width_z, width_y).astype(jnp.float32)


def body(
    bin_mass,
    wind_east,
    wind_north,
    supersaturation,
    potential_temp,
    terrain_height,
    fall_speed,
    growth_rate,
    latent_factor,
    bin_order,
    kernel_index,
    collision_kernels,
):
    local_bins, width_x, width_z, width_y = bin_mass.shape
    levels = lax.axis_index("vert") * width_z + lax.iota(jnp.int32, width_z)
    open_cells = (levels[None, :, None] >= terrain_height[:, None, :]).astype(jnp.float32)
    wind_x = wind_east * open_cells
    wind_y = wind_north * open_cells
    section_weights = (1.0 / 3.0, 0.5, 1.0)
    if width_x >= len(section_weights):
        section_field = advect_wide(bin_mass, wind_x, wind_y, section_weights)
    else:
        section_field = bin_mass
        for weight_now in section_weights:
            extended = extended_2(section_field, (("tiles", 1),), 1)
            section_field = bin_mass + weight_now * tendency(
                extended[:, 1:-1], extended[:, :-2], extended[:, 2:], wind_x, wind_y
            )
    rim_above = shifted(section_field[:, :, :1, :], "vert", -1)
    from_above = jnp.concatenate([section_field[:, :, 1:], rim_above], axis=2)
    speed = fall_speed[:, None, None, None]
    settled = (1.0 - speed) * section_field + speed * from_above
    growth = growth_rate[:, None, None, None]
    partial = (
        jnp.sum(growth * settled, axis=0),
        jnp.sum(latent_factor[:, None, None, None] * growth * settled, axis=0),
    )
    bin_devices = lax.axis_size("bins")
    if bin_devices == 2:
        swap = [(0, 1), (1, 0)]
        other = lax.ppermute(jnp.stack(partial), "bins", swap)
        uptake, heating = partial[0] + other[0], partial[1] + other[1]
    else:
        uptake, heating = lax.psum(partial, "bins")
    midway = supersaturation * jnp.exp(-0.5 * condense_rate * uptake)
    grown = settled * (1.0 + growth_gain * growth * midway)
    temp_next = potential_temp + heating_gain * midway * heating
    vapor_next = supersaturation * jnp.exp(-condense_rate * uptake)
    if bin_devices == 2 and width_x % 2 == 0:
        change = paired_collision(grown, bin_order, kernel_index, collision_kernels)
    else:
        change = spread_collision(grown, bin_order, kernel_index, collision_kernels)
    mass_next = (grown + change) * open_cells
    return (mass_next, temp_next, vapor_next)


def solution(mesh):
    return jax.shard_map(
        body,
        mesh=mesh,
        in_specs=(
            P("bins", ("groups", "tiles"), "vert", None),
            P(("groups", "tiles"), "vert", None),
            P(("groups", "tiles"), "vert", None),
            P(("groups", "tiles"), "vert", None),
            P(("groups", "tiles"), "vert", None),
            P(("groups", "tiles"), None),
            P("bins"),
            P("bins"),
            P("bins"),
            P(),
            P(),
            P(),
        ),
        out_specs=(
            P("bins", ("groups", "tiles"), "vert", None),
            P(("groups", "tiles"), "vert", None),
            P(("groups", "tiles"), "vert", None),
        ),
        check_vma=False,
    )
```

```python
import jax
import jax.numpy as jnp
from jax import lax
from jax.sharding import PartitionSpec as P

SUB = 8


collision_rate = 0.001
condense_rate = 0.02
heating_gain = 0.03
growth_gain = 0.5
highest = lax.Precision.HIGHEST


def extended_2(array, sides, width, link=jnp.float32):
    for axis, dim in sides:
        size, length = (lax.axis_size(axis), array.shape[dim])
        up = [(i, (i + 1) % size) for i in range(size - 1)]
        down = [(j, i) for i, j in up]
        last = lax.slice_in_dim(array, length - width, length, axis=dim)
        first = lax.slice_in_dim(array, 0, width, axis=dim)
        before = lax.ppermute(last.astype(link), axis, up).astype(array.dtype)
        after = lax.ppermute(first.astype(link), axis, down).astype(array.dtype)
        array = jnp.concatenate([before, array, after], axis=dim)
    return array


def shifted(block, axis, distance):
    devices = range(lax.axis_size(axis))
    route = [(i - distance, i) for i in devices if i - distance in devices]
    return lax.ppermute(block, axis, route)


def tendency(center_cells, left_cells, right_cells, wind_x, wind_y):
    south_cells = jnp.roll(center_cells, 1, axis=3)
    north_cells = jnp.roll(center_cells, -1, axis=3)
    along_x = jnp.maximum(wind_x, 0.0) * (center_cells - left_cells) + jnp.minimum(wind_x, 0.0) * (
        right_cells - center_cells
    )
    along_y = jnp.maximum(wind_y, 0.0) * (center_cells - south_cells) + jnp.minimum(wind_y, 0.0) * (
        north_cells - center_cells
    )
    return -along_x - along_y


def coupling_table(bin_order, kernel_index, collision_kernels):
    class_count = kernel_index.shape[0]
    table_count = collision_kernels.shape[0]
    class_bins = collision_kernels.shape[1]
    bin_class = bin_order // class_bins
    bin_within = bin_order % class_bins
    kernel_pick = (kernel_index[:, :, None] == lax.iota(jnp.int32, table_count)).astype(jnp.float32)
    block_table = jnp.einsum(
        "ack,kmn->acmn", kernel_pick, collision_kernels.astype(jnp.float32), precision=highest
    )
    class_hot = (bin_class[:, None] == lax.iota(jnp.int32, class_count)).astype(jnp.float32)
    within_hot = (bin_within[:, None] == lax.iota(jnp.int32, class_bins)).astype(jnp.float32)
    row_table = jnp.einsum("bm,acmn->bacn", within_hot, block_table, precision=highest)
    row_table = jnp.einsum("ba,bacn->bcn", class_hot, row_table, precision=highest)
    coupling = jnp.einsum("bcn,dc,dn->bd", row_table, class_hot, within_hot, precision=highest)
    same_class = jnp.dot(class_hot, class_hot.T, precision=highest)
    return jnp.concatenate([coupling, same_class], axis=0).astype(jnp.bfloat16)


def collide(table, first):
    all_bins = table.shape[1]
    iterate = first
    for substep in range(SUB):
        products = jnp.dot(table, iterate.astype(jnp.bfloat16), preferred_element_type=jnp.float32)
        iterate = iterate + collision_rate * products[all_bins:] * products[:all_bins]
    return (iterate - first).astype(jnp.bfloat16)


def spread_collision(grown, bin_order, kernel_index, collision_kernels):
    local_bins, width_x, width_z, width_y = grown.shape
    table = coupling_table(bin_order, kernel_index, collision_kernels)
    all_bins = table.shape[1]
    start = grown.astype(jnp.bfloat16).reshape(local_bins, width_x, width_z * width_y)
    cell_block = lax.all_to_all(start, "bins", split_axis=2, concat_axis=0, tiled=True)
    block_shape = cell_block.shape
    first = cell_block.reshape(all_bins, -1).astype(jnp.float32)
    change = collide(table, first).reshape(block_shape)
    change = lax.all_to_all(change, "bins", split_axis=0, concat_axis=2, tiled=True)
    return change.reshape(local_bins, width_x, width_z, width_y).astype(jnp.float32)


def paired_collision(grown, bin_order, kernel_index, collision_kernels):
    local_bins, width_x, width_z, width_y = grown.shape
    swap = [(0, 1), (1, 0)]
    me = lax.axis_index("bins")
    order = lax.dynamic_slice_in_dim(
        jnp.concatenate([bin_order, bin_order]), me * local_bins, 2 * local_bins
    )
    table = coupling_table(order, kernel_index, collision_kernels)
    halves = grown.astype(jnp.bfloat16).reshape(local_bins, 2, width_x // 2, width_z, width_y)
    own = lax.dynamic_index_in_dim(halves, me, axis=1, keepdims=False)
    away = lax.dynamic_index_in_dim(halves, 1 - me, axis=1, keepdims=False)
    arrived = lax.ppermute(away, "bins", swap)
    first = jnp.concatenate([own, arrived], axis=0).reshape(2 * local_bins, -1).astype(jnp.float32)
    change = collide(table, first).reshape(2 * local_bins, width_x // 2, width_z, width_y)
    back = lax.ppermute(change[local_bins:], "bins", swap)
    pair = jnp.stack([change[:local_bins], back], axis=1)
    pair = jnp.where(me == 0, pair, pair[:, ::-1])
    return pair.reshape(local_bins, width_x, width_z, width_y).astype(jnp.float32)


def body(
    bin_mass,
    wind_east,
    wind_north,
    supersaturation,
    potential_temp,
    terrain_height,
    fall_speed,
    growth_rate,
    latent_factor,
    bin_order,
    kernel_index,
    collision_kernels,
):
    local_bins, width_x, width_z, width_y = bin_mass.shape
    levels = lax.axis_index("vert") * width_z + lax.iota(jnp.int32, width_z)
    open_cells = (levels[None, :, None] >= terrain_height[:, None, :]).astype(jnp.float32)
    wind_x = wind_east * open_cells
    wind_y = wind_north * open_cells
    section_weights = (1.0 / 3.0, 0.5, 1.0)
    section_field = bin_mass
    for weight_now in section_weights:
        extended = extended_2(section_field, (("tiles", 1),), 1, jnp.bfloat16)
        section_field = bin_mass + weight_now * tendency(
            extended[:, 1:-1], extended[:, :-2], extended[:, 2:], wind_x, wind_y
        )
    rim_above = shifted(section_field[:, :, :1, :], "vert", -1)
    from_above = jnp.concatenate([section_field[:, :, 1:], rim_above], axis=2)
    speed = fall_speed[:, None, None, None]
    settled = (1.0 - speed) * section_field + speed * from_above
    growth = growth_rate[:, None, None, None]
    partial = (
        jnp.sum(growth * settled, axis=0),
        jnp.sum(latent_factor[:, None, None, None] * growth * settled, axis=0),
    )
    bin_devices = lax.axis_size("bins")
    if bin_devices == 2:
        swap = [(0, 1), (1, 0)]
        other = lax.ppermute(jnp.stack(partial), "bins", swap)
        uptake, heating = partial[0] + other[0], partial[1] + other[1]
    else:
        uptake, heating = lax.psum(partial, "bins")
    midway = supersaturation * jnp.exp(-0.5 * condense_rate * uptake)
    grown = settled * (1.0 + growth_gain * growth * midway)
    temp_next = potential_temp + heating_gain * midway * heating
    vapor_next = supersaturation * jnp.exp(-condense_rate * uptake)
    if bin_devices == 2 and width_x % 2 == 0:
        change = paired_collision(grown, bin_order, kernel_index, collision_kernels)
    else:
        change = spread_collision(grown, bin_order, kernel_index, collision_kernels)
    mass_next = (grown + change) * open_cells
    return (mass_next, temp_next, vapor_next)


def solution(mesh):
    return jax.shard_map(
        body,
        mesh=mesh,
        in_specs=(
            P("bins", ("groups", "tiles"), "vert", None),
            P(("groups", "tiles"), "vert", None),
            P(("groups", "tiles"), "vert", None),
            P(("groups", "tiles"), "vert", None),
            P(("groups", "tiles"), "vert", None),
            P(("groups", "tiles"), None),
            P("bins"),
            P("bins"),
            P("bins"),
            P(),
            P(),
            P(),
        ),
        out_specs=(
            P("bins", ("groups", "tiles"), "vert", None),
            P(("groups", "tiles"), "vert", None),
            P(("groups", "tiles"), "vert", None),
        ),
        check_vma=False,
    )
```

```python
import jax
import jax.numpy as jnp
from jax import lax
from jax.experimental import pallas as pl
from jax.sharding import PartitionSpec as P

SUB = 8


collision_rate = 0.001
condense_rate = 0.02
heating_gain = 0.03
growth_gain = 0.5
highest = lax.Precision.HIGHEST


def extended_2(array, sides, width, link=jnp.float32):
    for axis, dim in sides:
        size, length = (lax.axis_size(axis), array.shape[dim])
        up = [(i, (i + 1) % size) for i in range(size - 1)]
        down = [(j, i) for i, j in up]
        last = lax.slice_in_dim(array, length - width, length, axis=dim)
        first = lax.slice_in_dim(array, 0, width, axis=dim)
        before = lax.ppermute(last.astype(link), axis, up).astype(array.dtype)
        after = lax.ppermute(first.astype(link), axis, down).astype(array.dtype)
        array = jnp.concatenate([before, array, after], axis=dim)
    return array


def shifted(block, axis, distance):
    devices = range(lax.axis_size(axis))
    route = [(i - distance, i) for i in devices if i - distance in devices]
    return lax.ppermute(block, axis, route)


def tendency(center_cells, left_cells, right_cells, wind_x, wind_y):
    south_cells = jnp.roll(center_cells, 1, axis=3)
    north_cells = jnp.roll(center_cells, -1, axis=3)
    along_x = jnp.maximum(wind_x, 0.0) * (center_cells - left_cells) + jnp.minimum(wind_x, 0.0) * (
        right_cells - center_cells
    )
    along_y = jnp.maximum(wind_y, 0.0) * (center_cells - south_cells) + jnp.minimum(wind_y, 0.0) * (
        north_cells - center_cells
    )
    return -along_x - along_y


def coupling_table(bin_order, kernel_index, collision_kernels):
    class_count = kernel_index.shape[0]
    table_count = collision_kernels.shape[0]
    class_bins = collision_kernels.shape[1]
    bin_class = bin_order // class_bins
    bin_within = bin_order % class_bins
    kernel_pick = (kernel_index[:, :, None] == lax.iota(jnp.int32, table_count)).astype(jnp.float32)
    block_table = jnp.einsum(
        "ack,kmn->acmn", kernel_pick, collision_kernels.astype(jnp.float32), precision=highest
    )
    class_hot = (bin_class[:, None] == lax.iota(jnp.int32, class_count)).astype(jnp.float32)
    within_hot = (bin_within[:, None] == lax.iota(jnp.int32, class_bins)).astype(jnp.float32)
    row_table = jnp.einsum("bm,acmn->bacn", within_hot, block_table, precision=highest)
    row_table = jnp.einsum("ba,bacn->bcn", class_hot, row_table, precision=highest)
    coupling = jnp.einsum("bcn,dc,dn->bd", row_table, class_hot, within_hot, precision=highest)
    same_class = jnp.dot(class_hot, class_hot.T, precision=highest)
    return jnp.concatenate([coupling, same_class], axis=0).astype(jnp.bfloat16)


def collide(table, first):
    all_bins = table.shape[1]
    iterate = first
    for substep in range(SUB):
        products = jnp.dot(table, iterate.astype(jnp.bfloat16), preferred_element_type=jnp.float32)
        iterate = iterate + collision_rate * products[all_bins:] * products[:all_bins]
    return (iterate - first).astype(jnp.bfloat16)


def spread_collision(grown, bin_order, kernel_index, collision_kernels):
    local_bins, width_x, width_z, width_y = grown.shape
    table = coupling_table(bin_order, kernel_index, collision_kernels)
    all_bins = table.shape[1]
    start = grown.astype(jnp.bfloat16).reshape(local_bins, width_x, width_z * width_y)
    cell_block = lax.all_to_all(start, "bins", split_axis=2, concat_axis=0, tiled=True)
    block_shape = cell_block.shape
    first = cell_block.reshape(all_bins, -1).astype(jnp.float32)
    change = collide(table, first).reshape(block_shape)
    change = lax.all_to_all(change, "bins", split_axis=0, concat_axis=2, tiled=True)
    return change.reshape(local_bins, width_x, width_z, width_y).astype(jnp.float32)


def collision_kernel(table_ref, first_ref, change_ref):
    rows = first_ref.shape[0]
    first = first_ref[...].astype(jnp.float32)
    table = table_ref[...]
    iterate = first
    for substep in range(SUB):
        products = jnp.dot(table, iterate.astype(jnp.bfloat16), preferred_element_type=jnp.float32)
        iterate = iterate + collision_rate * products[rows:] * products[:rows]
    change_ref[...] = (iterate - first).astype(change_ref.dtype)


def collide_tiled(table, first, tile=512):
    rows, cells = first.shape
    tile = min(tile, cells)
    return pl.pallas_call(
        collision_kernel,
        out_shape=jax.ShapeDtypeStruct((rows, cells), jnp.bfloat16),
        grid=(cells // tile,),
        in_specs=[
            pl.BlockSpec((2 * rows, rows), lambda i: (0, 0)),
            pl.BlockSpec((rows, tile), lambda i: (0, i)),
        ],
        out_specs=pl.BlockSpec((rows, tile), lambda i: (0, i)),
        cost_estimate=pl.CostEstimate(
            flops=SUB * 4 * rows * rows * cells,
            bytes_accessed=4 * rows * cells + 4 * rows * rows,
            transcendentals=0,
        ),
    )(table, first)


def padded_bins(array, axis, part, pad):
    pieces = []
    for lo in (0, part):
        pieces.append(lax.slice_in_dim(array, lo, lo + part, axis=axis))
        shape = list(array.shape)
        shape[axis] = pad
        pieces.append(jnp.zeros(shape, array.dtype))
    return jnp.concatenate(pieces, axis=axis)


def paired_collision(grown, bin_order, kernel_index, collision_kernels):
    local_bins, width_x, width_z, width_y = grown.shape
    pad = -local_bins % 8
    part = local_bins + pad
    swap = [(0, 1), (1, 0)]
    me = lax.axis_index("bins")
    order = lax.dynamic_slice_in_dim(
        jnp.concatenate([bin_order, bin_order]), me * local_bins, 2 * local_bins
    )
    table = coupling_table(order, kernel_index, collision_kernels)
    all_bins = table.shape[1]
    table = jnp.concatenate(
        [
            padded_bins(padded_bins(table[:all_bins], 0, local_bins, pad), 1, local_bins, pad),
            padded_bins(padded_bins(table[all_bins:], 0, local_bins, pad), 1, local_bins, pad),
        ],
        axis=0,
    )
    halves = grown.astype(jnp.bfloat16).reshape(local_bins, 2, -1)
    own = lax.dynamic_index_in_dim(halves, me, axis=1, keepdims=False)
    away = lax.dynamic_index_in_dim(halves, 1 - me, axis=1, keepdims=False)
    arrived = lax.ppermute(away, "bins", swap)
    gap = jnp.zeros((pad, own.shape[1]), own.dtype)
    first = jnp.concatenate([own, gap, arrived, gap], axis=0)
    change = collide_tiled(table, first)
    back = lax.ppermute(change[part : part + local_bins], "bins", swap)
    pair = jnp.stack([change[:local_bins], back], axis=1)
    pair = jnp.where(me == 0, pair, pair[:, ::-1])
    return pair.reshape(local_bins, width_x, width_z, width_y).astype(jnp.float32)

def body(
    bin_mass,
    wind_east,
    wind_north,
    supersaturation,
    potential_temp,
    terrain_height,
    fall_speed,
    growth_rate,
    latent_factor,
    bin_order,
    kernel_index,
    collision_kernels,
):
    local_bins, width_x, width_z, width_y = bin_mass.shape
    levels = lax.axis_index("vert") * width_z + lax.iota(jnp.int32, width_z)
    open_cells = (levels[None, :, None] >= terrain_height[:, None, :]).astype(jnp.float32)
    wind_x = wind_east * open_cells
    wind_y = wind_north * open_cells
    section_weights = (1.0 / 3.0, 0.5, 1.0)
    section_field = bin_mass
    for weight_now in section_weights:
        extended = extended_2(section_field, (("tiles", 1),), 1, jnp.bfloat16)
        section_field = bin_mass + weight_now * tendency(
            extended[:, 1:-1], extended[:, :-2], extended[:, 2:], wind_x, wind_y
        )
    rim_above = shifted(section_field[:, :, :1, :], "vert", -1)
    from_above = jnp.concatenate([section_field[:, :, 1:], rim_above], axis=2)
    speed = fall_speed[:, None, None, None]
    settled = (1.0 - speed) * section_field + speed * from_above
    growth = growth_rate[:, None, None, None]
    partial = (
        jnp.sum(growth * settled, axis=0),
        jnp.sum(latent_factor[:, None, None, None] * growth * settled, axis=0),
    )
    bin_devices = lax.axis_size("bins")
    if bin_devices == 2:
        swap = [(0, 1), (1, 0)]
        other = lax.ppermute(jnp.stack(partial), "bins", swap)
        uptake, heating = partial[0] + other[0], partial[1] + other[1]
    else:
        uptake, heating = lax.psum(partial, "bins")
    midway = supersaturation * jnp.exp(-0.5 * condense_rate * uptake)
    grown = settled * (1.0 + growth_gain * growth * midway)
    temp_next = potential_temp + heating_gain * midway * heating
    vapor_next = supersaturation * jnp.exp(-condense_rate * uptake)
    if bin_devices == 2 and width_x % 2 == 0:
        change = paired_collision(grown, bin_order, kernel_index, collision_kernels)
    else:
        change = spread_collision(grown, bin_order, kernel_index, collision_kernels)
    mass_next = (grown + change) * open_cells
    return (mass_next, temp_next, vapor_next)


def solution(mesh):
    return jax.shard_map(
        body,
        mesh=mesh,
        in_specs=(
            P("bins", ("groups", "tiles"), "vert", None),
            P(("groups", "tiles"), "vert", None),
            P(("groups", "tiles"), "vert", None),
            P(("groups", "tiles"), "vert", None),
            P(("groups", "tiles"), "vert", None),
            P(("groups", "tiles"), None),
            P("bins"),
            P("bins"),
            P("bins"),
            P(),
            P(),
            P(),
        ),
        out_specs=(
            P("bins", ("groups", "tiles"), "vert", None),
            P(("groups", "tiles"), "vert", None),
            P(("groups", "tiles"), "vert", None),
        ),
        check_vma=False,
    )
```

```python
import jax
import jax.numpy as jnp
from jax import lax
from jax.sharding import PartitionSpec as P

SUB = 8


collision_rate = 0.001
condense_rate = 0.02
heating_gain = 0.03
growth_gain = 0.5
highest = lax.Precision.HIGHEST


def extended_2(array, sides, width, link=jnp.float32):
    for axis, dim in sides:
        size, length = (lax.axis_size(axis), array.shape[dim])
        up = [(i, (i + 1) % size) for i in range(size - 1)]
        down = [(j, i) for i, j in up]
        last = lax.slice_in_dim(array, length - width, length, axis=dim)
        first = lax.slice_in_dim(array, 0, width, axis=dim)
        before = lax.ppermute(last.astype(link), axis, up).astype(array.dtype)
        after = lax.ppermute(first.astype(link), axis, down).astype(array.dtype)
        array = jnp.concatenate([before, array, after], axis=dim)
    return array


def shifted(block, axis, distance):
    devices = range(lax.axis_size(axis))
    route = [(i - distance, i) for i in devices if i - distance in devices]
    return lax.ppermute(block, axis, route)


def tendency(center_cells, left_cells, right_cells, wind_x, wind_y):
    south_cells = jnp.roll(center_cells, 1, axis=3)
    north_cells = jnp.roll(center_cells, -1, axis=3)
    along_x = jnp.maximum(wind_x, 0.0) * (center_cells - left_cells) + jnp.minimum(wind_x, 0.0) * (
        right_cells - center_cells
    )
    along_y = jnp.maximum(wind_y, 0.0) * (center_cells - south_cells) + jnp.minimum(wind_y, 0.0) * (
        north_cells - center_cells
    )
    return -along_x - along_y


def coupling_table(bin_order, kernel_index, collision_kernels):
    class_count = kernel_index.shape[0]
    table_count = collision_kernels.shape[0]
    class_bins = collision_kernels.shape[1]
    bin_class = bin_order // class_bins
    bin_within = bin_order % class_bins
    kernel_pick = (kernel_index[:, :, None] == lax.iota(jnp.int32, table_count)).astype(jnp.float32)
    block_table = jnp.einsum(
        "ack,kmn->acmn", kernel_pick, collision_kernels.astype(jnp.float32), precision=highest
    )
    class_hot = (bin_class[:, None] == lax.iota(jnp.int32, class_count)).astype(jnp.float32)
    within_hot = (bin_within[:, None] == lax.iota(jnp.int32, class_bins)).astype(jnp.float32)
    row_table = jnp.einsum("bm,acmn->bacn", within_hot, block_table, precision=highest)
    row_table = jnp.einsum("ba,bacn->bcn", class_hot, row_table, precision=highest)
    coupling = jnp.einsum("bcn,dc,dn->bd", row_table, class_hot, within_hot, precision=highest)
    same_class = jnp.dot(class_hot, class_hot.T, precision=highest)
    return jnp.concatenate([coupling, same_class], axis=0).astype(jnp.bfloat16)


def collide(table, first):
    all_bins = table.shape[1]
    iterate = first
    for substep in range(SUB):
        products = jnp.dot(table, iterate.astype(jnp.bfloat16), preferred_element_type=jnp.float32)
        iterate = iterate + collision_rate * products[all_bins:] * products[:all_bins]
    return (iterate - first).astype(jnp.bfloat16)


def spread_collision(grown, bin_order, kernel_index, collision_kernels):
    local_bins, width_x, width_z, width_y = grown.shape
    table = coupling_table(bin_order, kernel_index, collision_kernels)
    all_bins = table.shape[1]
    start = grown.astype(jnp.bfloat16).reshape(local_bins, width_x, width_z * width_y)
    cell_block = lax.all_to_all(start, "bins", split_axis=2, concat_axis=0, tiled=True)
    block_shape = cell_block.shape
    first = cell_block.reshape(all_bins, -1).astype(jnp.float32)
    change = collide(table, first).reshape(block_shape)
    change = lax.all_to_all(change, "bins", split_axis=0, concat_axis=2, tiled=True)
    return change.reshape(local_bins, width_x, width_z, width_y).astype(jnp.float32)


def paired_collision(grown, bin_order, kernel_index, collision_kernels):
    local_bins, width_x, width_z, width_y = grown.shape
    swap = [(0, 1), (1, 0)]
    me = lax.axis_index("bins")
    order = lax.dynamic_slice_in_dim(
        jnp.concatenate([bin_order, bin_order]), me * local_bins, 2 * local_bins
    )
    table = coupling_table(order, kernel_index, collision_kernels)
    halves = grown.astype(jnp.bfloat16).reshape(local_bins, 2, width_x // 2, width_z, width_y)
    own = lax.dynamic_index_in_dim(halves, me, axis=1, keepdims=False)
    away = lax.dynamic_index_in_dim(halves, 1 - me, axis=1, keepdims=False)
    kept, returned = [], []
    for chunk in range(width_x // 2):
        arrived = lax.ppermute(away[:, chunk], "bins", swap)
        first = jnp.concatenate([own[:, chunk], arrived], axis=0).reshape(2 * local_bins, -1).astype(jnp.float32)
        change = collide(table, first).reshape(2 * local_bins, width_z, width_y)
        returned.append(lax.ppermute(change[local_bins:], "bins", swap))
        kept.append(change[:local_bins])
    pair = jnp.stack([jnp.stack(kept, axis=1), jnp.stack(returned, axis=1)], axis=1)
    pair = jnp.where(me == 0, pair, pair[:, ::-1])
    return pair.reshape(local_bins, width_x, width_z, width_y).astype(jnp.float32)

def body(
    bin_mass,
    wind_east,
    wind_north,
    supersaturation,
    potential_temp,
    terrain_height,
    fall_speed,
    growth_rate,
    latent_factor,
    bin_order,
    kernel_index,
    collision_kernels,
):
    local_bins, width_x, width_z, width_y = bin_mass.shape
    levels = lax.axis_index("vert") * width_z + lax.iota(jnp.int32, width_z)
    open_cells = (levels[None, :, None] >= terrain_height[:, None, :]).astype(jnp.float32)
    wind_x = wind_east * open_cells
    wind_y = wind_north * open_cells
    section_weights = (1.0 / 3.0, 0.5, 1.0)
    section_field = bin_mass
    for weight_now in section_weights:
        extended = extended_2(section_field, (("tiles", 1),), 1, jnp.bfloat16)
        section_field = bin_mass + weight_now * tendency(
            extended[:, 1:-1], extended[:, :-2], extended[:, 2:], wind_x, wind_y
        )
    rim_above = shifted(section_field[:, :, :1, :], "vert", -1)
    from_above = jnp.concatenate([section_field[:, :, 1:], rim_above], axis=2)
    speed = fall_speed[:, None, None, None]
    settled = (1.0 - speed) * section_field + speed * from_above
    growth = growth_rate[:, None, None, None]
    partial = (
        jnp.sum(growth * settled, axis=0),
        jnp.sum(latent_factor[:, None, None, None] * growth * settled, axis=0),
    )
    bin_devices = lax.axis_size("bins")
    if bin_devices == 2:
        swap = [(0, 1), (1, 0)]
        other = lax.ppermute(jnp.stack(partial), "bins", swap)
        uptake, heating = partial[0] + other[0], partial[1] + other[1]
    else:
        uptake, heating = lax.psum(partial, "bins")
    midway = supersaturation * jnp.exp(-0.5 * condense_rate * uptake)
    grown = settled * (1.0 + growth_gain * growth * midway)
    temp_next = potential_temp + heating_gain * midway * heating
    vapor_next = supersaturation * jnp.exp(-condense_rate * uptake)
    if bin_devices == 2 and width_x % 2 == 0:
        change = paired_collision(grown, bin_order, kernel_index, collision_kernels)
    else:
        change = spread_collision(grown, bin_order, kernel_index, collision_kernels)
    mass_next = (grown + change) * open_cells
    return (mass_next, temp_next, vapor_next)


def solution(mesh):
    return jax.shard_map(
        body,
        mesh=mesh,
        in_specs=(
            P("bins", ("groups", "tiles"), "vert", None),
            P(("groups", "tiles"), "vert", None),
            P(("groups", "tiles"), "vert", None),
            P(("groups", "tiles"), "vert", None),
            P(("groups", "tiles"), "vert", None),
            P(("groups", "tiles"), None),
            P("bins"),
            P("bins"),
            P("bins"),
            P(),
            P(),
            P(),
        ),
        out_specs=(
            P("bins", ("groups", "tiles"), "vert", None),
            P(("groups", "tiles"), "vert", None),
            P(("groups", "tiles"), "vert", None),
        ),
        check_vma=False,
    )
```

```python
import jax
import jax.numpy as jnp
from jax import lax
from jax.sharding import PartitionSpec as P

SUB = 8


collision_rate = 0.001
condense_rate = 0.02
heating_gain = 0.03
growth_gain = 0.5
highest = lax.Precision.HIGHEST


def extended_2(array, sides, width, link=jnp.float32):
    for axis, dim in sides:
        size, length = (lax.axis_size(axis), array.shape[dim])
        up = [(i, (i + 1) % size) for i in range(size - 1)]
        down = [(j, i) for i, j in up]
        last = lax.slice_in_dim(array, length - width, length, axis=dim)
        first = lax.slice_in_dim(array, 0, width, axis=dim)
        before = lax.ppermute(last.astype(link), axis, up).astype(array.dtype)
        after = lax.ppermute(first.astype(link), axis, down).astype(array.dtype)
        array = jnp.concatenate([before, array, after], axis=dim)
    return array


def advect_rims(bin_mass, wind_x, wind_y, section_weights):
    local_bins, width_x = bin_mass.shape[:2]
    depth = len(section_weights)
    tiles = lax.axis_size("tiles")
    up = [(i, i + 1) for i in range(tiles - 1)]
    down = [(j, i) for i, j in up]

    def rim(lo, hi):
        winds = jnp.stack([wind_x[lo:hi], wind_y[lo:hi]])
        high = winds.astype(jnp.bfloat16)
        low = (winds - high.astype(jnp.float32)).astype(jnp.bfloat16)
        return jnp.concatenate([bin_mass[:, lo:hi].astype(jnp.bfloat16), high, low], axis=0)

    def unpack(message):
        message = message.astype(jnp.float32)
        winds = message[local_bins : local_bins + 2] + message[local_bins + 2 :]
        return message[:local_bins], winds[0], winds[1]

    q_left, wx_left, wy_left = unpack(lax.ppermute(rim(width_x - depth, width_x), "tiles", up))
    q_right, wx_right, wy_right = unpack(lax.ppermute(rim(0, depth), "tiles", down))
    left, right, own = q_left, q_right, bin_mass
    for stage, weight_now in enumerate(section_weights, start=1):
        reach = depth - stage
        own_next = bin_mass + weight_now * tendency(
            own,
            jnp.concatenate([left[:, -1:], own[:, :-1]], axis=1),
            jnp.concatenate([own[:, 1:], right[:, :1]], axis=1),
            wind_x,
            wind_y,
        )
        if reach > 0:
            left_next = q_left[:, -reach:] + weight_now * tendency(
                left[:, -reach:],
                left[:, -reach - 1 : -1],
                jnp.concatenate([left[:, -reach + 1 :], own[:, :1]], axis=1) if reach > 1 else own[:, :1],
                wx_left[-reach:],
                wy_left[-reach:],
            )
            right_next = q_right[:, :reach] + weight_now * tendency(
                right[:, :reach],
                jnp.concatenate([own[:, -1:], right[:, : reach - 1]], axis=1) if reach > 1 else own[:, -1:],
                right[:, 1 : reach + 1],
                wx_right[:reach],
                wy_right[:reach],
            )
            left, right = left_next, right_next
        own = own_next
    return own


def shifted(block, axis, distance):
    devices = range(lax.axis_size(axis))
    route = [(i - distance, i) for i in devices if i - distance in devices]
    return lax.ppermute(block, axis, route)


def tendency(center_cells, left_cells, right_cells, wind_x, wind_y):
    south_cells = jnp.roll(center_cells, 1, axis=3)
    north_cells = jnp.roll(center_cells, -1, axis=3)
    along_x = jnp.maximum(wind_x, 0.0) * (center_cells - left_cells) + jnp.minimum(wind_x, 0.0) * (
        right_cells - center_cells
    )
    along_y = jnp.maximum(wind_y, 0.0) * (center_cells - south_cells) + jnp.minimum(wind_y, 0.0) * (
        north_cells - center_cells
    )
    return -along_x - along_y


def coupling_table(bin_order, kernel_index, collision_kernels):
    class_count = kernel_index.shape[0]
    table_count = collision_kernels.shape[0]
    class_bins = collision_kernels.shape[1]
    bin_class = bin_order // class_bins
    bin_within = bin_order % class_bins
    kernel_pick = (kernel_index[:, :, None] == lax.iota(jnp.int32, table_count)).astype(jnp.float32)
    block_table = jnp.einsum(
        "ack,kmn->acmn", kernel_pick, collision_kernels.astype(jnp.float32), precision=highest
    )
    class_hot = (bin_class[:, None] == lax.iota(jnp.int32, class_count)).astype(jnp.float32)
    within_hot = (bin_within[:, None] == lax.iota(jnp.int32, class_bins)).astype(jnp.float32)
    row_table = jnp.einsum("bm,acmn->bacn", within_hot, block_table, precision=highest)
    row_table = jnp.einsum("ba,bacn->bcn", class_hot, row_table, precision=highest)
    coupling = jnp.einsum("bcn,dc,dn->bd", row_table, class_hot, within_hot, precision=highest)
    same_class = jnp.dot(class_hot, class_hot.T, precision=highest)
    return jnp.concatenate([coupling, same_class], axis=0).astype(jnp.bfloat16)


def collide(table, first):
    all_bins = table.shape[1]
    iterate = first
    for substep in range(SUB):
        products = jnp.dot(table, iterate.astype(jnp.bfloat16), preferred_element_type=jnp.float32)
        iterate = iterate + collision_rate * products[all_bins:] * products[:all_bins]
    return (iterate - first).astype(jnp.bfloat16)


def spread_collision(grown, bin_order, kernel_index, collision_kernels):
    local_bins, width_x, width_z, width_y = grown.shape
    table = coupling_table(bin_order, kernel_index, collision_kernels)
    all_bins = table.shape[1]
    start = grown.astype(jnp.bfloat16).reshape(local_bins, width_x, width_z * width_y)
    cell_block = lax.all_to_all(start, "bins", split_axis=2, concat_axis=0, tiled=True)
    block_shape = cell_block.shape
    first = cell_block.reshape(all_bins, -1).astype(jnp.float32)
    change = collide(table, first).reshape(block_shape)
    change = lax.all_to_all(change, "bins", split_axis=0, concat_axis=2, tiled=True)
    return change.reshape(local_bins, width_x, width_z, width_y).astype(jnp.float32)


def paired_collision(grown, bin_order, kernel_index, collision_kernels):
    local_bins, width_x, width_z, width_y = grown.shape
    swap = [(0, 1), (1, 0)]
    me = lax.axis_index("bins")
    order = lax.dynamic_slice_in_dim(
        jnp.concatenate([bin_order, bin_order]), me * local_bins, 2 * local_bins
    )
    table = coupling_table(order, kernel_index, collision_kernels)
    halves = grown.astype(jnp.bfloat16).reshape(local_bins, 2, width_x // 2, width_z, width_y)
    own = lax.dynamic_index_in_dim(halves, me, axis=1, keepdims=False)
    away = lax.dynamic_index_in_dim(halves, 1 - me, axis=1, keepdims=False)
    kept, returned = [], []
    for chunk in range(width_x // 2):
        arrived = lax.ppermute(away[:, chunk], "bins", swap)
        first = jnp.concatenate([own[:, chunk], arrived], axis=0).reshape(2 * local_bins, -1).astype(jnp.float32)
        change = collide(table, first).reshape(2 * local_bins, width_z, width_y)
        returned.append(lax.ppermute(change[local_bins:], "bins", swap))
        kept.append(change[:local_bins])
    pair = jnp.stack([jnp.stack(kept, axis=1), jnp.stack(returned, axis=1)], axis=1)
    pair = jnp.where(me == 0, pair, pair[:, ::-1])
    return pair.reshape(local_bins, width_x, width_z, width_y).astype(jnp.float32)

def body(
    bin_mass,
    wind_east,
    wind_north,
    supersaturation,
    potential_temp,
    terrain_height,
    fall_speed,
    growth_rate,
    latent_factor,
    bin_order,
    kernel_index,
    collision_kernels,
):
    local_bins, width_x, width_z, width_y = bin_mass.shape
    levels = lax.axis_index("vert") * width_z + lax.iota(jnp.int32, width_z)
    open_cells = (levels[None, :, None] >= terrain_height[:, None, :]).astype(jnp.float32)
    wind_x = wind_east * open_cells
    wind_y = wind_north * open_cells
    section_weights = (1.0 / 3.0, 0.5, 1.0)
    if width_x >= len(section_weights):
        section_field = advect_rims(bin_mass, wind_x, wind_y, section_weights)
    else:
        section_field = bin_mass
        for weight_now in section_weights:
            extended = extended_2(section_field, (("tiles", 1),), 1, jnp.bfloat16)
            section_field = bin_mass + weight_now * tendency(
                extended[:, 1:-1], extended[:, :-2], extended[:, 2:], wind_x, wind_y
            )
    rim_above = shifted(section_field[:, :, :1, :], "vert", -1)
    from_above = jnp.concatenate([section_field[:, :, 1:], rim_above], axis=2)
    speed = fall_speed[:, None, None, None]
    settled = (1.0 - speed) * section_field + speed * from_above
    growth = growth_rate[:, None, None, None]
    partial = (
        jnp.sum(growth * settled, axis=0),
        jnp.sum(latent_factor[:, None, None, None] * growth * settled, axis=0),
    )
    bin_devices = lax.axis_size("bins")
    if bin_devices == 2:
        swap = [(0, 1), (1, 0)]
        other = lax.ppermute(jnp.stack(partial), "bins", swap)
        uptake, heating = partial[0] + other[0], partial[1] + other[1]
    else:
        uptake, heating = lax.psum(partial, "bins")
    midway = supersaturation * jnp.exp(-0.5 * condense_rate * uptake)
    grown = settled * (1.0 + growth_gain * growth * midway)
    temp_next = potential_temp + heating_gain * midway * heating
    vapor_next = supersaturation * jnp.exp(-condense_rate * uptake)
    if bin_devices == 2 and width_x % 2 == 0:
        change = paired_collision(grown, bin_order, kernel_index, collision_kernels)
    else:
        change = spread_collision(grown, bin_order, kernel_index, collision_kernels)
    mass_next = (grown + change) * open_cells
    return (mass_next, temp_next, vapor_next)


def solution(mesh):
    return jax.shard_map(
        body,
        mesh=mesh,
        in_specs=(
            P("bins", ("groups", "tiles"), "vert", None),
            P(("groups", "tiles"), "vert", None),
            P(("groups", "tiles"), "vert", None),
            P(("groups", "tiles"), "vert", None),
            P(("groups", "tiles"), "vert", None),
            P(("groups", "tiles"), None),
            P("bins"),
            P("bins"),
            P("bins"),
            P(),
            P(),
            P(),
        ),
        out_specs=(
            P("bins", ("groups", "tiles"), "vert", None),
            P(("groups", "tiles"), "vert", None),
            P(("groups", "tiles"), "vert", None),
        ),
        check_vma=False,
    )
```

```python
import functools

import jax
import jax.numpy as jnp
from jax import lax
from jax.experimental import pallas as pl
from jax.experimental.pallas import tpu as pltpu
from jax.sharding import PartitionSpec as P

SUB = 8


collision_rate = 0.001
condense_rate = 0.02
heating_gain = 0.03
growth_gain = 0.5
highest = lax.Precision.HIGHEST


def extended_2(array, sides, width, link=jnp.float32):
    for axis, dim in sides:
        size, length = (lax.axis_size(axis), array.shape[dim])
        up = [(i, (i + 1) % size) for i in range(size - 1)]
        down = [(j, i) for i, j in up]
        last = lax.slice_in_dim(array, length - width, length, axis=dim)
        first = lax.slice_in_dim(array, 0, width, axis=dim)
        before = lax.ppermute(last.astype(link), axis, up).astype(array.dtype)
        after = lax.ppermute(first.astype(link), axis, down).astype(array.dtype)
        array = jnp.concatenate([before, array, after], axis=dim)
    return array


def advect_kernel(weights, q_ref, left_ref, right_ref, wx_ref, wy_ref, out_ref):
    depth = len(weights)
    width = q_ref.shape[1]
    field = jnp.concatenate([left_ref[...], q_ref[...], right_ref[...]], axis=1)
    wx = wx_ref[...]
    wy = wy_ref[...]
    section = field
    for stage, weight_now in enumerate(weights, start=1):
        span = width + 2 * (depth - stage)
        center = section[:, 1 : 1 + span]
        west = section[:, 0:span]
        east = section[:, 2 : 2 + span]
        south = pltpu.roll(center, 1, 3)
        north = pltpu.roll(center, center.shape[3] - 1, 3)
        wind_a = wx[stage : stage + span]
        wind_b = wy[stage : stage + span]
        along_x = jnp.maximum(wind_a, 0.0) * (center - west) + jnp.minimum(wind_a, 0.0) * (east - center)
        along_y = jnp.maximum(wind_b, 0.0) * (center - south) + jnp.minimum(wind_b, 0.0) * (north - center)
        section = field[:, stage : stage + span] + weight_now * (-along_x - along_y)
    out_ref[...] = section


def advect_kernel_call(bin_mass, wind_x, wind_y, section_weights):
    local_bins, width_x, width_z, width_y = bin_mass.shape
    depth = len(section_weights)
    tiles = lax.axis_size("tiles")
    up = [(i, i + 1) for i in range(tiles - 1)]
    down = [(j, i) for i, j in up]

    def rim(lo, hi):
        winds = jnp.stack([wind_x[lo:hi], wind_y[lo:hi]])
        high = winds.astype(jnp.bfloat16)
        low = (winds - high.astype(jnp.float32)).astype(jnp.bfloat16)
        return jnp.concatenate([bin_mass[:, lo:hi].astype(jnp.bfloat16), high, low], axis=0)

    def unpack(message):
        message = message.astype(jnp.float32)
        winds = message[local_bins : local_bins + 2] + message[local_bins + 2 :]
        return message[:local_bins], winds[0], winds[1]

    q_left, wx_left, wy_left = unpack(lax.ppermute(rim(width_x - depth, width_x), "tiles", up))
    q_right, wx_right, wy_right = unpack(lax.ppermute(rim(0, depth), "tiles", down))
    wx = jnp.concatenate([wx_left, wind_x, wx_right], axis=0)
    wy = jnp.concatenate([wy_left, wind_y, wy_right], axis=0)
    block = max(d for d in range(1, 34) if local_bins % d == 0)
    rim_spec = pl.BlockSpec((block, depth, width_z, width_y), lambda i: (i, 0, 0, 0))
    own_spec = pl.BlockSpec((block, width_x, width_z, width_y), lambda i: (i, 0, 0, 0))
    wind_spec = pl.BlockSpec(wx.shape, lambda i: (0, 0, 0))
    cells = local_bins * width_x * width_z * width_y
    return pl.pallas_call(
        functools.partial(advect_kernel, section_weights),
        out_shape=jax.ShapeDtypeStruct(bin_mass.shape, bin_mass.dtype),
        grid=(local_bins // block,),
        in_specs=[own_spec, rim_spec, rim_spec, wind_spec, wind_spec],
        out_specs=own_spec,
        cost_estimate=pl.CostEstimate(flops=80 * cells, bytes_accessed=20 * cells, transcendentals=0),
    )(bin_mass, q_left, q_right, wx, wy)


def shifted(block, axis, distance):
    devices = range(lax.axis_size(axis))
    route = [(i - distance, i) for i in devices if i - distance in devices]
    return lax.ppermute(block, axis, route)


def tendency(center_cells, left_cells, right_cells, wind_x, wind_y):
    south_cells = jnp.roll(center_cells, 1, axis=3)
    north_cells = jnp.roll(center_cells, -1, axis=3)
    along_x = jnp.maximum(wind_x, 0.0) * (center_cells - left_cells) + jnp.minimum(wind_x, 0.0) * (
        right_cells - center_cells
    )
    along_y = jnp.maximum(wind_y, 0.0) * (center_cells - south_cells) + jnp.minimum(wind_y, 0.0) * (
        north_cells - center_cells
    )
    return -along_x - along_y


def coupling_table(bin_order, kernel_index, collision_kernels):
    class_count = kernel_index.shape[0]
    table_count = collision_kernels.shape[0]
    class_bins = collision_kernels.shape[1]
    bin_class = bin_order // class_bins
    bin_within = bin_order % class_bins
    kernel_pick = (kernel_index[:, :, None] == lax.iota(jnp.int32, table_count)).astype(jnp.float32)
    block_table = jnp.einsum(
        "ack,kmn->acmn", kernel_pick, collision_kernels.astype(jnp.float32), precision=highest
    )
    class_hot = (bin_class[:, None] == lax.iota(jnp.int32, class_count)).astype(jnp.float32)
    within_hot = (bin_within[:, None] == lax.iota(jnp.int32, class_bins)).astype(jnp.float32)
    row_table = jnp.einsum("bm,acmn->bacn", within_hot, block_table, precision=highest)
    row_table = jnp.einsum("ba,bacn->bcn", class_hot, row_table, precision=highest)
    coupling = jnp.einsum("bcn,dc,dn->bd", row_table, class_hot, within_hot, precision=highest)
    same_class = jnp.dot(class_hot, class_hot.T, precision=highest)
    return jnp.concatenate([coupling, same_class], axis=0).astype(jnp.bfloat16)


def collide(table, first):
    all_bins = table.shape[1]
    iterate = first
    for substep in range(SUB):
        products = jnp.dot(table, iterate.astype(jnp.bfloat16), preferred_element_type=jnp.float32)
        iterate = iterate + collision_rate * products[all_bins:] * products[:all_bins]
    return (iterate - first).astype(jnp.bfloat16)


def spread_collision(grown, bin_order, kernel_index, collision_kernels):
    local_bins, width_x, width_z, width_y = grown.shape
    table = coupling_table(bin_order, kernel_index, collision_kernels)
    all_bins = table.shape[1]
    start = grown.astype(jnp.bfloat16).reshape(local_bins, width_x, width_z * width_y)
    cell_block = lax.all_to_all(start, "bins", split_axis=2, concat_axis=0, tiled=True)
    block_shape = cell_block.shape
    first = cell_block.reshape(all_bins, -1).astype(jnp.float32)
    change = collide(table, first).reshape(block_shape)
    change = lax.all_to_all(change, "bins", split_axis=0, concat_axis=2, tiled=True)
    return change.reshape(local_bins, width_x, width_z, width_y).astype(jnp.float32)


def paired_collision(grown, bin_order, kernel_index, collision_kernels):
    local_bins, width_x, width_z, width_y = grown.shape
    swap = [(0, 1), (1, 0)]
    me = lax.axis_index("bins")
    order = lax.dynamic_slice_in_dim(
        jnp.concatenate([bin_order, bin_order]), me * local_bins, 2 * local_bins
    )
    table = coupling_table(order, kernel_index, collision_kernels)
    halves = grown.astype(jnp.bfloat16).reshape(local_bins, 2, width_x // 2, width_z, width_y)
    own = lax.dynamic_index_in_dim(halves, me, axis=1, keepdims=False)
    away = lax.dynamic_index_in_dim(halves, 1 - me, axis=1, keepdims=False)
    kept, returned = [], []
    for chunk in range(width_x // 2):
        arrived = lax.ppermute(away[:, chunk], "bins", swap)
        first = jnp.concatenate([own[:, chunk], arrived], axis=0).reshape(2 * local_bins, -1).astype(jnp.float32)
        change = collide(table, first).reshape(2 * local_bins, width_z, width_y)
        returned.append(lax.ppermute(change[local_bins:], "bins", swap))
        kept.append(change[:local_bins])
    pair = jnp.stack([jnp.stack(kept, axis=1), jnp.stack(returned, axis=1)], axis=1)
    pair = jnp.where(me == 0, pair, pair[:, ::-1])
    return pair.reshape(local_bins, width_x, width_z, width_y).astype(jnp.float32)

def body(
    bin_mass,
    wind_east,
    wind_north,
    supersaturation,
    potential_temp,
    terrain_height,
    fall_speed,
    growth_rate,
    latent_factor,
    bin_order,
    kernel_index,
    collision_kernels,
):
    local_bins, width_x, width_z, width_y = bin_mass.shape
    levels = lax.axis_index("vert") * width_z + lax.iota(jnp.int32, width_z)
    open_cells = (levels[None, :, None] >= terrain_height[:, None, :]).astype(jnp.float32)
    wind_x = wind_east * open_cells
    wind_y = wind_north * open_cells
    section_weights = (1.0 / 3.0, 0.5, 1.0)
    if width_x >= len(section_weights):
        section_field = advect_kernel_call(bin_mass, wind_x, wind_y, section_weights)
    else:
        section_field = bin_mass
        for weight_now in section_weights:
            extended = extended_2(section_field, (("tiles", 1),), 1, jnp.bfloat16)
            section_field = bin_mass + weight_now * tendency(
                extended[:, 1:-1], extended[:, :-2], extended[:, 2:], wind_x, wind_y
            )
    rim_above = shifted(section_field[:, :, :1, :], "vert", -1)
    from_above = jnp.concatenate([section_field[:, :, 1:], rim_above], axis=2)
    speed = fall_speed[:, None, None, None]
    settled = (1.0 - speed) * section_field + speed * from_above
    growth = growth_rate[:, None, None, None]
    partial = (
        jnp.sum(growth * settled, axis=0),
        jnp.sum(latent_factor[:, None, None, None] * growth * settled, axis=0),
    )
    bin_devices = lax.axis_size("bins")
    if bin_devices == 2:
        swap = [(0, 1), (1, 0)]
        other = lax.ppermute(jnp.stack(partial), "bins", swap)
        uptake, heating = partial[0] + other[0], partial[1] + other[1]
    else:
        uptake, heating = lax.psum(partial, "bins")
    midway = supersaturation * jnp.exp(-0.5 * condense_rate * uptake)
    grown = settled * (1.0 + growth_gain * growth * midway)
    temp_next = potential_temp + heating_gain * midway * heating
    vapor_next = supersaturation * jnp.exp(-condense_rate * uptake)
    if bin_devices == 2 and width_x % 2 == 0:
        change = paired_collision(grown, bin_order, kernel_index, collision_kernels)
    else:
        change = spread_collision(grown, bin_order, kernel_index, collision_kernels)
    mass_next = (grown + change) * open_cells
    return (mass_next, temp_next, vapor_next)


def solution(mesh):
    return jax.shard_map(
        body,
        mesh=mesh,
        in_specs=(
            P("bins", ("groups", "tiles"), "vert", None),
            P(("groups", "tiles"), "vert", None),
            P(("groups", "tiles"), "vert", None),
            P(("groups", "tiles"), "vert", None),
            P(("groups", "tiles"), "vert", None),
            P(("groups", "tiles"), None),
            P("bins"),
            P("bins"),
            P("bins"),
            P(),
            P(),
            P(),
        ),
        out_specs=(
            P("bins", ("groups", "tiles"), "vert", None),
            P(("groups", "tiles"), "vert", None),
            P(("groups", "tiles"), "vert", None),
        ),
        check_vma=False,
    )
```

```python
import functools

import jax
import jax.numpy as jnp
from jax import lax
from jax.experimental import pallas as pl
from jax.experimental.pallas import tpu as pltpu
from jax.sharding import PartitionSpec as P

SUB = 8


collision_rate = 0.001
condense_rate = 0.02
heating_gain = 0.03
growth_gain = 0.5
highest = lax.Precision.HIGHEST


def extended_2(array, sides, width, link=jnp.float32):
    for axis, dim in sides:
        size, length = (lax.axis_size(axis), array.shape[dim])
        up = [(i, (i + 1) % size) for i in range(size - 1)]
        down = [(j, i) for i, j in up]
        last = lax.slice_in_dim(array, length - width, length, axis=dim)
        first = lax.slice_in_dim(array, 0, width, axis=dim)
        before = lax.ppermute(last.astype(link), axis, up).astype(array.dtype)
        after = lax.ppermute(first.astype(link), axis, down).astype(array.dtype)
        array = jnp.concatenate([before, array, after], axis=dim)
    return array


def advect_kernel(weights, q_ref, left_ref, right_ref, wx_ref, wy_ref, out_ref):
    depth = len(weights)
    width = q_ref.shape[1]
    field = jnp.concatenate([left_ref[...], q_ref[...], right_ref[...]], axis=1)
    wx = wx_ref[...]
    wy = wy_ref[...]
    section = field
    for stage, weight_now in enumerate(weights, start=1):
        span = width + 2 * (depth - stage)
        center = section[:, 1 : 1 + span]
        west = section[:, 0:span]
        east = section[:, 2 : 2 + span]
        south = pltpu.roll(center, 1, 3)
        north = pltpu.roll(center, center.shape[3] - 1, 3)
        wind_a = wx[stage : stage + span]
        wind_b = wy[stage : stage + span]
        along_x = jnp.maximum(wind_a, 0.0) * (center - west) + jnp.minimum(wind_a, 0.0) * (east - center)
        along_y = jnp.maximum(wind_b, 0.0) * (center - south) + jnp.minimum(wind_b, 0.0) * (north - center)
        section = field[:, stage : stage + span] + weight_now * (-along_x - along_y)
    out_ref[...] = section


def advect_kernel_call(bin_mass, wind_x, wind_y, section_weights):
    local_bins, width_x, width_z, width_y = bin_mass.shape
    depth = len(section_weights)
    tiles = lax.axis_size("tiles")
    up = [(i, i + 1) for i in range(tiles - 1)]
    down = [(j, i) for i, j in up]

    def rim(lo, hi):
        winds = jnp.stack([wind_x[lo:hi], wind_y[lo:hi]])
        high = winds.astype(jnp.bfloat16)
        low = (winds - high.astype(jnp.float32)).astype(jnp.bfloat16)
        return jnp.concatenate([bin_mass[:, lo:hi].astype(jnp.bfloat16), high, low], axis=0)

    def unpack(message):
        message = message.astype(jnp.float32)
        winds = message[local_bins : local_bins + 2] + message[local_bins + 2 :]
        return message[:local_bins], winds[0], winds[1]

    q_left, wx_left, wy_left = unpack(lax.ppermute(rim(width_x - depth, width_x), "tiles", up))
    q_right, wx_right, wy_right = unpack(lax.ppermute(rim(0, depth), "tiles", down))
    wx = jnp.concatenate([wx_left, wind_x, wx_right], axis=0)
    wy = jnp.concatenate([wy_left, wind_y, wy_right], axis=0)
    block = max(d for d in range(1, 34) if local_bins % d == 0)
    rim_spec = pl.BlockSpec((block, depth, width_z, width_y), lambda i: (i, 0, 0, 0))
    own_spec = pl.BlockSpec((block, width_x, width_z, width_y), lambda i: (i, 0, 0, 0))
    wind_spec = pl.BlockSpec(wx.shape, lambda i: (0, 0, 0))
    cells = local_bins * width_x * width_z * width_y
    return pl.pallas_call(
        functools.partial(advect_kernel, section_weights),
        out_shape=jax.ShapeDtypeStruct(bin_mass.shape, bin_mass.dtype),
        grid=(local_bins // block,),
        in_specs=[own_spec, rim_spec, rim_spec, wind_spec, wind_spec],
        out_specs=own_spec,
        cost_estimate=pl.CostEstimate(flops=80 * cells, bytes_accessed=20 * cells, transcendentals=0),
    )(bin_mass, q_left, q_right, wx, wy)


def shifted(block, axis, distance):
    devices = range(lax.axis_size(axis))
    route = [(i - distance, i) for i in devices if i - distance in devices]
    return lax.ppermute(block, axis, route)


def tendency(center_cells, left_cells, right_cells, wind_x, wind_y):
    south_cells = jnp.roll(center_cells, 1, axis=3)
    north_cells = jnp.roll(center_cells, -1, axis=3)
    along_x = jnp.maximum(wind_x, 0.0) * (center_cells - left_cells) + jnp.minimum(wind_x, 0.0) * (
        right_cells - center_cells
    )
    along_y = jnp.maximum(wind_y, 0.0) * (center_cells - south_cells) + jnp.minimum(wind_y, 0.0) * (
        north_cells - center_cells
    )
    return -along_x - along_y


def coupling_table(bin_order, kernel_index, collision_kernels):
    class_count = kernel_index.shape[0]
    table_count = collision_kernels.shape[0]
    class_bins = collision_kernels.shape[1]
    bin_class = bin_order // class_bins
    bin_within = bin_order % class_bins
    kernel_pick = (kernel_index[:, :, None] == lax.iota(jnp.int32, table_count)).astype(jnp.float32)
    block_table = jnp.einsum(
        "ack,kmn->acmn", kernel_pick, collision_kernels.astype(jnp.float32), precision=highest
    )
    class_hot = (bin_class[:, None] == lax.iota(jnp.int32, class_count)).astype(jnp.float32)
    within_hot = (bin_within[:, None] == lax.iota(jnp.int32, class_bins)).astype(jnp.float32)
    row_table = jnp.einsum("bm,acmn->bacn", within_hot, block_table, precision=highest)
    row_table = jnp.einsum("ba,bacn->bcn", class_hot, row_table, precision=highest)
    coupling = jnp.einsum("bcn,dc,dn->bd", row_table, class_hot, within_hot, precision=highest)
    same_class = jnp.dot(class_hot, class_hot.T, precision=highest)
    return jnp.concatenate([coupling, same_class], axis=0).astype(jnp.bfloat16)


def collide(table, first, tie=None):
    all_bins = table.shape[1]
    iterate = first
    for substep in range(SUB):
        if tie is not None and substep == SUB // 2:
            iterate, tie = lax.optimization_barrier((iterate, tie))
        products = jnp.dot(table, iterate.astype(jnp.bfloat16), preferred_element_type=jnp.float32)
        iterate = iterate + collision_rate * products[all_bins:] * products[:all_bins]
    change = (iterate - first).astype(jnp.bfloat16)
    return change if tie is None else (change, tie)


def spread_collision(grown, bin_order, kernel_index, collision_kernels):
    local_bins, width_x, width_z, width_y = grown.shape
    table = coupling_table(bin_order, kernel_index, collision_kernels)
    all_bins = table.shape[1]
    start = grown.astype(jnp.bfloat16).reshape(local_bins, width_x, width_z * width_y)
    cell_block = lax.all_to_all(start, "bins", split_axis=2, concat_axis=0, tiled=True)
    block_shape = cell_block.shape
    first = cell_block.reshape(all_bins, -1).astype(jnp.float32)
    change = collide(table, first).reshape(block_shape)
    change = lax.all_to_all(change, "bins", split_axis=0, concat_axis=2, tiled=True)
    return change.reshape(local_bins, width_x, width_z, width_y).astype(jnp.float32)


def paired_collision(grown, bin_order, kernel_index, collision_kernels):
    local_bins, width_x, width_z, width_y = grown.shape
    swap = [(0, 1), (1, 0)]
    me = lax.axis_index("bins")
    order = lax.dynamic_slice_in_dim(
        jnp.concatenate([bin_order, bin_order]), me * local_bins, 2 * local_bins
    )
    table = coupling_table(order, kernel_index, collision_kernels)
    halves = grown.astype(jnp.bfloat16).reshape(local_bins, 2, width_x // 2, width_z, width_y)
    own = lax.dynamic_index_in_dim(halves, me, axis=1, keepdims=False)
    away = lax.dynamic_index_in_dim(halves, 1 - me, axis=1, keepdims=False)
    kept, returned = [], []
    for chunk in range(width_x // 2):
        arrived = lax.ppermute(away[:, chunk], "bins", swap)
        first = jnp.concatenate([own[:, chunk], arrived], axis=0).reshape(2 * local_bins, -1).astype(jnp.float32)
        if returned:
            change, returned[-1] = collide(table, first, returned[-1])
        else:
            change = collide(table, first)
        change = change.reshape(2 * local_bins, width_z, width_y)
        returned.append(lax.ppermute(change[local_bins:], "bins", swap))
        kept.append(change[:local_bins])
    pair = jnp.stack([jnp.stack(kept, axis=1), jnp.stack(returned, axis=1)], axis=1)
    pair = jnp.where(me == 0, pair, pair[:, ::-1])
    return pair.reshape(local_bins, width_x, width_z, width_y).astype(jnp.float32)

def body(
    bin_mass,
    wind_east,
    wind_north,
    supersaturation,
    potential_temp,
    terrain_height,
    fall_speed,
    growth_rate,
    latent_factor,
    bin_order,
    kernel_index,
    collision_kernels,
):
    local_bins, width_x, width_z, width_y = bin_mass.shape
    levels = lax.axis_index("vert") * width_z + lax.iota(jnp.int32, width_z)
    open_cells = (levels[None, :, None] >= terrain_height[:, None, :]).astype(jnp.float32)
    wind_x = wind_east * open_cells
    wind_y = wind_north * open_cells
    section_weights = (1.0 / 3.0, 0.5, 1.0)
    if width_x >= len(section_weights):
        section_field = advect_kernel_call(bin_mass, wind_x, wind_y, section_weights)
    else:
        section_field = bin_mass
        for weight_now in section_weights:
            extended = extended_2(section_field, (("tiles", 1),), 1, jnp.bfloat16)
            section_field = bin_mass + weight_now * tendency(
                extended[:, 1:-1], extended[:, :-2], extended[:, 2:], wind_x, wind_y
            )
    rim_above = shifted(section_field[:, :, :1, :], "vert", -1)
    from_above = jnp.concatenate([section_field[:, :, 1:], rim_above], axis=2)
    speed = fall_speed[:, None, None, None]
    settled = (1.0 - speed) * section_field + speed * from_above
    growth = growth_rate[:, None, None, None]
    partial = (
        jnp.sum(growth * settled, axis=0),
        jnp.sum(latent_factor[:, None, None, None] * growth * settled, axis=0),
    )
    bin_devices = lax.axis_size("bins")
    if bin_devices == 2:
        swap = [(0, 1), (1, 0)]
        other = lax.ppermute(jnp.stack(partial), "bins", swap)
        uptake, heating = partial[0] + other[0], partial[1] + other[1]
    else:
        uptake, heating = lax.psum(partial, "bins")
    midway = supersaturation * jnp.exp(-0.5 * condense_rate * uptake)
    grown = settled * (1.0 + growth_gain * growth * midway)
    temp_next = potential_temp + heating_gain * midway * heating
    vapor_next = supersaturation * jnp.exp(-condense_rate * uptake)
    if bin_devices == 2 and width_x % 2 == 0:
        change = paired_collision(grown, bin_order, kernel_index, collision_kernels)
    else:
        change = spread_collision(grown, bin_order, kernel_index, collision_kernels)
    mass_next = (grown + change) * open_cells
    return (mass_next, temp_next, vapor_next)


def solution(mesh):
    return jax.shard_map(
        body,
        mesh=mesh,
        in_specs=(
            P("bins", ("groups", "tiles"), "vert", None),
            P(("groups", "tiles"), "vert", None),
            P(("groups", "tiles"), "vert", None),
            P(("groups", "tiles"), "vert", None),
            P(("groups", "tiles"), "vert", None),
            P(("groups", "tiles"), None),
            P("bins"),
            P("bins"),
            P("bins"),
            P(),
            P(),
            P(),
        ),
        out_specs=(
            P("bins", ("groups", "tiles"), "vert", None),
            P(("groups", "tiles"), "vert", None),
            P(("groups", "tiles"), "vert", None),
        ),
        check_vma=False,
    )
```

```python
import functools

import jax
import jax.numpy as jnp
from jax import lax
from jax.experimental import pallas as pl
from jax.experimental.pallas import tpu as pltpu
from jax.sharding import PartitionSpec as P

SUB = 8


collision_rate = 0.001
condense_rate = 0.02
heating_gain = 0.03
growth_gain = 0.5
highest = lax.Precision.HIGHEST


def extended_2(array, sides, width, link=jnp.float32):
    for axis, dim in sides:
        size, length = (lax.axis_size(axis), array.shape[dim])
        up = [(i, (i + 1) % size) for i in range(size - 1)]
        down = [(j, i) for i, j in up]
        last = lax.slice_in_dim(array, length - width, length, axis=dim)
        first = lax.slice_in_dim(array, 0, width, axis=dim)
        before = lax.ppermute(last.astype(link), axis, up).astype(array.dtype)
        after = lax.ppermute(first.astype(link), axis, down).astype(array.dtype)
        array = jnp.concatenate([before, array, after], axis=dim)
    return array


def advect_kernel(weights, q_ref, left_ref, right_ref, wx_ref, wy_ref, out_ref, bottom_ref):
    depth = len(weights)
    width = q_ref.shape[1]
    field = jnp.concatenate([left_ref[...], q_ref[...], right_ref[...]], axis=1)
    wx = wx_ref[...]
    wy = wy_ref[...]
    section = field
    for stage, weight_now in enumerate(weights, start=1):
        span = width + 2 * (depth - stage)
        center = section[:, 1 : 1 + span]
        west = section[:, 0:span]
        east = section[:, 2 : 2 + span]
        south = pltpu.roll(center, 1, 3)
        north = pltpu.roll(center, center.shape[3] - 1, 3)
        wind_a = wx[stage : stage + span]
        wind_b = wy[stage : stage + span]
        along_x = jnp.maximum(wind_a, 0.0) * (center - west) + jnp.minimum(wind_a, 0.0) * (east - center)
        along_y = jnp.maximum(wind_b, 0.0) * (center - south) + jnp.minimum(wind_b, 0.0) * (north - center)
        section = field[:, stage : stage + span] + weight_now * (-along_x - along_y)
    out_ref[...] = section
    bottom_ref[...] = section[:, :, :1]


def advect_kernel_call(bin_mass, wind_x, wind_y, section_weights):
    local_bins, width_x, width_z, width_y = bin_mass.shape
    depth = len(section_weights)
    tiles = lax.axis_size("tiles")
    up = [(i, i + 1) for i in range(tiles - 1)]
    down = [(j, i) for i, j in up]

    def rim(lo, hi):
        winds = jnp.stack([wind_x[lo:hi], wind_y[lo:hi]])
        high = winds.astype(jnp.bfloat16)
        low = (winds - high.astype(jnp.float32)).astype(jnp.bfloat16)
        return jnp.concatenate([bin_mass[:, lo:hi].astype(jnp.bfloat16), high, low], axis=0)

    def unpack(message):
        message = message.astype(jnp.float32)
        winds = message[local_bins : local_bins + 2] + message[local_bins + 2 :]
        return message[:local_bins], winds[0], winds[1]

    q_left, wx_left, wy_left = unpack(lax.ppermute(rim(width_x - depth, width_x), "tiles", up))
    q_right, wx_right, wy_right = unpack(lax.ppermute(rim(0, depth), "tiles", down))
    wx = jnp.concatenate([wx_left, wind_x, wx_right], axis=0)
    wy = jnp.concatenate([wy_left, wind_y, wy_right], axis=0)
    block = max(d for d in range(1, 34) if local_bins % d == 0)
    rim_spec = pl.BlockSpec((block, depth, width_z, width_y), lambda i: (i, 0, 0, 0))
    own_spec = pl.BlockSpec((block, width_x, width_z, width_y), lambda i: (i, 0, 0, 0))
    wind_spec = pl.BlockSpec(wx.shape, lambda i: (0, 0, 0))
    cells = local_bins * width_x * width_z * width_y
    return pl.pallas_call(
        functools.partial(advect_kernel, section_weights),
        out_shape=(
            jax.ShapeDtypeStruct(bin_mass.shape, bin_mass.dtype),
            jax.ShapeDtypeStruct((local_bins, width_x, 1, width_y), bin_mass.dtype),
        ),
        grid=(local_bins // block,),
        in_specs=[own_spec, rim_spec, rim_spec, wind_spec, wind_spec],
        out_specs=(own_spec, pl.BlockSpec((block, width_x, 1, width_y), lambda i: (i, 0, 0, 0))),
        cost_estimate=pl.CostEstimate(flops=80 * cells, bytes_accessed=20 * cells, transcendentals=0),
    )(bin_mass, q_left, q_right, wx, wy)


def shifted(block, axis, distance):
    devices = range(lax.axis_size(axis))
    route = [(i - distance, i) for i in devices if i - distance in devices]
    return lax.ppermute(block, axis, route)


def tendency(center_cells, left_cells, right_cells, wind_x, wind_y):
    south_cells = jnp.roll(center_cells, 1, axis=3)
    north_cells = jnp.roll(center_cells, -1, axis=3)
    along_x = jnp.maximum(wind_x, 0.0) * (center_cells - left_cells) + jnp.minimum(wind_x, 0.0) * (
        right_cells - center_cells
    )
    along_y = jnp.maximum(wind_y, 0.0) * (center_cells - south_cells) + jnp.minimum(wind_y, 0.0) * (
        north_cells - center_cells
    )
    return -along_x - along_y


def coupling_table(bin_order, kernel_index, collision_kernels):
    class_count = kernel_index.shape[0]
    table_count = collision_kernels.shape[0]
    class_bins = collision_kernels.shape[1]
    bin_class = bin_order // class_bins
    bin_within = bin_order % class_bins
    kernel_pick = (kernel_index[:, :, None] == lax.iota(jnp.int32, table_count)).astype(jnp.float32)
    block_table = jnp.einsum(
        "ack,kmn->acmn", kernel_pick, collision_kernels.astype(jnp.float32), precision=highest
    )
    class_hot = (bin_class[:, None] == lax.iota(jnp.int32, class_count)).astype(jnp.float32)
    within_hot = (bin_within[:, None] == lax.iota(jnp.int32, class_bins)).astype(jnp.float32)
    row_table = jnp.einsum("bm,acmn->bacn", within_hot, block_table, precision=highest)
    row_table = jnp.einsum("ba,bacn->bcn", class_hot, row_table, precision=highest)
    coupling = jnp.einsum("bcn,dc,dn->bd", row_table, class_hot, within_hot, precision=highest)
    same_class = jnp.dot(class_hot, class_hot.T, precision=highest)
    return jnp.concatenate([coupling, same_class], axis=0).astype(jnp.bfloat16)


def collide(table, first, tie=None):
    all_bins = table.shape[1]
    iterate = first
    for substep in range(SUB):
        if tie is not None and substep == SUB // 2:
            iterate, tie = lax.optimization_barrier((iterate, tie))
        products = jnp.dot(table, iterate.astype(jnp.bfloat16), preferred_element_type=jnp.float32)
        iterate = iterate + collision_rate * products[all_bins:] * products[:all_bins]
    change = (iterate - first).astype(jnp.bfloat16)
    return change if tie is None else (change, tie)


def spread_collision(grown, bin_order, kernel_index, collision_kernels):
    local_bins, width_x, width_z, width_y = grown.shape
    table = coupling_table(bin_order, kernel_index, collision_kernels)
    all_bins = table.shape[1]
    start = grown.astype(jnp.bfloat16).reshape(local_bins, width_x, width_z * width_y)
    cell_block = lax.all_to_all(start, "bins", split_axis=2, concat_axis=0, tiled=True)
    block_shape = cell_block.shape
    first = cell_block.reshape(all_bins, -1).astype(jnp.float32)
    change = collide(table, first).reshape(block_shape)
    change = lax.all_to_all(change, "bins", split_axis=0, concat_axis=2, tiled=True)
    return change.reshape(local_bins, width_x, width_z, width_y).astype(jnp.float32)


def paired_collision(grown, bin_order, kernel_index, collision_kernels):
    local_bins, width_x, width_z, width_y = grown.shape
    swap = [(0, 1), (1, 0)]
    me = lax.axis_index("bins")
    order = lax.dynamic_slice_in_dim(
        jnp.concatenate([bin_order, bin_order]), me * local_bins, 2 * local_bins
    )
    table = coupling_table(order, kernel_index, collision_kernels)
    halves = grown.astype(jnp.bfloat16).reshape(local_bins, 2, width_x // 2, width_z, width_y)
    own = lax.dynamic_index_in_dim(halves, me, axis=1, keepdims=False)
    away = lax.dynamic_index_in_dim(halves, 1 - me, axis=1, keepdims=False)
    kept, returned = [], []
    for chunk in range(width_x // 2):
        send = away[:, chunk]
        if chunk:
            send, _ = lax.optimization_barrier((send, arrived))
        arrived = lax.ppermute(send, "bins", swap)
        first = jnp.concatenate([own[:, chunk], arrived], axis=0).reshape(2 * local_bins, -1).astype(jnp.float32)
        if returned:
            change, returned[-1] = collide(table, first, returned[-1])
        else:
            change = collide(table, first)
        change = change.reshape(2 * local_bins, width_z, width_y)
        returned.append(lax.ppermute(change[local_bins:], "bins", swap))
        kept.append(change[:local_bins])
    pair = jnp.stack([jnp.stack(kept, axis=1), jnp.stack(returned, axis=1)], axis=1)
    pair = jnp.where(me == 0, pair, pair[:, ::-1])
    return pair.reshape(local_bins, width_x, width_z, width_y).astype(jnp.float32)

def body(
    bin_mass,
    wind_east,
    wind_north,
    supersaturation,
    potential_temp,
    terrain_height,
    fall_speed,
    growth_rate,
    latent_factor,
    bin_order,
    kernel_index,
    collision_kernels,
):
    local_bins, width_x, width_z, width_y = bin_mass.shape
    levels = lax.axis_index("vert") * width_z + lax.iota(jnp.int32, width_z)
    open_cells = (levels[None, :, None] >= terrain_height[:, None, :]).astype(jnp.float32)
    wind_x = wind_east * open_cells
    wind_y = wind_north * open_cells
    section_weights = (1.0 / 3.0, 0.5, 1.0)
    if width_x >= len(section_weights):
        section_field, bottom = advect_kernel_call(bin_mass, wind_x, wind_y, section_weights)
    else:
        section_field = bin_mass
        for weight_now in section_weights:
            extended = extended_2(section_field, (("tiles", 1),), 1, jnp.bfloat16)
            section_field = bin_mass + weight_now * tendency(
                extended[:, 1:-1], extended[:, :-2], extended[:, 2:], wind_x, wind_y
            )
        bottom = section_field[:, :, :1, :]
    rim_above = shifted(bottom, "vert", -1)
    from_above = jnp.concatenate([section_field[:, :, 1:], rim_above], axis=2)
    speed = fall_speed[:, None, None, None]
    settled = (1.0 - speed) * section_field + speed * from_above
    growth = growth_rate[:, None, None, None]
    partial = (
        jnp.sum(growth * settled, axis=0),
        jnp.sum(latent_factor[:, None, None, None] * growth * settled, axis=0),
    )
    bin_devices = lax.axis_size("bins")
    if bin_devices == 2:
        swap = [(0, 1), (1, 0)]
        other = lax.ppermute(jnp.stack(partial), "bins", swap)
        uptake, heating = partial[0] + other[0], partial[1] + other[1]
    else:
        uptake, heating = lax.psum(partial, "bins")
    midway = supersaturation * jnp.exp(-0.5 * condense_rate * uptake)
    grown = settled * (1.0 + growth_gain * growth * midway)
    temp_next = potential_temp + heating_gain * midway * heating
    vapor_next = supersaturation * jnp.exp(-condense_rate * uptake)
    if bin_devices == 2 and width_x % 2 == 0:
        change = paired_collision(grown, bin_order, kernel_index, collision_kernels)
    else:
        change = spread_collision(grown, bin_order, kernel_index, collision_kernels)
    mass_next = (grown + change) * open_cells
    return (mass_next, temp_next, vapor_next)


def solution(mesh):
    return jax.shard_map(
        body,
        mesh=mesh,
        in_specs=(
            P("bins", ("groups", "tiles"), "vert", None),
            P(("groups", "tiles"), "vert", None),
            P(("groups", "tiles"), "vert", None),
            P(("groups", "tiles"), "vert", None),
            P(("groups", "tiles"), "vert", None),
            P(("groups", "tiles"), None),
            P("bins"),
            P("bins"),
            P("bins"),
            P(),
            P(),
            P(),
        ),
        out_specs=(
            P("bins", ("groups", "tiles"), "vert", None),
            P(("groups", "tiles"), "vert", None),
            P(("groups", "tiles"), "vert", None),
        ),
        check_vma=False,
    )
```

```python
import functools

import jax
import jax.numpy as jnp
from jax import lax
from jax.experimental import pallas as pl
from jax.experimental.pallas import tpu as pltpu
from jax.sharding import PartitionSpec as P

SUB = 8


collision_rate = 0.001
condense_rate = 0.02
heating_gain = 0.03
growth_gain = 0.5
highest = lax.Precision.HIGHEST


def extended_2(array, sides, width, link=jnp.float32):
    for axis, dim in sides:
        size, length = (lax.axis_size(axis), array.shape[dim])
        up = [(i, (i + 1) % size) for i in range(size - 1)]
        down = [(j, i) for i, j in up]
        last = lax.slice_in_dim(array, length - width, length, axis=dim)
        first = lax.slice_in_dim(array, 0, width, axis=dim)
        before = lax.ppermute(last.astype(link), axis, up).astype(array.dtype)
        after = lax.ppermute(first.astype(link), axis, down).astype(array.dtype)
        array = jnp.concatenate([before, array, after], axis=dim)
    return array


def advect_kernel(weights, q_ref, left_ref, right_ref, *refs):
    left_winds, right_winds = refs[0:4], refs[4:8]
    wx_ref, wy_ref, out_ref, bottom_ref = refs[8:]
    depth = len(weights)
    width = q_ref.shape[1]

    def widened(ref):
        return ref[...].astype(jnp.float32)

    def winds(rows):
        return [widened(rows[k])[0] + widened(rows[k + 2])[0] for k in (0, 1)]

    (wx_left, wy_left), (wx_right, wy_right) = winds(left_winds), winds(right_winds)
    field = jnp.concatenate([widened(left_ref), q_ref[...], widened(right_ref)], axis=1)
    wx = jnp.concatenate([wx_left, wx_ref[...], wx_right], axis=0)
    wy = jnp.concatenate([wy_left, wy_ref[...], wy_right], axis=0)
    section = field
    for stage, weight_now in enumerate(weights, start=1):
        span = width + 2 * (depth - stage)
        center = section[:, 1 : 1 + span]
        west = section[:, 0:span]
        east = section[:, 2 : 2 + span]
        south = pltpu.roll(center, 1, 3)
        north = pltpu.roll(center, center.shape[3] - 1, 3)
        wind_a = wx[stage : stage + span]
        wind_b = wy[stage : stage + span]
        along_x = jnp.maximum(wind_a, 0.0) * (center - west) + jnp.minimum(wind_a, 0.0) * (east - center)
        along_y = jnp.maximum(wind_b, 0.0) * (center - south) + jnp.minimum(wind_b, 0.0) * (north - center)
        section = field[:, stage : stage + span] + weight_now * (-along_x - along_y)
    out_ref[...] = section
    bottom_ref[...] = section[:, :, :1]


def advect_kernel_call(bin_mass, wind_x, wind_y, section_weights):
    local_bins, width_x, width_z, width_y = bin_mass.shape
    depth = len(section_weights)
    tiles = lax.axis_size("tiles")
    up = [(i, i + 1) for i in range(tiles - 1)]
    down = [(j, i) for i, j in up]

    def rim(lo, hi):
        winds = jnp.stack([wind_x[lo:hi], wind_y[lo:hi]])
        high = winds.astype(jnp.bfloat16)
        low = (winds - high.astype(jnp.float32)).astype(jnp.bfloat16)
        return jnp.concatenate([bin_mass[:, lo:hi].astype(jnp.bfloat16), high, low], axis=0)

    left = lax.ppermute(rim(width_x - depth, width_x), "tiles", up)
    right = lax.ppermute(rim(0, depth), "tiles", down)
    block = max(d for d in range(1, 34) if local_bins % d == 0)
    rim_spec = pl.BlockSpec((block, depth, width_z, width_y), lambda i: (i, 0, 0, 0))
    row_specs = [
        pl.BlockSpec((1, depth, width_z, width_y), lambda i, row=local_bins + k: (row, 0, 0, 0))
        for k in range(4)
    ]
    own_spec = pl.BlockSpec((block, width_x, width_z, width_y), lambda i: (i, 0, 0, 0))
    wind_spec = pl.BlockSpec(wind_x.shape, lambda i: (0, 0, 0))
    cells = local_bins * width_x * width_z * width_y
    return pl.pallas_call(
        functools.partial(advect_kernel, section_weights),
        out_shape=(
            jax.ShapeDtypeStruct(bin_mass.shape, bin_mass.dtype),
            jax.ShapeDtypeStruct((local_bins, width_x, 1, width_y), bin_mass.dtype),
        ),
        grid=(local_bins // block,),
        in_specs=[own_spec, rim_spec, rim_spec] + row_specs + row_specs + [wind_spec, wind_spec],
        out_specs=(own_spec, pl.BlockSpec((block, width_x, 1, width_y), lambda i: (i, 0, 0, 0))),
        cost_estimate=pl.CostEstimate(flops=80 * cells, bytes_accessed=20 * cells, transcendentals=0),
    )(bin_mass, left, right, *([left] * 4), *([right] * 4), wind_x, wind_y)

def shifted(block, axis, distance):
    devices = range(lax.axis_size(axis))
    route = [(i - distance, i) for i in devices if i - distance in devices]
    return lax.ppermute(block, axis, route)


def tendency(center_cells, left_cells, right_cells, wind_x, wind_y):
    south_cells = jnp.roll(center_cells, 1, axis=3)
    north_cells = jnp.roll(center_cells, -1, axis=3)
    along_x = jnp.maximum(wind_x, 0.0) * (center_cells - left_cells) + jnp.minimum(wind_x, 0.0) * (
        right_cells - center_cells
    )
    along_y = jnp.maximum(wind_y, 0.0) * (center_cells - south_cells) + jnp.minimum(wind_y, 0.0) * (
        north_cells - center_cells
    )
    return -along_x - along_y


def coupling_table(bin_order, kernel_index, collision_kernels):
    class_count = kernel_index.shape[0]
    table_count = collision_kernels.shape[0]
    class_bins = collision_kernels.shape[1]
    bin_class = bin_order // class_bins
    bin_within = bin_order % class_bins
    kernel_pick = (kernel_index[:, :, None] == lax.iota(jnp.int32, table_count)).astype(jnp.float32)
    block_table = jnp.einsum(
        "ack,kmn->acmn", kernel_pick, collision_kernels.astype(jnp.float32), precision=highest
    )
    class_hot = (bin_class[:, None] == lax.iota(jnp.int32, class_count)).astype(jnp.float32)
    within_hot = (bin_within[:, None] == lax.iota(jnp.int32, class_bins)).astype(jnp.float32)
    row_table = jnp.einsum("bm,acmn->bacn", within_hot, block_table, precision=highest)
    row_table = jnp.einsum("ba,bacn->bcn", class_hot, row_table, precision=highest)
    coupling = jnp.einsum("bcn,dc,dn->bd", row_table, class_hot, within_hot, precision=highest)
    same_class = jnp.dot(class_hot, class_hot.T, precision=highest)
    return jnp.concatenate([coupling, same_class], axis=0).astype(jnp.bfloat16)


def collide(table, first, tie=None):
    all_bins = table.shape[1]
    iterate = first
    for substep in range(SUB):
        if tie is not None and substep == SUB // 2:
            iterate, tie = lax.optimization_barrier((iterate, tie))
        products = jnp.dot(table, iterate.astype(jnp.bfloat16), preferred_element_type=jnp.float32)
        iterate = iterate + collision_rate * products[all_bins:] * products[:all_bins]
    change = (iterate - first).astype(jnp.bfloat16)
    return change if tie is None else (change, tie)


def spread_collision(grown, bin_order, kernel_index, collision_kernels):
    local_bins, width_x, width_z, width_y = grown.shape
    table = coupling_table(bin_order, kernel_index, collision_kernels)
    all_bins = table.shape[1]
    start = grown.astype(jnp.bfloat16).reshape(local_bins, width_x, width_z * width_y)
    cell_block = lax.all_to_all(start, "bins", split_axis=2, concat_axis=0, tiled=True)
    block_shape = cell_block.shape
    first = cell_block.reshape(all_bins, -1).astype(jnp.float32)
    change = collide(table, first).reshape(block_shape)
    change = lax.all_to_all(change, "bins", split_axis=0, concat_axis=2, tiled=True)
    return change.reshape(local_bins, width_x, width_z, width_y).astype(jnp.float32)


def paired_collision(grown, bin_order, kernel_index, collision_kernels):
    local_bins, width_x, width_z, width_y = grown.shape
    swap = [(0, 1), (1, 0)]
    me = lax.axis_index("bins")
    order = lax.dynamic_slice_in_dim(
        jnp.concatenate([bin_order, bin_order]), me * local_bins, 2 * local_bins
    )
    table = coupling_table(order, kernel_index, collision_kernels)
    halves = grown.astype(jnp.bfloat16).reshape(local_bins, 2, width_x // 2, width_z, width_y)
    own = lax.dynamic_index_in_dim(halves, me, axis=1, keepdims=False)
    away = lax.dynamic_index_in_dim(halves, 1 - me, axis=1, keepdims=False)
    kept, returned = [], []
    for chunk in range(width_x // 2):
        arrived = lax.ppermute(away[:, chunk], "bins", swap)
        first = jnp.concatenate([own[:, chunk], arrived], axis=0).reshape(2 * local_bins, -1).astype(jnp.float32)
        if returned:
            change, returned[-1] = collide(table, first, returned[-1])
        else:
            change = collide(table, first)
        change = change.reshape(2 * local_bins, width_z, width_y)
        returned.append(lax.ppermute(change[local_bins:], "bins", swap))
        kept.append(change[:local_bins])
    pair = jnp.stack([jnp.stack(kept, axis=1), jnp.stack(returned, axis=1)], axis=1)
    pair = jnp.where(me == 0, pair, pair[:, ::-1])
    return pair.reshape(local_bins, width_x, width_z, width_y).astype(jnp.float32)

def body(
    bin_mass,
    wind_east,
    wind_north,
    supersaturation,
    potential_temp,
    terrain_height,
    fall_speed,
    growth_rate,
    latent_factor,
    bin_order,
    kernel_index,
    collision_kernels,
):
    local_bins, width_x, width_z, width_y = bin_mass.shape
    levels = lax.axis_index("vert") * width_z + lax.iota(jnp.int32, width_z)
    open_cells = (levels[None, :, None] >= terrain_height[:, None, :]).astype(jnp.float32)
    wind_x = wind_east * open_cells
    wind_y = wind_north * open_cells
    section_weights = (1.0 / 3.0, 0.5, 1.0)
    if width_x >= len(section_weights):
        section_field, bottom = advect_kernel_call(bin_mass, wind_x, wind_y, section_weights)
    else:
        section_field = bin_mass
        for weight_now in section_weights:
            extended = extended_2(section_field, (("tiles", 1),), 1, jnp.bfloat16)
            section_field = bin_mass + weight_now * tendency(
                extended[:, 1:-1], extended[:, :-2], extended[:, 2:], wind_x, wind_y
            )
        bottom = section_field[:, :, :1, :]
    rim_above = shifted(bottom, "vert", -1)
    from_above = jnp.concatenate([section_field[:, :, 1:], rim_above], axis=2)
    speed = fall_speed[:, None, None, None]
    settled = (1.0 - speed) * section_field + speed * from_above
    growth = growth_rate[:, None, None, None]
    partial = (
        jnp.sum(growth * settled, axis=0),
        jnp.sum(latent_factor[:, None, None, None] * growth * settled, axis=0),
    )
    bin_devices = lax.axis_size("bins")
    if bin_devices == 2:
        swap = [(0, 1), (1, 0)]
        other = lax.ppermute(jnp.stack(partial), "bins", swap)
        uptake, heating = partial[0] + other[0], partial[1] + other[1]
    else:
        uptake, heating = lax.psum(partial, "bins")
    midway = supersaturation * jnp.exp(-0.5 * condense_rate * uptake)
    grown = settled * (1.0 + growth_gain * growth * midway)
    temp_next = potential_temp + heating_gain * midway * heating
    vapor_next = supersaturation * jnp.exp(-condense_rate * uptake)
    if bin_devices == 2 and width_x % 2 == 0:
        change = paired_collision(grown, bin_order, kernel_index, collision_kernels)
    else:
        change = spread_collision(grown, bin_order, kernel_index, collision_kernels)
    mass_next = (grown + change) * open_cells
    return (mass_next, temp_next, vapor_next)


def solution(mesh):
    return jax.shard_map(
        body,
        mesh=mesh,
        in_specs=(
            P("bins", ("groups", "tiles"), "vert", None),
            P(("groups", "tiles"), "vert", None),
            P(("groups", "tiles"), "vert", None),
            P(("groups", "tiles"), "vert", None),
            P(("groups", "tiles"), "vert", None),
            P(("groups", "tiles"), None),
            P("bins"),
            P("bins"),
            P("bins"),
            P(),
            P(),
            P(),
        ),
        out_specs=(
            P("bins", ("groups", "tiles"), "vert", None),
            P(("groups", "tiles"), "vert", None),
            P(("groups", "tiles"), "vert", None),
        ),
        check_vma=False,
    )
```

```python
import functools

import jax
import jax.numpy as jnp
from jax import lax
from jax.experimental import pallas as pl
from jax.experimental.pallas import tpu as pltpu
from jax.sharding import PartitionSpec as P

SUB = 8


collision_rate = 0.001
condense_rate = 0.02
heating_gain = 0.03
growth_gain = 0.5
highest = lax.Precision.HIGHEST


def extended_2(array, sides, width, link=jnp.float32):
    for axis, dim in sides:
        size, length = (lax.axis_size(axis), array.shape[dim])
        up = [(i, (i + 1) % size) for i in range(size - 1)]
        down = [(j, i) for i, j in up]
        last = lax.slice_in_dim(array, length - width, length, axis=dim)
        first = lax.slice_in_dim(array, 0, width, axis=dim)
        before = lax.ppermute(last.astype(link), axis, up).astype(array.dtype)
        after = lax.ppermute(first.astype(link), axis, down).astype(array.dtype)
        array = jnp.concatenate([before, array, after], axis=dim)
    return array


def rim_kernel(depth, q_ref, wx_ref, wy_ref, left_ref, right_ref):
    local_bins, width_x = q_ref.shape[:2]
    for out_ref, lo in ((left_ref, width_x - depth), (right_ref, 0)):
        out_ref[0:local_bins] = q_ref[:, lo : lo + depth].astype(out_ref.dtype)
        for k, wind_ref in enumerate((wx_ref, wy_ref)):
            wind = wind_ref[lo : lo + depth]
            high = wind.astype(out_ref.dtype)
            low = (wind - high.astype(jnp.float32)).astype(out_ref.dtype)
            out_ref[local_bins + k] = high
            out_ref[local_bins + 2 + k] = low


def rims(bin_mass, wind_x, wind_y, depth):
    local_bins, width_x, width_z, width_y = bin_mass.shape
    shape = jax.ShapeDtypeStruct((local_bins + 4, depth, width_z, width_y), jnp.bfloat16)
    return pl.pallas_call(
        functools.partial(rim_kernel, depth),
        out_shape=(shape, shape),
    )(bin_mass, wind_x, wind_y)


def advect_kernel(weights, q_ref, left_ref, right_ref, *refs):
    left_winds, right_winds = refs[0:4], refs[4:8]
    wx_ref, wy_ref, out_ref, bottom_ref = refs[8:]
    depth = len(weights)
    width = q_ref.shape[1]

    def widened(ref):
        return ref[...].astype(jnp.float32)

    def winds(rows):
        return [widened(rows[k])[0] + widened(rows[k + 2])[0] for k in (0, 1)]

    (wx_left, wy_left), (wx_right, wy_right) = winds(left_winds), winds(right_winds)
    field = jnp.concatenate([widened(left_ref), q_ref[...], widened(right_ref)], axis=1)
    wx = jnp.concatenate([wx_left, wx_ref[...], wx_right], axis=0)
    wy = jnp.concatenate([wy_left, wy_ref[...], wy_right], axis=0)
    section = field
    for stage, weight_now in enumerate(weights, start=1):
        span = width + 2 * (depth - stage)
        center = section[:, 1 : 1 + span]
        west = section[:, 0:span]
        east = section[:, 2 : 2 + span]
        south = pltpu.roll(center, 1, 3)
        north = pltpu.roll(center, center.shape[3] - 1, 3)
        wind_a = wx[stage : stage + span]
        wind_b = wy[stage : stage + span]
        along_x = jnp.maximum(wind_a, 0.0) * (center - west) + jnp.minimum(wind_a, 0.0) * (east - center)
        along_y = jnp.maximum(wind_b, 0.0) * (center - south) + jnp.minimum(wind_b, 0.0) * (north - center)
        section = field[:, stage : stage + span] + weight_now * (-along_x - along_y)
    out_ref[...] = section
    bottom_ref[...] = section[:, :, :1]


def advect_kernel_call(bin_mass, wind_x, wind_y, section_weights):
    local_bins, width_x, width_z, width_y = bin_mass.shape
    depth = len(section_weights)
    tiles = lax.axis_size("tiles")
    up = [(i, i + 1) for i in range(tiles - 1)]
    down = [(j, i) for i, j in up]

    left, right = (
        lax.ppermute(message, "tiles", pairs)
        for message, pairs in zip(rims(bin_mass, wind_x, wind_y, depth), (up, down))
    )
    block = max(d for d in range(1, 34) if local_bins % d == 0)
    rim_spec = pl.BlockSpec((block, depth, width_z, width_y), lambda i: (i, 0, 0, 0))
    row_specs = [
        pl.BlockSpec((1, depth, width_z, width_y), lambda i, row=local_bins + k: (row, 0, 0, 0))
        for k in range(4)
    ]
    own_spec = pl.BlockSpec((block, width_x, width_z, width_y), lambda i: (i, 0, 0, 0))
    wind_spec = pl.BlockSpec(wind_x.shape, lambda i: (0, 0, 0))
    cells = local_bins * width_x * width_z * width_y
    return pl.pallas_call(
        functools.partial(advect_kernel, section_weights),
        out_shape=(
            jax.ShapeDtypeStruct(bin_mass.shape, bin_mass.dtype),
            jax.ShapeDtypeStruct((local_bins, width_x, 1, width_y), bin_mass.dtype),
        ),
        grid=(local_bins // block,),
        in_specs=[own_spec, rim_spec, rim_spec] + row_specs + row_specs + [wind_spec, wind_spec],
        out_specs=(own_spec, pl.BlockSpec((block, width_x, 1, width_y), lambda i: (i, 0, 0, 0))),
        cost_estimate=pl.CostEstimate(flops=80 * cells, bytes_accessed=20 * cells, transcendentals=0),
    )(bin_mass, left, right, *([left] * 4), *([right] * 4), wind_x, wind_y)

def shifted(block, axis, distance):
    devices = range(lax.axis_size(axis))
    route = [(i - distance, i) for i in devices if i - distance in devices]
    return lax.ppermute(block, axis, route)


def tendency(center_cells, left_cells, right_cells, wind_x, wind_y):
    south_cells = jnp.roll(center_cells, 1, axis=3)
    north_cells = jnp.roll(center_cells, -1, axis=3)
    along_x = jnp.maximum(wind_x, 0.0) * (center_cells - left_cells) + jnp.minimum(wind_x, 0.0) * (
        right_cells - center_cells
    )
    along_y = jnp.maximum(wind_y, 0.0) * (center_cells - south_cells) + jnp.minimum(wind_y, 0.0) * (
        north_cells - center_cells
    )
    return -along_x - along_y


def coupling_table(bin_order, kernel_index, collision_kernels):
    class_count = kernel_index.shape[0]
    table_count = collision_kernels.shape[0]
    class_bins = collision_kernels.shape[1]
    bin_class = bin_order // class_bins
    bin_within = bin_order % class_bins
    kernel_pick = (kernel_index[:, :, None] == lax.iota(jnp.int32, table_count)).astype(jnp.float32)
    block_table = jnp.einsum(
        "ack,kmn->acmn", kernel_pick, collision_kernels.astype(jnp.float32), precision=highest
    )
    class_hot = (bin_class[:, None] == lax.iota(jnp.int32, class_count)).astype(jnp.float32)
    within_hot = (bin_within[:, None] == lax.iota(jnp.int32, class_bins)).astype(jnp.float32)
    row_table = jnp.einsum("bm,acmn->bacn", within_hot, block_table, precision=highest)
    row_table = jnp.einsum("ba,bacn->bcn", class_hot, row_table, precision=highest)
    coupling = jnp.einsum("bcn,dc,dn->bd", row_table, class_hot, within_hot, precision=highest)
    same_class = jnp.dot(class_hot, class_hot.T, precision=highest)
    return jnp.concatenate([coupling, same_class], axis=0).astype(jnp.bfloat16)


def collide(table, first, tie=None):
    all_bins = table.shape[1]
    iterate = first
    for substep in range(SUB):
        if tie is not None and substep == SUB // 2:
            iterate, tie = lax.optimization_barrier((iterate, tie))
        products = jnp.dot(table, iterate.astype(jnp.bfloat16), preferred_element_type=jnp.float32)
        iterate = iterate + collision_rate * products[all_bins:] * products[:all_bins]
    change = (iterate - first).astype(jnp.bfloat16)
    return change if tie is None else (change, tie)


def spread_collision(grown, bin_order, kernel_index, collision_kernels):
    local_bins, width_x, width_z, width_y = grown.shape
    table = coupling_table(bin_order, kernel_index, collision_kernels)
    all_bins = table.shape[1]
    start = grown.astype(jnp.bfloat16).reshape(local_bins, width_x, width_z * width_y)
    cell_block = lax.all_to_all(start, "bins", split_axis=2, concat_axis=0, tiled=True)
    block_shape = cell_block.shape
    first = cell_block.reshape(all_bins, -1).astype(jnp.float32)
    change = collide(table, first).reshape(block_shape)
    change = lax.all_to_all(change, "bins", split_axis=0, concat_axis=2, tiled=True)
    return change.reshape(local_bins, width_x, width_z, width_y).astype(jnp.float32)


def paired_collision(grown, bin_order, kernel_index, collision_kernels):
    local_bins, width_x, width_z, width_y = grown.shape
    swap = [(0, 1), (1, 0)]
    me = lax.axis_index("bins")
    order = lax.dynamic_slice_in_dim(
        jnp.concatenate([bin_order, bin_order]), me * local_bins, 2 * local_bins
    )
    table = coupling_table(order, kernel_index, collision_kernels)
    halves = grown.astype(jnp.bfloat16).reshape(local_bins, 2, width_x // 2, width_z, width_y)
    own = lax.dynamic_index_in_dim(halves, me, axis=1, keepdims=False)
    away = lax.dynamic_index_in_dim(halves, 1 - me, axis=1, keepdims=False)
    kept, returned = [], []
    for chunk in range(width_x // 2):
        arrived = lax.ppermute(away[:, chunk], "bins", swap)
        first = jnp.concatenate([own[:, chunk], arrived], axis=0).reshape(2 * local_bins, -1).astype(jnp.float32)
        if returned:
            change, returned[-1] = collide(table, first, returned[-1])
        else:
            change = collide(table, first)
        change = change.reshape(2 * local_bins, width_z, width_y)
        returned.append(lax.ppermute(change[local_bins:], "bins", swap))
        kept.append(change[:local_bins])
    pair = jnp.stack([jnp.stack(kept, axis=1), jnp.stack(returned, axis=1)], axis=1)
    pair = jnp.where(me == 0, pair, pair[:, ::-1])
    return pair.reshape(local_bins, width_x, width_z, width_y).astype(jnp.float32)

def body(
    bin_mass,
    wind_east,
    wind_north,
    supersaturation,
    potential_temp,
    terrain_height,
    fall_speed,
    growth_rate,
    latent_factor,
    bin_order,
    kernel_index,
    collision_kernels,
):
    local_bins, width_x, width_z, width_y = bin_mass.shape
    levels = lax.axis_index("vert") * width_z + lax.iota(jnp.int32, width_z)
    open_cells = (levels[None, :, None] >= terrain_height[:, None, :]).astype(jnp.float32)
    wind_x = wind_east * open_cells
    wind_y = wind_north * open_cells
    section_weights = (1.0 / 3.0, 0.5, 1.0)
    if width_x >= len(section_weights):
        section_field, bottom = advect_kernel_call(bin_mass, wind_x, wind_y, section_weights)
    else:
        section_field = bin_mass
        for weight_now in section_weights:
            extended = extended_2(section_field, (("tiles", 1),), 1, jnp.bfloat16)
            section_field = bin_mass + weight_now * tendency(
                extended[:, 1:-1], extended[:, :-2], extended[:, 2:], wind_x, wind_y
            )
        bottom = section_field[:, :, :1, :]
    rim_above = shifted(bottom, "vert", -1)
    from_above = jnp.concatenate([section_field[:, :, 1:], rim_above], axis=2)
    speed = fall_speed[:, None, None, None]
    settled = (1.0 - speed) * section_field + speed * from_above
    growth = growth_rate[:, None, None, None]
    partial = (
        jnp.sum(growth * settled, axis=0),
        jnp.sum(latent_factor[:, None, None, None] * growth * settled, axis=0),
    )
    bin_devices = lax.axis_size("bins")
    if bin_devices == 2:
        swap = [(0, 1), (1, 0)]
        other = lax.ppermute(jnp.stack(partial), "bins", swap)
        uptake, heating = partial[0] + other[0], partial[1] + other[1]
    else:
        uptake, heating = lax.psum(partial, "bins")
    midway = supersaturation * jnp.exp(-0.5 * condense_rate * uptake)
    grown = settled * (1.0 + growth_gain * growth * midway)
    temp_next = potential_temp + heating_gain * midway * heating
    vapor_next = supersaturation * jnp.exp(-condense_rate * uptake)
    if bin_devices == 2 and width_x % 2 == 0:
        change = paired_collision(grown, bin_order, kernel_index, collision_kernels)
    else:
        change = spread_collision(grown, bin_order, kernel_index, collision_kernels)
    mass_next = (grown + change) * open_cells
    return (mass_next, temp_next, vapor_next)


def solution(mesh):
    return jax.shard_map(
        body,
        mesh=mesh,
        in_specs=(
            P("bins", ("groups", "tiles"), "vert", None),
            P(("groups", "tiles"), "vert", None),
            P(("groups", "tiles"), "vert", None),
            P(("groups", "tiles"), "vert", None),
            P(("groups", "tiles"), "vert", None),
            P(("groups", "tiles"), None),
            P("bins"),
            P("bins"),
            P("bins"),
            P(),
            P(),
            P(),
        ),
        out_specs=(
            P("bins", ("groups", "tiles"), "vert", None),
            P(("groups", "tiles"), "vert", None),
            P(("groups", "tiles"), "vert", None),
        ),
        check_vma=False,
    )
```

```python
import functools

import jax
import jax.numpy as jnp
from jax import lax
from jax.experimental import pallas as pl
from jax.experimental.pallas import tpu as pltpu
from jax.sharding import PartitionSpec as P

SUB = 8


collision_rate = 0.001
condense_rate = 0.02
heating_gain = 0.03
growth_gain = 0.5
highest = lax.Precision.HIGHEST


def extended_2(array, sides, width, link=jnp.float32):
    for axis, dim in sides:
        size, length = (lax.axis_size(axis), array.shape[dim])
        up = [(i, (i + 1) % size) for i in range(size - 1)]
        down = [(j, i) for i, j in up]
        last = lax.slice_in_dim(array, length - width, length, axis=dim)
        first = lax.slice_in_dim(array, 0, width, axis=dim)
        before = lax.ppermute(last.astype(link), axis, up).astype(array.dtype)
        after = lax.ppermute(first.astype(link), axis, down).astype(array.dtype)
        array = jnp.concatenate([before, array, after], axis=dim)
    return array


def rim_kernel(depth, q_ref, wx_ref, wy_ref, left_ref, right_ref):
    local_bins, width_x = q_ref.shape[:2]
    for out_ref, lo in ((left_ref, width_x - depth), (right_ref, 0)):
        out_ref[0:local_bins] = q_ref[:, lo : lo + depth].astype(out_ref.dtype)
        for k, wind_ref in enumerate((wx_ref, wy_ref)):
            wind = wind_ref[lo : lo + depth]
            high = wind.astype(out_ref.dtype)
            low = (wind - high.astype(jnp.float32)).astype(out_ref.dtype)
            out_ref[local_bins + k] = high
            out_ref[local_bins + 2 + k] = low


def rims(bin_mass, wind_x, wind_y, depth):
    local_bins, width_x, width_z, width_y = bin_mass.shape
    shape = jax.ShapeDtypeStruct((local_bins + 4, depth, width_z, width_y), jnp.bfloat16)
    return pl.pallas_call(
        functools.partial(rim_kernel, depth),
        out_shape=(shape, shape),
    )(bin_mass, wind_x, wind_y)


def advect_kernel(weights, q_ref, left_ref, right_ref, *refs):
    left_winds, right_winds = refs[0:4], refs[4:8]
    wx_ref, wy_ref, out_ref, bottom_ref = refs[8:]
    depth = len(weights)
    width = q_ref.shape[1]

    def widened(ref):
        return ref[...].astype(jnp.float32)

    def winds(rows):
        return [widened(rows[k])[0] + widened(rows[k + 2])[0] for k in (0, 1)]

    (wx_left, wy_left), (wx_right, wy_right) = winds(left_winds), winds(right_winds)
    field = jnp.concatenate([widened(left_ref), q_ref[...], widened(right_ref)], axis=1)
    wx = jnp.concatenate([wx_left, wx_ref[...], wx_right], axis=0)
    wy = jnp.concatenate([wy_left, wy_ref[...], wy_right], axis=0)
    section = field
    for stage, weight_now in enumerate(weights, start=1):
        span = width + 2 * (depth - stage)
        center = section[:, 1 : 1 + span]
        west = section[:, 0:span]
        east = section[:, 2 : 2 + span]
        south = pltpu.roll(center, 1, 3)
        north = pltpu.roll(center, center.shape[3] - 1, 3)
        wind_a = wx[stage : stage + span]
        wind_b = wy[stage : stage + span]
        along_x = jnp.maximum(wind_a, 0.0) * (center - west) + jnp.minimum(wind_a, 0.0) * (east - center)
        along_y = jnp.maximum(wind_b, 0.0) * (center - south) + jnp.minimum(wind_b, 0.0) * (north - center)
        section = field[:, stage : stage + span] + weight_now * (-along_x - along_y)
    out_ref[...] = section
    bottom_ref[...] = section[:, :, :1]


def advect_kernel_call(bin_mass, wind_x, wind_y, section_weights):
    local_bins, width_x, width_z, width_y = bin_mass.shape
    depth = len(section_weights)
    tiles = lax.axis_size("tiles")
    up = [(i, i + 1) for i in range(tiles - 1)]
    down = [(j, i) for i, j in up]

    left, right = (
        lax.ppermute(message, "tiles", pairs)
        for message, pairs in zip(rims(bin_mass, wind_x, wind_y, depth), (up, down))
    )
    block = max(d for d in range(1, 34) if local_bins % d == 0)
    rim_spec = pl.BlockSpec((block, depth, width_z, width_y), lambda i: (i, 0, 0, 0))
    row_specs = [
        pl.BlockSpec((1, depth, width_z, width_y), lambda i, row=local_bins + k: (row, 0, 0, 0))
        for k in range(4)
    ]
    own_spec = pl.BlockSpec((block, width_x, width_z, width_y), lambda i: (i, 0, 0, 0))
    wind_spec = pl.BlockSpec(wind_x.shape, lambda i: (0, 0, 0))
    cells = local_bins * width_x * width_z * width_y
    return pl.pallas_call(
        functools.partial(advect_kernel, section_weights),
        out_shape=(
            jax.ShapeDtypeStruct(bin_mass.shape, bin_mass.dtype),
            jax.ShapeDtypeStruct((local_bins, width_x, 1, width_y), bin_mass.dtype),
        ),
        grid=(local_bins // block,),
        in_specs=[own_spec, rim_spec, rim_spec] + row_specs + row_specs + [wind_spec, wind_spec],
        out_specs=(own_spec, pl.BlockSpec((block, width_x, 1, width_y), lambda i: (i, 0, 0, 0))),
        cost_estimate=pl.CostEstimate(flops=80 * cells, bytes_accessed=20 * cells, transcendentals=0),
    )(bin_mass, left, right, *([left] * 4), *([right] * 4), wind_x, wind_y)

def settle_kernel(fall_ref, growth_ref, latent_ref, adv_ref, above_ref, settled_ref, partial_ref):
    block = adv_ref.shape[0]
    first = pl.program_id(0) * block
    levels = adv_ref.shape[2]
    top = lax.broadcasted_iota(jnp.int32, adv_ref.shape[1:], 1) == levels - 1

    @pl.when(pl.program_id(0) == 0)
    def _():
        partial_ref[...] = jnp.zeros_like(partial_ref)

    def one_bin(b, sums):
        uptake, heating = sums
        speed = fall_ref[first + b]
        growth = growth_ref[first + b]
        latent = latent_ref[first + b]
        field = adv_ref[b]
        from_above = jnp.where(
            top, jnp.broadcast_to(above_ref[b], field.shape), pltpu.roll(field, levels - 1, 1)
        )
        settled = (1.0 - speed) * field + speed * from_above
        settled_ref[b] = settled
        return uptake + growth * settled, heating + latent * growth * settled

    zeros = jnp.zeros(adv_ref.shape[1:], jnp.float32)
    uptake, heating = lax.fori_loop(0, block, one_bin, (zeros, zeros))
    partial_ref[0] += uptake
    partial_ref[1] += heating


def settle_call(advected, above, fall_speed, growth_rate, latent_factor):
    local_bins, width_x, width_z, width_y = advected.shape
    block = max(d for d in range(1, 34) if local_bins % d == 0)
    field_spec = pl.BlockSpec((block, width_x, width_z, width_y), lambda i: (i, 0, 0, 0))
    scalar_spec = pl.BlockSpec(memory_space=pltpu.SMEM)
    return pl.pallas_call(
        settle_kernel,
        out_shape=(
            jax.ShapeDtypeStruct(advected.shape, advected.dtype),
            jax.ShapeDtypeStruct((2, width_x, width_z, width_y), jnp.float32),
        ),
        grid=(local_bins // block,),
        in_specs=[
            scalar_spec,
            scalar_spec,
            scalar_spec,
            field_spec,
            pl.BlockSpec((block, width_x, 1, width_y), lambda i: (i, 0, 0, 0)),
        ],
        out_specs=(field_spec, pl.BlockSpec((2, width_x, width_z, width_y), lambda i: (0, 0, 0, 0))),
    )(fall_speed, growth_rate, latent_factor, advected, above)


def shifted(block, axis, distance):
    devices = range(lax.axis_size(axis))
    route = [(i - distance, i) for i in devices if i - distance in devices]
    return lax.ppermute(block, axis, route)


def tendency(center_cells, left_cells, right_cells, wind_x, wind_y):
    south_cells = jnp.roll(center_cells, 1, axis=3)
    north_cells = jnp.roll(center_cells, -1, axis=3)
    along_x = jnp.maximum(wind_x, 0.0) * (center_cells - left_cells) + jnp.minimum(wind_x, 0.0) * (
        right_cells - center_cells
    )
    along_y = jnp.maximum(wind_y, 0.0) * (center_cells - south_cells) + jnp.minimum(wind_y, 0.0) * (
        north_cells - center_cells
    )
    return -along_x - along_y


def coupling_table(bin_order, kernel_index, collision_kernels):
    class_count = kernel_index.shape[0]
    table_count = collision_kernels.shape[0]
    class_bins = collision_kernels.shape[1]
    bin_class = bin_order // class_bins
    bin_within = bin_order % class_bins
    kernel_pick = (kernel_index[:, :, None] == lax.iota(jnp.int32, table_count)).astype(jnp.float32)
    block_table = jnp.einsum(
        "ack,kmn->acmn", kernel_pick, collision_kernels.astype(jnp.float32), precision=highest
    )
    class_hot = (bin_class[:, None] == lax.iota(jnp.int32, class_count)).astype(jnp.float32)
    within_hot = (bin_within[:, None] == lax.iota(jnp.int32, class_bins)).astype(jnp.float32)
    row_table = jnp.einsum("bm,acmn->bacn", within_hot, block_table, precision=highest)
    row_table = jnp.einsum("ba,bacn->bcn", class_hot, row_table, precision=highest)
    coupling = jnp.einsum("bcn,dc,dn->bd", row_table, class_hot, within_hot, precision=highest)
    same_class = jnp.dot(class_hot, class_hot.T, precision=highest)
    return jnp.concatenate([coupling, same_class], axis=0).astype(jnp.bfloat16)


def collide(table, first, tie=None):
    all_bins = table.shape[1]
    iterate = first
    for substep in range(SUB):
        if tie is not None and substep == SUB // 2:
            iterate, tie = lax.optimization_barrier((iterate, tie))
        products = jnp.dot(table, iterate.astype(jnp.bfloat16), preferred_element_type=jnp.float32)
        iterate = iterate + collision_rate * products[all_bins:] * products[:all_bins]
    change = (iterate - first).astype(jnp.bfloat16)
    return change if tie is None else (change, tie)


def spread_collision(grown, bin_order, kernel_index, collision_kernels):
    local_bins, width_x, width_z, width_y = grown.shape
    table = coupling_table(bin_order, kernel_index, collision_kernels)
    all_bins = table.shape[1]
    start = grown.astype(jnp.bfloat16).reshape(local_bins, width_x, width_z * width_y)
    cell_block = lax.all_to_all(start, "bins", split_axis=2, concat_axis=0, tiled=True)
    block_shape = cell_block.shape
    first = cell_block.reshape(all_bins, -1).astype(jnp.float32)
    change = collide(table, first).reshape(block_shape)
    change = lax.all_to_all(change, "bins", split_axis=0, concat_axis=2, tiled=True)
    return change.reshape(local_bins, width_x, width_z, width_y).astype(jnp.float32)


def paired_collision(grown, bin_order, kernel_index, collision_kernels):
    local_bins, width_x, width_z, width_y = grown.shape
    swap = [(0, 1), (1, 0)]
    me = lax.axis_index("bins")
    order = lax.dynamic_slice_in_dim(
        jnp.concatenate([bin_order, bin_order]), me * local_bins, 2 * local_bins
    )
    table = coupling_table(order, kernel_index, collision_kernels)
    halves = grown.astype(jnp.bfloat16).reshape(local_bins, 2, width_x // 2, width_z, width_y)
    own = lax.dynamic_index_in_dim(halves, me, axis=1, keepdims=False)
    away = lax.dynamic_index_in_dim(halves, 1 - me, axis=1, keepdims=False)
    kept, returned = [], []
    for chunk in range(width_x // 2):
        arrived = lax.ppermute(away[:, chunk], "bins", swap)
        first = jnp.concatenate([own[:, chunk], arrived], axis=0).reshape(2 * local_bins, -1).astype(jnp.float32)
        if returned:
            change, returned[-1] = collide(table, first, returned[-1])
        else:
            change = collide(table, first)
        change = change.reshape(2 * local_bins, width_z, width_y)
        returned.append(lax.ppermute(change[local_bins:], "bins", swap))
        kept.append(change[:local_bins])
    pair = jnp.stack([jnp.stack(kept, axis=1), jnp.stack(returned, axis=1)], axis=1)
    pair = jnp.where(me == 0, pair, pair[:, ::-1])
    return pair.reshape(local_bins, width_x, width_z, width_y).astype(jnp.float32)

def body(
    bin_mass,
    wind_east,
    wind_north,
    supersaturation,
    potential_temp,
    terrain_height,
    fall_speed,
    growth_rate,
    latent_factor,
    bin_order,
    kernel_index,
    collision_kernels,
):
    local_bins, width_x, width_z, width_y = bin_mass.shape
    levels = lax.axis_index("vert") * width_z + lax.iota(jnp.int32, width_z)
    open_cells = (levels[None, :, None] >= terrain_height[:, None, :]).astype(jnp.float32)
    wind_x = wind_east * open_cells
    wind_y = wind_north * open_cells
    section_weights = (1.0 / 3.0, 0.5, 1.0)
    if width_x >= len(section_weights):
        section_field, bottom = advect_kernel_call(bin_mass, wind_x, wind_y, section_weights)
    else:
        section_field = bin_mass
        for weight_now in section_weights:
            extended = extended_2(section_field, (("tiles", 1),), 1, jnp.bfloat16)
            section_field = bin_mass + weight_now * tendency(
                extended[:, 1:-1], extended[:, :-2], extended[:, 2:], wind_x, wind_y
            )
        bottom = section_field[:, :, :1, :]
    rim_above = shifted(bottom, "vert", -1)
    growth = growth_rate[:, None, None, None]
    settled, partial = settle_call(section_field, rim_above, fall_speed, growth_rate, latent_factor)
    bin_devices = lax.axis_size("bins")
    if bin_devices == 2:
        swap = [(0, 1), (1, 0)]
        other = lax.ppermute(jnp.stack(partial), "bins", swap)
        uptake, heating = partial[0] + other[0], partial[1] + other[1]
    else:
        uptake, heating = lax.psum(partial, "bins")
    midway = supersaturation * jnp.exp(-0.5 * condense_rate * uptake)
    grown = settled * (1.0 + growth_gain * growth * midway)
    temp_next = potential_temp + heating_gain * midway * heating
    vapor_next = supersaturation * jnp.exp(-condense_rate * uptake)
    if bin_devices == 2 and width_x % 2 == 0:
        change = paired_collision(grown, bin_order, kernel_index, collision_kernels)
    else:
        change = spread_collision(grown, bin_order, kernel_index, collision_kernels)
    mass_next = (grown + change) * open_cells
    return (mass_next, temp_next, vapor_next)


def solution(mesh):
    return jax.shard_map(
        body,
        mesh=mesh,
        in_specs=(
            P("bins", ("groups", "tiles"), "vert", None),
            P(("groups", "tiles"), "vert", None),
            P(("groups", "tiles"), "vert", None),
            P(("groups", "tiles"), "vert", None),
            P(("groups", "tiles"), "vert", None),
            P(("groups", "tiles"), None),
            P("bins"),
            P("bins"),
            P("bins"),
            P(),
            P(),
            P(),
        ),
        out_specs=(
            P("bins", ("groups", "tiles"), "vert", None),
            P(("groups", "tiles"), "vert", None),
            P(("groups", "tiles"), "vert", None),
        ),
        check_vma=False,
    )
```

```python
import functools

import jax
import jax.numpy as jnp
from jax import lax
from jax.experimental import pallas as pl
from jax.experimental.pallas import tpu as pltpu
from jax.sharding import PartitionSpec as P

SUB = 8


collision_rate = 0.001
condense_rate = 0.02
heating_gain = 0.03
growth_gain = 0.5
highest = lax.Precision.HIGHEST


def extended_2(array, sides, width, link=jnp.float32):
    for axis, dim in sides:
        size, length = (lax.axis_size(axis), array.shape[dim])
        up = [(i, (i + 1) % size) for i in range(size - 1)]
        down = [(j, i) for i, j in up]
        last = lax.slice_in_dim(array, length - width, length, axis=dim)
        first = lax.slice_in_dim(array, 0, width, axis=dim)
        before = lax.ppermute(last.astype(link), axis, up).astype(array.dtype)
        after = lax.ppermute(first.astype(link), axis, down).astype(array.dtype)
        array = jnp.concatenate([before, array, after], axis=dim)
    return array


def rim_kernel(depth, q_ref, wx_ref, wy_ref, left_ref, right_ref):
    local_bins, width_x = q_ref.shape[:2]
    for out_ref, lo in ((left_ref, width_x - depth), (right_ref, 0)):
        out_ref[0:local_bins] = q_ref[:, lo : lo + depth].astype(out_ref.dtype)
        for k, wind_ref in enumerate((wx_ref, wy_ref)):
            wind = wind_ref[lo : lo + depth]
            high = wind.astype(out_ref.dtype)
            low = (wind - high.astype(jnp.float32)).astype(out_ref.dtype)
            out_ref[local_bins + k] = high
            out_ref[local_bins + 2 + k] = low


def rims(bin_mass, wind_x, wind_y, depth):
    local_bins, width_x, width_z, width_y = bin_mass.shape
    shape = jax.ShapeDtypeStruct((local_bins + 4, depth, width_z, width_y), jnp.bfloat16)
    return pl.pallas_call(
        functools.partial(rim_kernel, depth),
        out_shape=(shape, shape),
    )(bin_mass, wind_x, wind_y)


def advect_kernel(weights, q_ref, left_ref, right_ref, *refs):
    left_winds, right_winds = refs[0:4], refs[4:8]
    wx_ref, wy_ref, out_ref, bottom_ref = refs[8:]
    depth = len(weights)
    width = q_ref.shape[1]

    def widened(ref):
        return ref[...].astype(jnp.float32)

    def winds(rows):
        return [widened(rows[k])[0] + widened(rows[k + 2])[0] for k in (0, 1)]

    (wx_left, wy_left), (wx_right, wy_right) = winds(left_winds), winds(right_winds)
    field = jnp.concatenate([widened(left_ref), q_ref[...], widened(right_ref)], axis=1)
    wx = jnp.concatenate([wx_left, wx_ref[...], wx_right], axis=0)
    wy = jnp.concatenate([wy_left, wy_ref[...], wy_right], axis=0)
    section = field
    for stage, weight_now in enumerate(weights, start=1):
        span = width + 2 * (depth - stage)
        center = section[:, 1 : 1 + span]
        west = section[:, 0:span]
        east = section[:, 2 : 2 + span]
        south = pltpu.roll(center, 1, 3)
        north = pltpu.roll(center, center.shape[3] - 1, 3)
        wind_a = wx[stage : stage + span]
        wind_b = wy[stage : stage + span]
        along_x = jnp.maximum(wind_a, 0.0) * (center - west) + jnp.minimum(wind_a, 0.0) * (east - center)
        along_y = jnp.maximum(wind_b, 0.0) * (center - south) + jnp.minimum(wind_b, 0.0) * (north - center)
        section = field[:, stage : stage + span] + weight_now * (-along_x - along_y)
    out_ref[...] = section
    bottom_ref[...] = section[:, :, :1]


def advect_kernel_call(bin_mass, wind_x, wind_y, section_weights, tie):
    local_bins, width_x, width_z, width_y = bin_mass.shape
    depth = len(section_weights)
    tiles = lax.axis_size("tiles")
    up = [(i, i + 1) for i in range(tiles - 1)]
    down = [(j, i) for i, j in up]

    left, right = (
        lax.ppermute(message, "tiles", pairs)
        for message, pairs in zip(rims(bin_mass, wind_x, wind_y, depth), (up, down))
    )
    left, tie = lax.optimization_barrier((left, tie))
    block = max(d for d in range(1, 34) if local_bins % d == 0)
    rim_spec = pl.BlockSpec((block, depth, width_z, width_y), lambda i: (i, 0, 0, 0))
    row_specs = [
        pl.BlockSpec((1, depth, width_z, width_y), lambda i, row=local_bins + k: (row, 0, 0, 0))
        for k in range(4)
    ]
    own_spec = pl.BlockSpec((block, width_x, width_z, width_y), lambda i: (i, 0, 0, 0))
    wind_spec = pl.BlockSpec(wind_x.shape, lambda i: (0, 0, 0))
    cells = local_bins * width_x * width_z * width_y
    return tie, pl.pallas_call(
        functools.partial(advect_kernel, section_weights),
        out_shape=(
            jax.ShapeDtypeStruct(bin_mass.shape, bin_mass.dtype),
            jax.ShapeDtypeStruct((local_bins, width_x, 1, width_y), bin_mass.dtype),
        ),
        grid=(local_bins // block,),
        in_specs=[own_spec, rim_spec, rim_spec] + row_specs + row_specs + [wind_spec, wind_spec],
        out_specs=(own_spec, pl.BlockSpec((block, width_x, 1, width_y), lambda i: (i, 0, 0, 0))),
        cost_estimate=pl.CostEstimate(flops=80 * cells, bytes_accessed=20 * cells, transcendentals=0),
    )(bin_mass, left, right, *([left] * 4), *([right] * 4), wind_x, wind_y)

def shifted(block, axis, distance):
    devices = range(lax.axis_size(axis))
    route = [(i - distance, i) for i in devices if i - distance in devices]
    return lax.ppermute(block, axis, route)


def tendency(center_cells, left_cells, right_cells, wind_x, wind_y):
    south_cells = jnp.roll(center_cells, 1, axis=3)
    north_cells = jnp.roll(center_cells, -1, axis=3)
    along_x = jnp.maximum(wind_x, 0.0) * (center_cells - left_cells) + jnp.minimum(wind_x, 0.0) * (
        right_cells - center_cells
    )
    along_y = jnp.maximum(wind_y, 0.0) * (center_cells - south_cells) + jnp.minimum(wind_y, 0.0) * (
        north_cells - center_cells
    )
    return -along_x - along_y


def coupling_table(bin_order, kernel_index, collision_kernels):
    class_count = kernel_index.shape[0]
    table_count = collision_kernels.shape[0]
    class_bins = collision_kernels.shape[1]
    bin_class = bin_order // class_bins
    bin_within = bin_order % class_bins
    kernel_pick = (kernel_index[:, :, None] == lax.iota(jnp.int32, table_count)).astype(jnp.float32)
    block_table = jnp.einsum(
        "ack,kmn->acmn", kernel_pick, collision_kernels.astype(jnp.float32), precision=highest
    )
    class_hot = (bin_class[:, None] == lax.iota(jnp.int32, class_count)).astype(jnp.float32)
    within_hot = (bin_within[:, None] == lax.iota(jnp.int32, class_bins)).astype(jnp.float32)
    row_table = jnp.einsum("bm,acmn->bacn", within_hot, block_table, precision=highest)
    row_table = jnp.einsum("ba,bacn->bcn", class_hot, row_table, precision=highest)
    coupling = jnp.einsum("bcn,dc,dn->bd", row_table, class_hot, within_hot, precision=highest)
    same_class = jnp.dot(class_hot, class_hot.T, precision=highest)
    return jnp.concatenate([coupling, same_class], axis=0).astype(jnp.bfloat16)


def collide(table, first, tie=None):
    all_bins = table.shape[1]
    iterate = first
    for substep in range(SUB):
        if tie is not None and substep == SUB // 2:
            iterate, tie = lax.optimization_barrier((iterate, tie))
        products = jnp.dot(table, iterate.astype(jnp.bfloat16), preferred_element_type=jnp.float32)
        iterate = iterate + collision_rate * products[all_bins:] * products[:all_bins]
    change = (iterate - first).astype(jnp.bfloat16)
    return change if tie is None else (change, tie)


def spread_collision(grown, bin_order, kernel_index, collision_kernels):
    local_bins, width_x, width_z, width_y = grown.shape
    table = coupling_table(bin_order, kernel_index, collision_kernels)
    all_bins = table.shape[1]
    start = grown.astype(jnp.bfloat16).reshape(local_bins, width_x, width_z * width_y)
    cell_block = lax.all_to_all(start, "bins", split_axis=2, concat_axis=0, tiled=True)
    block_shape = cell_block.shape
    first = cell_block.reshape(all_bins, -1).astype(jnp.float32)
    change = collide(table, first).reshape(block_shape)
    change = lax.all_to_all(change, "bins", split_axis=0, concat_axis=2, tiled=True)
    return change.reshape(local_bins, width_x, width_z, width_y).astype(jnp.float32)


def paired_table(bin_order, kernel_index, collision_kernels):
    local_bins = bin_order.shape[0] // 2
    me = lax.axis_index("bins")
    order = lax.dynamic_slice_in_dim(
        jnp.concatenate([bin_order, bin_order]), me * local_bins, 2 * local_bins
    )
    return coupling_table(order, kernel_index, collision_kernels)


def paired_collision(grown, table):
    local_bins, width_x, width_z, width_y = grown.shape
    swap = [(0, 1), (1, 0)]
    me = lax.axis_index("bins")
    halves = grown.astype(jnp.bfloat16).reshape(local_bins, 2, width_x // 2, width_z, width_y)
    own = lax.dynamic_index_in_dim(halves, me, axis=1, keepdims=False)
    away = lax.dynamic_index_in_dim(halves, 1 - me, axis=1, keepdims=False)
    kept, returned = [], []
    for chunk in range(width_x // 2):
        arrived = lax.ppermute(away[:, chunk], "bins", swap)
        first = jnp.concatenate([own[:, chunk], arrived], axis=0).reshape(2 * local_bins, -1).astype(jnp.float32)
        if returned:
            change, returned[-1] = collide(table, first, returned[-1])
        else:
            change = collide(table, first)
        change = change.reshape(2 * local_bins, width_z, width_y)
        returned.append(lax.ppermute(change[local_bins:], "bins", swap))
        kept.append(change[:local_bins])
    pair = jnp.stack([jnp.stack(kept, axis=1), jnp.stack(returned, axis=1)], axis=1)
    pair = jnp.where(me == 0, pair, pair[:, ::-1])
    return pair.reshape(local_bins, width_x, width_z, width_y).astype(jnp.float32)


def body(
    bin_mass,
    wind_east,
    wind_north,
    supersaturation,
    potential_temp,
    terrain_height,
    fall_speed,
    growth_rate,
    latent_factor,
    bin_order,
    kernel_index,
    collision_kernels,
):
    local_bins, width_x, width_z, width_y = bin_mass.shape
    levels = lax.axis_index("vert") * width_z + lax.iota(jnp.int32, width_z)
    open_cells = (levels[None, :, None] >= terrain_height[:, None, :]).astype(jnp.float32)
    wind_x = wind_east * open_cells
    wind_y = wind_north * open_cells
    section_weights = (1.0 / 3.0, 0.5, 1.0)
    paired = lax.axis_size("bins") == 2 and width_x % 2 == 0
    table = paired_table(bin_order, kernel_index, collision_kernels) if paired else None
    if width_x >= len(section_weights):
        table, (section_field, bottom) = advect_kernel_call(
            bin_mass, wind_x, wind_y, section_weights, table
        )
    else:
        section_field = bin_mass
        for weight_now in section_weights:
            extended = extended_2(section_field, (("tiles", 1),), 1, jnp.bfloat16)
            section_field = bin_mass + weight_now * tendency(
                extended[:, 1:-1], extended[:, :-2], extended[:, 2:], wind_x, wind_y
            )
        bottom = section_field[:, :, :1, :]
    rim_above = shifted(bottom, "vert", -1)
    from_above = jnp.concatenate([section_field[:, :, 1:], rim_above], axis=2)
    speed = fall_speed[:, None, None, None]
    settled = (1.0 - speed) * section_field + speed * from_above
    growth = growth_rate[:, None, None, None]
    partial = (
        jnp.sum(growth * settled, axis=0),
        jnp.sum(latent_factor[:, None, None, None] * growth * settled, axis=0),
    )
    bin_devices = lax.axis_size("bins")
    if bin_devices == 2:
        swap = [(0, 1), (1, 0)]
        other = lax.ppermute(jnp.stack(partial), "bins", swap)
        uptake, heating = partial[0] + other[0], partial[1] + other[1]
    else:
        uptake, heating = lax.psum(partial, "bins")
    midway = supersaturation * jnp.exp(-0.5 * condense_rate * uptake)
    grown = settled * (1.0 + growth_gain * growth * midway)
    temp_next = potential_temp + heating_gain * midway * heating
    vapor_next = supersaturation * jnp.exp(-condense_rate * uptake)
    if paired:
        change = paired_collision(grown, table)
    else:
        change = spread_collision(grown, bin_order, kernel_index, collision_kernels)
    mass_next = (grown + change) * open_cells
    return (mass_next, temp_next, vapor_next)


def solution(mesh):
    return jax.shard_map(
        body,
        mesh=mesh,
        in_specs=(
            P("bins", ("groups", "tiles"), "vert", None),
            P(("groups", "tiles"), "vert", None),
            P(("groups", "tiles"), "vert", None),
            P(("groups", "tiles"), "vert", None),
            P(("groups", "tiles"), "vert", None),
            P(("groups", "tiles"), None),
            P("bins"),
            P("bins"),
            P("bins"),
            P(),
            P(),
            P(),
        ),
        out_specs=(
            P("bins", ("groups", "tiles"), "vert", None),
            P(("groups", "tiles"), "vert", None),
            P(("groups", "tiles"), "vert", None),
        ),
        check_vma=False,
    )
```

```python
import functools

import jax
import jax.numpy as jnp
from jax import lax
from jax.experimental import pallas as pl
from jax.experimental.pallas import tpu as pltpu
from jax.sharding import PartitionSpec as P

SUB = 8


collision_rate = 0.001
condense_rate = 0.02
heating_gain = 0.03
growth_gain = 0.5
highest = lax.Precision.HIGHEST


def extended_2(array, sides, width, link=jnp.float32):
    for axis, dim in sides:
        size, length = (lax.axis_size(axis), array.shape[dim])
        up = [(i, (i + 1) % size) for i in range(size - 1)]
        down = [(j, i) for i, j in up]
        last = lax.slice_in_dim(array, length - width, length, axis=dim)
        first = lax.slice_in_dim(array, 0, width, axis=dim)
        before = lax.ppermute(last.astype(link), axis, up).astype(array.dtype)
        after = lax.ppermute(first.astype(link), axis, down).astype(array.dtype)
        array = jnp.concatenate([before, array, after], axis=dim)
    return array


def rim_kernel(depth, q_ref, wx_ref, wy_ref, left_ref, right_ref):
    local_bins, width_x = q_ref.shape[:2]
    for out_ref, lo in ((left_ref, width_x - depth), (right_ref, 0)):
        out_ref[0:local_bins] = q_ref[:, lo : lo + depth].astype(out_ref.dtype)
        for k, wind_ref in enumerate((wx_ref, wy_ref)):
            wind = wind_ref[lo : lo + depth]
            high = wind.astype(out_ref.dtype)
            low = (wind - high.astype(jnp.float32)).astype(out_ref.dtype)
            out_ref[local_bins + k] = high
            out_ref[local_bins + 2 + k] = low


def rims(bin_mass, wind_x, wind_y, depth):
    local_bins, width_x, width_z, width_y = bin_mass.shape
    shape = jax.ShapeDtypeStruct((local_bins + 4, depth, width_z, width_y), jnp.bfloat16)
    return pl.pallas_call(
        functools.partial(rim_kernel, depth),
        out_shape=(shape, shape),
    )(bin_mass, wind_x, wind_y)


def advect_kernel(weights, q_ref, left_ref, right_ref, *refs):
    left_winds, right_winds = refs[0:4], refs[4:8]
    wx_ref, wy_ref, out_ref, bottom_ref, lifted_ref = refs[8:]
    depth = len(weights)
    width = q_ref.shape[1]

    def widened(ref):
        return ref[...].astype(jnp.float32)

    def winds(rows):
        return [widened(rows[k])[0] + widened(rows[k + 2])[0] for k in (0, 1)]

    (wx_left, wy_left), (wx_right, wy_right) = winds(left_winds), winds(right_winds)
    field = jnp.concatenate([widened(left_ref), q_ref[...], widened(right_ref)], axis=1)
    wx = jnp.concatenate([wx_left, wx_ref[...], wx_right], axis=0)
    wy = jnp.concatenate([wy_left, wy_ref[...], wy_right], axis=0)
    section = field
    for stage, weight_now in enumerate(weights, start=1):
        span = width + 2 * (depth - stage)
        center = section[:, 1 : 1 + span]
        west = section[:, 0:span]
        east = section[:, 2 : 2 + span]
        south = pltpu.roll(center, 1, 3)
        north = pltpu.roll(center, center.shape[3] - 1, 3)
        wind_a = wx[stage : stage + span]
        wind_b = wy[stage : stage + span]
        along_x = jnp.maximum(wind_a, 0.0) * (center - west) + jnp.minimum(wind_a, 0.0) * (east - center)
        along_y = jnp.maximum(wind_b, 0.0) * (center - south) + jnp.minimum(wind_b, 0.0) * (north - center)
        section = field[:, stage : stage + span] + weight_now * (-along_x - along_y)
    out_ref[...] = section
    bottom_ref[...] = section[:, :, :1]
    lifted_ref[...] = pltpu.roll(section, section.shape[2] - 1, 2)


def advect_kernel_call(bin_mass, wind_x, wind_y, section_weights, tie):
    local_bins, width_x, width_z, width_y = bin_mass.shape
    depth = len(section_weights)
    tiles = lax.axis_size("tiles")
    up = [(i, i + 1) for i in range(tiles - 1)]
    down = [(j, i) for i, j in up]

    left, right = (
        lax.ppermute(message, "tiles", pairs)
        for message, pairs in zip(rims(bin_mass, wind_x, wind_y, depth), (up, down))
    )
    left, tie = lax.optimization_barrier((left, tie))
    block = max(d for d in range(1, 34) if local_bins % d == 0)
    rim_spec = pl.BlockSpec((block, depth, width_z, width_y), lambda i: (i, 0, 0, 0))
    row_specs = [
        pl.BlockSpec((1, depth, width_z, width_y), lambda i, row=local_bins + k: (row, 0, 0, 0))
        for k in range(4)
    ]
    own_spec = pl.BlockSpec((block, width_x, width_z, width_y), lambda i: (i, 0, 0, 0))
    wind_spec = pl.BlockSpec(wind_x.shape, lambda i: (0, 0, 0))
    cells = local_bins * width_x * width_z * width_y
    return tie, pl.pallas_call(
        functools.partial(advect_kernel, section_weights),
        out_shape=(
            jax.ShapeDtypeStruct(bin_mass.shape, bin_mass.dtype),
            jax.ShapeDtypeStruct((local_bins, width_x, 1, width_y), bin_mass.dtype),
            jax.ShapeDtypeStruct(bin_mass.shape, bin_mass.dtype),
        ),
        grid=(local_bins // block,),
        in_specs=[own_spec, rim_spec, rim_spec] + row_specs + row_specs + [wind_spec, wind_spec],
        out_specs=(own_spec, pl.BlockSpec((block, width_x, 1, width_y), lambda i: (i, 0, 0, 0)), own_spec),
        cost_estimate=pl.CostEstimate(flops=80 * cells, bytes_accessed=20 * cells, transcendentals=0),
    )(bin_mass, left, right, *([left] * 4), *([right] * 4), wind_x, wind_y)

def shifted(block, axis, distance):
    devices = range(lax.axis_size(axis))
    route = [(i - distance, i) for i in devices if i - distance in devices]
    return lax.ppermute(block, axis, route)


def tendency(center_cells, left_cells, right_cells, wind_x, wind_y):
    south_cells = jnp.roll(center_cells, 1, axis=3)
    north_cells = jnp.roll(center_cells, -1, axis=3)
    along_x = jnp.maximum(wind_x, 0.0) * (center_cells - left_cells) + jnp.minimum(wind_x, 0.0) * (
        right_cells - center_cells
    )
    along_y = jnp.maximum(wind_y, 0.0) * (center_cells - south_cells) + jnp.minimum(wind_y, 0.0) * (
        north_cells - center_cells
    )
    return -along_x - along_y


def coupling_table(bin_order, kernel_index, collision_kernels):
    class_count = kernel_index.shape[0]
    table_count = collision_kernels.shape[0]
    class_bins = collision_kernels.shape[1]
    bin_class = bin_order // class_bins
    bin_within = bin_order % class_bins
    kernel_pick = (kernel_index[:, :, None] == lax.iota(jnp.int32, table_count)).astype(jnp.float32)
    block_table = jnp.einsum(
        "ack,kmn->acmn", kernel_pick, collision_kernels.astype(jnp.float32), precision=highest
    )
    class_hot = (bin_class[:, None] == lax.iota(jnp.int32, class_count)).astype(jnp.float32)
    within_hot = (bin_within[:, None] == lax.iota(jnp.int32, class_bins)).astype(jnp.float32)
    row_table = jnp.einsum("bm,acmn->bacn", within_hot, block_table, precision=highest)
    row_table = jnp.einsum("ba,bacn->bcn", class_hot, row_table, precision=highest)
    coupling = jnp.einsum("bcn,dc,dn->bd", row_table, class_hot, within_hot, precision=highest)
    same_class = jnp.dot(class_hot, class_hot.T, precision=highest)
    return jnp.concatenate([coupling, same_class], axis=0).astype(jnp.bfloat16)


def collide(table, first, tie=None):
    all_bins = table.shape[1]
    iterate = first
    for substep in range(SUB):
        if tie is not None and substep == SUB // 2:
            iterate, tie = lax.optimization_barrier((iterate, tie))
        products = jnp.dot(table, iterate.astype(jnp.bfloat16), preferred_element_type=jnp.float32)
        iterate = iterate + collision_rate * products[all_bins:] * products[:all_bins]
    change = (iterate - first).astype(jnp.bfloat16)
    return change if tie is None else (change, tie)


def spread_collision(grown, bin_order, kernel_index, collision_kernels):
    local_bins, width_x, width_z, width_y = grown.shape
    table = coupling_table(bin_order, kernel_index, collision_kernels)
    all_bins = table.shape[1]
    start = grown.astype(jnp.bfloat16).reshape(local_bins, width_x, width_z * width_y)
    cell_block = lax.all_to_all(start, "bins", split_axis=2, concat_axis=0, tiled=True)
    block_shape = cell_block.shape
    first = cell_block.reshape(all_bins, -1).astype(jnp.float32)
    change = collide(table, first).reshape(block_shape)
    change = lax.all_to_all(change, "bins", split_axis=0, concat_axis=2, tiled=True)
    return change.reshape(local_bins, width_x, width_z, width_y).astype(jnp.float32)


def paired_table(bin_order, kernel_index, collision_kernels):
    local_bins = bin_order.shape[0] // 2
    me = lax.axis_index("bins")
    order = lax.dynamic_slice_in_dim(
        jnp.concatenate([bin_order, bin_order]), me * local_bins, 2 * local_bins
    )
    return coupling_table(order, kernel_index, collision_kernels)


def paired_collision(grown, table):
    local_bins, width_x, width_z, width_y = grown.shape
    swap = [(0, 1), (1, 0)]
    me = lax.axis_index("bins")
    halves = grown.astype(jnp.bfloat16).reshape(local_bins, 2, width_x // 2, width_z, width_y)
    own = lax.dynamic_index_in_dim(halves, me, axis=1, keepdims=False)
    away = lax.dynamic_index_in_dim(halves, 1 - me, axis=1, keepdims=False)
    kept, returned = [], []
    for chunk in range(width_x // 2):
        arrived = lax.ppermute(away[:, chunk], "bins", swap)
        first = jnp.concatenate([own[:, chunk], arrived], axis=0).reshape(2 * local_bins, -1).astype(jnp.float32)
        if returned:
            change, returned[-1] = collide(table, first, returned[-1])
        else:
            change = collide(table, first)
        change = change.reshape(2 * local_bins, width_z, width_y)
        returned.append(lax.ppermute(change[local_bins:], "bins", swap))
        kept.append(change[:local_bins])
    pair = jnp.stack([jnp.stack(kept, axis=1), jnp.stack(returned, axis=1)], axis=1)
    pair = jnp.where(me == 0, pair, pair[:, ::-1])
    return pair.reshape(local_bins, width_x, width_z, width_y).astype(jnp.float32)


def body(
    bin_mass,
    wind_east,
    wind_north,
    supersaturation,
    potential_temp,
    terrain_height,
    fall_speed,
    growth_rate,
    latent_factor,
    bin_order,
    kernel_index,
    collision_kernels,
):
    local_bins, width_x, width_z, width_y = bin_mass.shape
    levels = lax.axis_index("vert") * width_z + lax.iota(jnp.int32, width_z)
    open_cells = (levels[None, :, None] >= terrain_height[:, None, :]).astype(jnp.float32)
    wind_x = wind_east * open_cells
    wind_y = wind_north * open_cells
    section_weights = (1.0 / 3.0, 0.5, 1.0)
    paired = lax.axis_size("bins") == 2 and width_x % 2 == 0
    table = paired_table(bin_order, kernel_index, collision_kernels) if paired else None
    if width_x >= len(section_weights):
        table, (section_field, bottom, lifted) = advect_kernel_call(
            bin_mass, wind_x, wind_y, section_weights, table
        )
    else:
        section_field = bin_mass
        for weight_now in section_weights:
            extended = extended_2(section_field, (("tiles", 1),), 1, jnp.bfloat16)
            section_field = bin_mass + weight_now * tendency(
                extended[:, 1:-1], extended[:, :-2], extended[:, 2:], wind_x, wind_y
            )
        bottom = section_field[:, :, :1, :]
        lifted = jnp.roll(section_field, -1, axis=2)
    rim_above = shifted(bottom, "vert", -1)
    top = lax.broadcasted_iota(jnp.int32, section_field.shape, 2) == width_z - 1
    from_above = jnp.where(top, rim_above, lifted)
    speed = fall_speed[:, None, None, None]
    settled = (1.0 - speed) * section_field + speed * from_above
    growth = growth_rate[:, None, None, None]
    partial = (
        jnp.sum(growth * settled, axis=0),
        jnp.sum(latent_factor[:, None, None, None] * growth * settled, axis=0),
    )
    bin_devices = lax.axis_size("bins")
    if bin_devices == 2:
        swap = [(0, 1), (1, 0)]
        other = lax.ppermute(jnp.stack(partial), "bins", swap)
        uptake, heating = partial[0] + other[0], partial[1] + other[1]
    else:
        uptake, heating = lax.psum(partial, "bins")
    midway = supersaturation * jnp.exp(-0.5 * condense_rate * uptake)
    grown = settled * (1.0 + growth_gain * growth * midway)
    temp_next = potential_temp + heating_gain * midway * heating
    vapor_next = supersaturation * jnp.exp(-condense_rate * uptake)
    if paired:
        change = paired_collision(grown, table)
    else:
        change = spread_collision(grown, bin_order, kernel_index, collision_kernels)
    mass_next = (grown + change) * open_cells
    return (mass_next, temp_next, vapor_next)


def solution(mesh):
    return jax.shard_map(
        body,
        mesh=mesh,
        in_specs=(
            P("bins", ("groups", "tiles"), "vert", None),
            P(("groups", "tiles"), "vert", None),
            P(("groups", "tiles"), "vert", None),
            P(("groups", "tiles"), "vert", None),
            P(("groups", "tiles"), "vert", None),
            P(("groups", "tiles"), None),
            P("bins"),
            P("bins"),
            P("bins"),
            P(),
            P(),
            P(),
        ),
        out_specs=(
            P("bins", ("groups", "tiles"), "vert", None),
            P(("groups", "tiles"), "vert", None),
            P(("groups", "tiles"), "vert", None),
        ),
        check_vma=False,
    )
```

```python
import functools

import jax
import jax.numpy as jnp
from jax import lax
from jax.experimental import pallas as pl
from jax.experimental.pallas import tpu as pltpu
from jax.sharding import PartitionSpec as P

SUB = 8


collision_rate = 0.001
condense_rate = 0.02
heating_gain = 0.03
growth_gain = 0.5
highest = lax.Precision.HIGHEST


def extended_2(array, sides, width, link=jnp.float32):
    for axis, dim in sides:
        size, length = (lax.axis_size(axis), array.shape[dim])
        up = [(i, (i + 1) % size) for i in range(size - 1)]
        down = [(j, i) for i, j in up]
        last = lax.slice_in_dim(array, length - width, length, axis=dim)
        first = lax.slice_in_dim(array, 0, width, axis=dim)
        before = lax.ppermute(last.astype(link), axis, up).astype(array.dtype)
        after = lax.ppermute(first.astype(link), axis, down).astype(array.dtype)
        array = jnp.concatenate([before, array, after], axis=dim)
    return array


def rim_kernel(depth, q_ref, wx_ref, wy_ref, left_ref, right_ref):
    local_bins, width_x = q_ref.shape[:2]
    for out_ref, lo in ((left_ref, width_x - depth), (right_ref, 0)):
        out_ref[0:local_bins] = q_ref[:, lo : lo + depth].astype(out_ref.dtype)
        for k, wind_ref in enumerate((wx_ref, wy_ref)):
            wind = wind_ref[lo : lo + depth]
            high = wind.astype(out_ref.dtype)
            low = (wind - high.astype(jnp.float32)).astype(out_ref.dtype)
            out_ref[local_bins + k] = high
            out_ref[local_bins + 2 + k] = low


def rims(bin_mass, wind_x, wind_y, depth):
    local_bins, width_x, width_z, width_y = bin_mass.shape
    shape = jax.ShapeDtypeStruct((local_bins + 4, depth, width_z, width_y), jnp.bfloat16)
    return pl.pallas_call(
        functools.partial(rim_kernel, depth),
        out_shape=(shape, shape),
    )(bin_mass, wind_x, wind_y)


def advect_kernel(weights, q_ref, left_ref, right_ref, *refs):
    left_winds, right_winds = refs[0:4], refs[4:8]
    wx_ref, wy_ref, out_ref, bottom_ref = refs[8:]
    depth = len(weights)
    width = q_ref.shape[1]

    def widened(ref):
        return ref[...].astype(jnp.float32)

    def winds(rows):
        return [widened(rows[k])[0] + widened(rows[k + 2])[0] for k in (0, 1)]

    (wx_left, wy_left), (wx_right, wy_right) = winds(left_winds), winds(right_winds)
    field = jnp.concatenate([widened(left_ref), q_ref[...], widened(right_ref)], axis=1)
    wx = jnp.concatenate([wx_left, wx_ref[...], wx_right], axis=0)
    wy = jnp.concatenate([wy_left, wy_ref[...], wy_right], axis=0)
    section = field
    for stage, weight_now in enumerate(weights, start=1):
        span = width + 2 * (depth - stage)
        center = section[:, 1 : 1 + span]
        west = section[:, 0:span]
        east = section[:, 2 : 2 + span]
        south = pltpu.roll(center, 1, 3)
        north = pltpu.roll(center, center.shape[3] - 1, 3)
        wind_a = wx[stage : stage + span]
        wind_b = wy[stage : stage + span]
        along_x = wind_a * jnp.where(wind_a > 0.0, center - west, east - center)
        along_y = wind_b * jnp.where(wind_b > 0.0, center - south, north - center)
        section = field[:, stage : stage + span] + weight_now * (-along_x - along_y)
    out_ref[...] = section
    bottom_ref[...] = section[:, :, :1]


def advect_kernel_call(bin_mass, wind_x, wind_y, section_weights, tie):
    local_bins, width_x, width_z, width_y = bin_mass.shape
    depth = len(section_weights)
    tiles = lax.axis_size("tiles")
    up = [(i, i + 1) for i in range(tiles - 1)]
    down = [(j, i) for i, j in up]

    left, right = (
        lax.ppermute(message, "tiles", pairs)
        for message, pairs in zip(rims(bin_mass, wind_x, wind_y, depth), (up, down))
    )
    left, tie = lax.optimization_barrier((left, tie))
    block = max(d for d in range(1, 34) if local_bins % d == 0)
    rim_spec = pl.BlockSpec((block, depth, width_z, width_y), lambda i: (i, 0, 0, 0))
    row_specs = [
        pl.BlockSpec((1, depth, width_z, width_y), lambda i, row=local_bins + k: (row, 0, 0, 0))
        for k in range(4)
    ]
    own_spec = pl.BlockSpec((block, width_x, width_z, width_y), lambda i: (i, 0, 0, 0))
    wind_spec = pl.BlockSpec(wind_x.shape, lambda i: (0, 0, 0))
    cells = local_bins * width_x * width_z * width_y
    return tie, pl.pallas_call(
        functools.partial(advect_kernel, section_weights),
        out_shape=(
            jax.ShapeDtypeStruct(bin_mass.shape, bin_mass.dtype),
            jax.ShapeDtypeStruct((local_bins, width_x, 1, width_y), bin_mass.dtype),
        ),
        grid=(local_bins // block,),
        in_specs=[own_spec, rim_spec, rim_spec] + row_specs + row_specs + [wind_spec, wind_spec],
        out_specs=(own_spec, pl.BlockSpec((block, width_x, 1, width_y), lambda i: (i, 0, 0, 0))),
        cost_estimate=pl.CostEstimate(flops=80 * cells, bytes_accessed=20 * cells, transcendentals=0),
    )(bin_mass, left, right, *([left] * 4), *([right] * 4), wind_x, wind_y)

def shifted(block, axis, distance):
    devices = range(lax.axis_size(axis))
    route = [(i - distance, i) for i in devices if i - distance in devices]
    return lax.ppermute(block, axis, route)


def tendency(center_cells, left_cells, right_cells, wind_x, wind_y):
    south_cells = jnp.roll(center_cells, 1, axis=3)
    north_cells = jnp.roll(center_cells, -1, axis=3)
    along_x = jnp.maximum(wind_x, 0.0) * (center_cells - left_cells) + jnp.minimum(wind_x, 0.0) * (
        right_cells - center_cells
    )
    along_y = jnp.maximum(wind_y, 0.0) * (center_cells - south_cells) + jnp.minimum(wind_y, 0.0) * (
        north_cells - center_cells
    )
    return -along_x - along_y


def coupling_table(bin_order, kernel_index, collision_kernels):
    class_count = kernel_index.shape[0]
    table_count = collision_kernels.shape[0]
    class_bins = collision_kernels.shape[1]
    bin_class = bin_order // class_bins
    bin_within = bin_order % class_bins
    kernel_pick = (kernel_index[:, :, None] == lax.iota(jnp.int32, table_count)).astype(jnp.float32)
    block_table = jnp.einsum(
        "ack,kmn->acmn", kernel_pick, collision_kernels.astype(jnp.float32), precision=highest
    )
    class_hot = (bin_class[:, None] == lax.iota(jnp.int32, class_count)).astype(jnp.float32)
    within_hot = (bin_within[:, None] == lax.iota(jnp.int32, class_bins)).astype(jnp.float32)
    row_table = jnp.einsum("bm,acmn->bacn", within_hot, block_table, precision=highest)
    row_table = jnp.einsum("ba,bacn->bcn", class_hot, row_table, precision=highest)
    coupling = jnp.einsum("bcn,dc,dn->bd", row_table, class_hot, within_hot, precision=highest)
    same_class = jnp.dot(class_hot, class_hot.T, precision=highest)
    return jnp.concatenate([coupling, same_class], axis=0).astype(jnp.bfloat16)


def collide(table, first, tie=None):
    all_bins = table.shape[1]
    iterate = first
    for substep in range(SUB):
        if tie is not None and substep == SUB // 2:
            iterate, tie = lax.optimization_barrier((iterate, tie))
        products = jnp.dot(table, iterate.astype(jnp.bfloat16), preferred_element_type=jnp.float32)
        iterate = iterate + collision_rate * products[all_bins:] * products[:all_bins]
    change = (iterate - first).astype(jnp.bfloat16)
    return change if tie is None else (change, tie)


def spread_collision(grown, bin_order, kernel_index, collision_kernels):
    local_bins, width_x, width_z, width_y = grown.shape
    table = coupling_table(bin_order, kernel_index, collision_kernels)
    all_bins = table.shape[1]
    start = grown.astype(jnp.bfloat16).reshape(local_bins, width_x, width_z * width_y)
    cell_block = lax.all_to_all(start, "bins", split_axis=2, concat_axis=0, tiled=True)
    block_shape = cell_block.shape
    first = cell_block.reshape(all_bins, -1).astype(jnp.float32)
    change = collide(table, first).reshape(block_shape)
    change = lax.all_to_all(change, "bins", split_axis=0, concat_axis=2, tiled=True)
    return change.reshape(local_bins, width_x, width_z, width_y).astype(jnp.float32)


def paired_table(bin_order, kernel_index, collision_kernels):
    local_bins = bin_order.shape[0] // 2
    me = lax.axis_index("bins")
    order = lax.dynamic_slice_in_dim(
        jnp.concatenate([bin_order, bin_order]), me * local_bins, 2 * local_bins
    )
    return coupling_table(order, kernel_index, collision_kernels)


def paired_collision(grown, table):
    local_bins, width_x, width_z, width_y = grown.shape
    swap = [(0, 1), (1, 0)]
    me = lax.axis_index("bins")
    halves = grown.astype(jnp.bfloat16).reshape(local_bins, 2, width_x // 2, width_z, width_y)
    own = lax.dynamic_index_in_dim(halves, me, axis=1, keepdims=False)
    away = lax.dynamic_index_in_dim(halves, 1 - me, axis=1, keepdims=False)
    kept, returned = [], []
    for chunk in range(width_x // 2):
        arrived = lax.ppermute(away[:, chunk], "bins", swap)
        first = jnp.concatenate([own[:, chunk], arrived], axis=0).reshape(2 * local_bins, -1).astype(jnp.float32)
        if returned:
            change, returned[-1] = collide(table, first, returned[-1])
        else:
            change = collide(table, first)
        change = change.reshape(2 * local_bins, width_z, width_y)
        returned.append(lax.ppermute(change[local_bins:], "bins", swap))
        kept.append(change[:local_bins])
    pair = jnp.stack([jnp.stack(kept, axis=1), jnp.stack(returned, axis=1)], axis=1)
    pair = jnp.where(me == 0, pair, pair[:, ::-1])
    return pair.reshape(local_bins, width_x, width_z, width_y).astype(jnp.float32)


def body(
    bin_mass,
    wind_east,
    wind_north,
    supersaturation,
    potential_temp,
    terrain_height,
    fall_speed,
    growth_rate,
    latent_factor,
    bin_order,
    kernel_index,
    collision_kernels,
):
    local_bins, width_x, width_z, width_y = bin_mass.shape
    levels = lax.axis_index("vert") * width_z + lax.iota(jnp.int32, width_z)
    open_cells = (levels[None, :, None] >= terrain_height[:, None, :]).astype(jnp.float32)
    wind_x = wind_east * open_cells
    wind_y = wind_north * open_cells
    section_weights = (1.0 / 3.0, 0.5, 1.0)
    paired = lax.axis_size("bins") == 2 and width_x % 2 == 0
    table = paired_table(bin_order, kernel_index, collision_kernels) if paired else None
    if width_x >= len(section_weights):
        table, (section_field, bottom) = advect_kernel_call(
            bin_mass, wind_x, wind_y, section_weights, table
        )
    else:
        section_field = bin_mass
        for weight_now in section_weights:
            extended = extended_2(section_field, (("tiles", 1),), 1, jnp.bfloat16)
            section_field = bin_mass + weight_now * tendency(
                extended[:, 1:-1], extended[:, :-2], extended[:, 2:], wind_x, wind_y
            )
        bottom = section_field[:, :, :1, :]
    rim_above = shifted(bottom, "vert", -1)
    from_above = jnp.concatenate([section_field[:, :, 1:], rim_above], axis=2)
    speed = fall_speed[:, None, None, None]
    settled = (1.0 - speed) * section_field + speed * from_above
    growth = growth_rate[:, None, None, None]
    partial = (
        jnp.sum(growth * settled, axis=0),
        jnp.sum(latent_factor[:, None, None, None] * growth * settled, axis=0),
    )
    bin_devices = lax.axis_size("bins")
    if bin_devices == 2:
        swap = [(0, 1), (1, 0)]
        other = lax.ppermute(jnp.stack(partial), "bins", swap)
        uptake, heating = partial[0] + other[0], partial[1] + other[1]
    else:
        uptake, heating = lax.psum(partial, "bins")
    midway = supersaturation * jnp.exp(-0.5 * condense_rate * uptake)
    grown = settled * (1.0 + growth_gain * growth * midway)
    temp_next = potential_temp + heating_gain * midway * heating
    vapor_next = supersaturation * jnp.exp(-condense_rate * uptake)
    if paired:
        change = paired_collision(grown, table)
    else:
        change = spread_collision(grown, bin_order, kernel_index, collision_kernels)
    mass_next = (grown + change) * open_cells
    return (mass_next, temp_next, vapor_next)


def solution(mesh):
    return jax.shard_map(
        body,
        mesh=mesh,
        in_specs=(
            P("bins", ("groups", "tiles"), "vert", None),
            P(("groups", "tiles"), "vert", None),
            P(("groups", "tiles"), "vert", None),
            P(("groups", "tiles"), "vert", None),
            P(("groups", "tiles"), "vert", None),
            P(("groups", "tiles"), None),
            P("bins"),
            P("bins"),
            P("bins"),
            P(),
            P(),
            P(),
        ),
        out_specs=(
            P("bins", ("groups", "tiles"), "vert", None),
            P(("groups", "tiles"), "vert", None),
            P(("groups", "tiles"), "vert", None),
        ),
        check_vma=False,
    )
```

```python
import functools

import jax
import jax.numpy as jnp
from jax import lax
from jax.experimental import pallas as pl
from jax.experimental.pallas import tpu as pltpu
from jax.sharding import PartitionSpec as P

SUB = 8


collision_rate = 0.001
condense_rate = 0.02
heating_gain = 0.03
growth_gain = 0.5
highest = lax.Precision.HIGHEST


def extended_2(array, sides, width, link=jnp.float32):
    for axis, dim in sides:
        size, length = (lax.axis_size(axis), array.shape[dim])
        up = [(i, (i + 1) % size) for i in range(size - 1)]
        down = [(j, i) for i, j in up]
        last = lax.slice_in_dim(array, length - width, length, axis=dim)
        first = lax.slice_in_dim(array, 0, width, axis=dim)
        before = lax.ppermute(last.astype(link), axis, up).astype(array.dtype)
        after = lax.ppermute(first.astype(link), axis, down).astype(array.dtype)
        array = jnp.concatenate([before, array, after], axis=dim)
    return array


def rim_kernel(depth, q_ref, wx_ref, wy_ref, left_ref, right_ref):
    local_bins, width_x = q_ref.shape[:2]
    for out_ref, lo in ((left_ref, width_x - depth), (right_ref, 0)):
        out_ref[0:local_bins] = q_ref[:, lo : lo + depth].astype(out_ref.dtype)
        for k, wind_ref in enumerate((wx_ref, wy_ref)):
            wind = wind_ref[lo : lo + depth]
            high = wind.astype(out_ref.dtype)
            low = (wind - high.astype(jnp.float32)).astype(out_ref.dtype)
            out_ref[local_bins + k] = high
            out_ref[local_bins + 2 + k] = low


def rims(bin_mass, wind_x, wind_y, depth):
    local_bins, width_x, width_z, width_y = bin_mass.shape
    shape = jax.ShapeDtypeStruct((local_bins + 4, depth, width_z, width_y), jnp.bfloat16)
    return pl.pallas_call(
        functools.partial(rim_kernel, depth),
        out_shape=(shape, shape),
    )(bin_mass, wind_x, wind_y)


def advect_kernel(weights, q_ref, left_ref, right_ref, *refs):
    left_winds, right_winds = refs[0:4], refs[4:8]
    wx_ref, wy_ref, out_ref, bottom_ref = refs[8:]
    depth = len(weights)
    width = q_ref.shape[1]

    def widened(ref):
        return ref[...].astype(jnp.float32)

    def winds(rows):
        return [widened(rows[k])[0] + widened(rows[k + 2])[0] for k in (0, 1)]

    (wx_left, wy_left), (wx_right, wy_right) = winds(left_winds), winds(right_winds)
    wx = jnp.concatenate([wx_left, wx_ref[...], wx_right], axis=0)
    wy = jnp.concatenate([wy_left, wy_ref[...], wy_right], axis=0)

    def one_bin(b, carry):
        field = jnp.concatenate(
            [left_ref[b].astype(jnp.float32), q_ref[b], right_ref[b].astype(jnp.float32)], axis=0
        )
        section = field
        for stage, weight_now in enumerate(weights, start=1):
            span = width + 2 * (depth - stage)
            center = section[1 : 1 + span]
            west = section[0:span]
            east = section[2 : 2 + span]
            south = pltpu.roll(center, 1, 2)
            north = pltpu.roll(center, center.shape[2] - 1, 2)
            wind_a = wx[stage : stage + span]
            wind_b = wy[stage : stage + span]
            along_x = wind_a * jnp.where(wind_a > 0.0, center - west, east - center)
            along_y = wind_b * jnp.where(wind_b > 0.0, center - south, north - center)
            section = field[stage : stage + span] + weight_now * (-along_x - along_y)
        out_ref[b] = section
        bottom_ref[b] = section[:, :1]
        return carry

    lax.fori_loop(0, q_ref.shape[0], one_bin, 0)


def advect_kernel_call(bin_mass, wind_x, wind_y, section_weights, tie):
    local_bins, width_x, width_z, width_y = bin_mass.shape
    depth = len(section_weights)
    tiles = lax.axis_size("tiles")
    up = [(i, i + 1) for i in range(tiles - 1)]
    down = [(j, i) for i, j in up]

    left, right = (
        lax.ppermute(message, "tiles", pairs)
        for message, pairs in zip(rims(bin_mass, wind_x, wind_y, depth), (up, down))
    )
    left, tie = lax.optimization_barrier((left, tie))
    block = max(d for d in range(1, 34) if local_bins % d == 0)
    rim_spec = pl.BlockSpec((block, depth, width_z, width_y), lambda i: (i, 0, 0, 0))
    row_specs = [
        pl.BlockSpec((1, depth, width_z, width_y), lambda i, row=local_bins + k: (row, 0, 0, 0))
        for k in range(4)
    ]
    own_spec = pl.BlockSpec((block, width_x, width_z, width_y), lambda i: (i, 0, 0, 0))
    wind_spec = pl.BlockSpec(wind_x.shape, lambda i: (0, 0, 0))
    cells = local_bins * width_x * width_z * width_y
    return tie, pl.pallas_call(
        functools.partial(advect_kernel, section_weights),
        out_shape=(
            jax.ShapeDtypeStruct(bin_mass.shape, bin_mass.dtype),
            jax.ShapeDtypeStruct((local_bins, width_x, 1, width_y), bin_mass.dtype),
        ),
        grid=(local_bins // block,),
        in_specs=[own_spec, rim_spec, rim_spec] + row_specs + row_specs + [wind_spec, wind_spec],
        out_specs=(own_spec, pl.BlockSpec((block, width_x, 1, width_y), lambda i: (i, 0, 0, 0))),
        cost_estimate=pl.CostEstimate(flops=80 * cells, bytes_accessed=20 * cells, transcendentals=0),
    )(bin_mass, left, right, *([left] * 4), *([right] * 4), wind_x, wind_y)

def shifted(block, axis, distance):
    devices = range(lax.axis_size(axis))
    route = [(i - distance, i) for i in devices if i - distance in devices]
    return lax.ppermute(block, axis, route)


def tendency(center_cells, left_cells, right_cells, wind_x, wind_y):
    south_cells = jnp.roll(center_cells, 1, axis=3)
    north_cells = jnp.roll(center_cells, -1, axis=3)
    along_x = jnp.maximum(wind_x, 0.0) * (center_cells - left_cells) + jnp.minimum(wind_x, 0.0) * (
        right_cells - center_cells
    )
    along_y = jnp.maximum(wind_y, 0.0) * (center_cells - south_cells) + jnp.minimum(wind_y, 0.0) * (
        north_cells - center_cells
    )
    return -along_x - along_y


def coupling_table(bin_order, kernel_index, collision_kernels):
    class_count = kernel_index.shape[0]
    table_count = collision_kernels.shape[0]
    class_bins = collision_kernels.shape[1]
    bin_class = bin_order // class_bins
    bin_within = bin_order % class_bins
    kernel_pick = (kernel_index[:, :, None] == lax.iota(jnp.int32, table_count)).astype(jnp.float32)
    block_table = jnp.einsum(
        "ack,kmn->acmn", kernel_pick, collision_kernels.astype(jnp.float32), precision=highest
    )
    class_hot = (bin_class[:, None] == lax.iota(jnp.int32, class_count)).astype(jnp.float32)
    within_hot = (bin_within[:, None] == lax.iota(jnp.int32, class_bins)).astype(jnp.float32)
    row_table = jnp.einsum("bm,acmn->bacn", within_hot, block_table, precision=highest)
    row_table = jnp.einsum("ba,bacn->bcn", class_hot, row_table, precision=highest)
    coupling = jnp.einsum("bcn,dc,dn->bd", row_table, class_hot, within_hot, precision=highest)
    same_class = jnp.dot(class_hot, class_hot.T, precision=highest)
    return jnp.concatenate([coupling, same_class], axis=0).astype(jnp.bfloat16)


def collide(table, first, tie=None):
    all_bins = table.shape[1]
    iterate = first
    for substep in range(SUB):
        if tie is not None and substep == SUB // 2:
            iterate, tie = lax.optimization_barrier((iterate, tie))
        products = jnp.dot(table, iterate.astype(jnp.bfloat16), preferred_element_type=jnp.float32)
        iterate = iterate + collision_rate * products[all_bins:] * products[:all_bins]
    change = (iterate - first).astype(jnp.bfloat16)
    return change if tie is None else (change, tie)


def spread_collision(grown, bin_order, kernel_index, collision_kernels):
    local_bins, width_x, width_z, width_y = grown.shape
    table = coupling_table(bin_order, kernel_index, collision_kernels)
    all_bins = table.shape[1]
    start = grown.astype(jnp.bfloat16).reshape(local_bins, width_x, width_z * width_y)
    cell_block = lax.all_to_all(start, "bins", split_axis=2, concat_axis=0, tiled=True)
    block_shape = cell_block.shape
    first = cell_block.reshape(all_bins, -1).astype(jnp.float32)
    change = collide(table, first).reshape(block_shape)
    change = lax.all_to_all(change, "bins", split_axis=0, concat_axis=2, tiled=True)
    return change.reshape(local_bins, width_x, width_z, width_y).astype(jnp.float32)


def paired_table(bin_order, kernel_index, collision_kernels):
    local_bins = bin_order.shape[0] // 2
    me = lax.axis_index("bins")
    order = lax.dynamic_slice_in_dim(
        jnp.concatenate([bin_order, bin_order]), me * local_bins, 2 * local_bins
    )
    return coupling_table(order, kernel_index, collision_kernels)


def paired_collision(grown, table):
    local_bins, width_x, width_z, width_y = grown.shape
    swap = [(0, 1), (1, 0)]
    me = lax.axis_index("bins")
    halves = grown.astype(jnp.bfloat16).reshape(local_bins, 2, width_x // 2, width_z, width_y)
    own = lax.dynamic_index_in_dim(halves, me, axis=1, keepdims=False)
    away = lax.dynamic_index_in_dim(halves, 1 - me, axis=1, keepdims=False)
    kept, returned = [], []
    for chunk in range(width_x // 2):
        arrived = lax.ppermute(away[:, chunk], "bins", swap)
        first = jnp.concatenate([own[:, chunk], arrived], axis=0).reshape(2 * local_bins, -1).astype(jnp.float32)
        if returned:
            change, returned[-1] = collide(table, first, returned[-1])
        else:
            change = collide(table, first)
        change = change.reshape(2 * local_bins, width_z, width_y)
        returned.append(lax.ppermute(change[local_bins:], "bins", swap))
        kept.append(change[:local_bins])
    pair = jnp.stack([jnp.stack(kept, axis=1), jnp.stack(returned, axis=1)], axis=1)
    pair = jnp.where(me == 0, pair, pair[:, ::-1])
    return pair.reshape(local_bins, width_x, width_z, width_y).astype(jnp.float32)


def body(
    bin_mass,
    wind_east,
    wind_north,
    supersaturation,
    potential_temp,
    terrain_height,
    fall_speed,
    growth_rate,
    latent_factor,
    bin_order,
    kernel_index,
    collision_kernels,
):
    local_bins, width_x, width_z, width_y = bin_mass.shape
    levels = lax.axis_index("vert") * width_z + lax.iota(jnp.int32, width_z)
    open_cells = (levels[None, :, None] >= terrain_height[:, None, :]).astype(jnp.float32)
    wind_x = wind_east * open_cells
    wind_y = wind_north * open_cells
    section_weights = (1.0 / 3.0, 0.5, 1.0)
    paired = lax.axis_size("bins") == 2 and width_x % 2 == 0
    table = paired_table(bin_order, kernel_index, collision_kernels) if paired else None
    if width_x >= len(section_weights):
        table, (section_field, bottom) = advect_kernel_call(
            bin_mass, wind_x, wind_y, section_weights, table
        )
    else:
        section_field = bin_mass
        for weight_now in section_weights:
            extended = extended_2(section_field, (("tiles", 1),), 1, jnp.bfloat16)
            section_field = bin_mass + weight_now * tendency(
                extended[:, 1:-1], extended[:, :-2], extended[:, 2:], wind_x, wind_y
            )
        bottom = section_field[:, :, :1, :]
    rim_above = shifted(bottom, "vert", -1)
    from_above = jnp.concatenate([section_field[:, :, 1:], rim_above], axis=2)
    speed = fall_speed[:, None, None, None]
    settled = (1.0 - speed) * section_field + speed * from_above
    growth = growth_rate[:, None, None, None]
    partial = (
        jnp.sum(growth * settled, axis=0),
        jnp.sum(latent_factor[:, None, None, None] * growth * settled, axis=0),
    )
    bin_devices = lax.axis_size("bins")
    if bin_devices == 2:
        swap = [(0, 1), (1, 0)]
        other = lax.ppermute(jnp.stack(partial), "bins", swap)
        uptake, heating = partial[0] + other[0], partial[1] + other[1]
    else:
        uptake, heating = lax.psum(partial, "bins")
    midway = supersaturation * jnp.exp(-0.5 * condense_rate * uptake)
    grown = settled * (1.0 + growth_gain * growth * midway)
    temp_next = potential_temp + heating_gain * midway * heating
    vapor_next = supersaturation * jnp.exp(-condense_rate * uptake)
    if paired:
        change = paired_collision(grown, table)
    else:
        change = spread_collision(grown, bin_order, kernel_index, collision_kernels)
    mass_next = (grown + change) * open_cells
    return (mass_next, temp_next, vapor_next)


def solution(mesh):
    return jax.shard_map(
        body,
        mesh=mesh,
        in_specs=(
            P("bins", ("groups", "tiles"), "vert", None),
            P(("groups", "tiles"), "vert", None),
            P(("groups", "tiles"), "vert", None),
            P(("groups", "tiles"), "vert", None),
            P(("groups", "tiles"), "vert", None),
            P(("groups", "tiles"), None),
            P("bins"),
            P("bins"),
            P("bins"),
            P(),
            P(),
            P(),
        ),
        out_specs=(
            P("bins", ("groups", "tiles"), "vert", None),
            P(("groups", "tiles"), "vert", None),
            P(("groups", "tiles"), "vert", None),
        ),
        check_vma=False,
    )
```

```python
import functools

import jax
import jax.numpy as jnp
from jax import lax
from jax.experimental import pallas as pl
from jax.experimental.pallas import tpu as pltpu
from jax.sharding import PartitionSpec as P

SUB = 8


collision_rate = 0.001
condense_rate = 0.02
heating_gain = 0.03
growth_gain = 0.5
highest = lax.Precision.HIGHEST


def extended_2(array, sides, width, link=jnp.float32):
    for axis, dim in sides:
        size, length = (lax.axis_size(axis), array.shape[dim])
        up = [(i, (i + 1) % size) for i in range(size - 1)]
        down = [(j, i) for i, j in up]
        last = lax.slice_in_dim(array, length - width, length, axis=dim)
        first = lax.slice_in_dim(array, 0, width, axis=dim)
        before = lax.ppermute(last.astype(link), axis, up).astype(array.dtype)
        after = lax.ppermute(first.astype(link), axis, down).astype(array.dtype)
        array = jnp.concatenate([before, array, after], axis=dim)
    return array


def rim_kernel(depth, q_ref, wx_ref, wy_ref, left_ref, right_ref):
    local_bins, width_x = q_ref.shape[:2]
    for out_ref, lo in ((left_ref, width_x - depth), (right_ref, 0)):
        out_ref[0:local_bins] = q_ref[:, lo : lo + depth].astype(out_ref.dtype)
        for k, wind_ref in enumerate((wx_ref, wy_ref)):
            wind = wind_ref[lo : lo + depth]
            high = wind.astype(out_ref.dtype)
            low = (wind - high.astype(jnp.float32)).astype(out_ref.dtype)
            out_ref[local_bins + k] = high
            out_ref[local_bins + 2 + k] = low


def rims(bin_mass, wind_x, wind_y, depth):
    local_bins, width_x, width_z, width_y = bin_mass.shape
    shape = jax.ShapeDtypeStruct((local_bins + 4, depth, width_z, width_y), jnp.bfloat16)
    return pl.pallas_call(
        functools.partial(rim_kernel, depth),
        out_shape=(shape, shape),
    )(bin_mass, wind_x, wind_y)


def advect_kernel(weights, q_ref, left_ref, right_ref, *refs):
    left_winds, right_winds = refs[0:4], refs[4:8]
    wx_ref, wy_ref, out_ref, bottom_ref = refs[8:]
    depth = len(weights)
    width = q_ref.shape[1]

    def widened(ref):
        return ref[...].astype(jnp.float32)

    def winds(rows):
        return [widened(rows[k])[0] + widened(rows[k + 2])[0] for k in (0, 1)]

    (wx_left, wy_left), (wx_right, wy_right) = winds(left_winds), winds(right_winds)
    field = jnp.concatenate([widened(left_ref), q_ref[...], widened(right_ref)], axis=1)
    wx = jnp.concatenate([wx_left, wx_ref[...], wx_right], axis=0)
    wy = jnp.concatenate([wy_left, wy_ref[...], wy_right], axis=0)
    section = field
    for stage, weight_now in enumerate(weights, start=1):
        span = width + 2 * (depth - stage)
        center = section[:, 1 : 1 + span]
        west = section[:, 0:span]
        east = section[:, 2 : 2 + span]
        south = pltpu.roll(center, 1, 3)
        north = pltpu.roll(center, center.shape[3] - 1, 3)
        wind_a = wx[stage : stage + span]
        wind_b = wy[stage : stage + span]
        along_x = jnp.maximum(wind_a, 0.0) * (center - west) + jnp.minimum(wind_a, 0.0) * (east - center)
        along_y = jnp.maximum(wind_b, 0.0) * (center - south) + jnp.minimum(wind_b, 0.0) * (north - center)
        section = field[:, stage : stage + span] + weight_now * (-along_x - along_y)
    out_ref[...] = section
    bottom_ref[...] = section[:, :, :1]


def advect_kernel_call(bin_mass, wind_x, wind_y, section_weights, tie):
    local_bins, width_x, width_z, width_y = bin_mass.shape
    depth = len(section_weights)
    tiles = lax.axis_size("tiles")
    up = [(i, i + 1) for i in range(tiles - 1)]
    down = [(j, i) for i, j in up]

    left, right = (
        lax.ppermute(message, "tiles", pairs)
        for message, pairs in zip(rims(bin_mass, wind_x, wind_y, depth), (up, down))
    )
    left, tie = lax.optimization_barrier((left, tie))
    block = max(d for d in range(1, 13) if local_bins % d == 0)
    rim_spec = pl.BlockSpec((block, depth, width_z, width_y), lambda i: (i, 0, 0, 0))
    row_specs = [
        pl.BlockSpec((1, depth, width_z, width_y), lambda i, row=local_bins + k: (row, 0, 0, 0))
        for k in range(4)
    ]
    own_spec = pl.BlockSpec((block, width_x, width_z, width_y), lambda i: (i, 0, 0, 0))
    wind_spec = pl.BlockSpec(wind_x.shape, lambda i: (0, 0, 0))
    cells = local_bins * width_x * width_z * width_y
    return tie, pl.pallas_call(
        functools.partial(advect_kernel, section_weights),
        out_shape=(
            jax.ShapeDtypeStruct(bin_mass.shape, bin_mass.dtype),
            jax.ShapeDtypeStruct((local_bins, width_x, 1, width_y), bin_mass.dtype),
        ),
        grid=(local_bins // block,),
        in_specs=[own_spec, rim_spec, rim_spec] + row_specs + row_specs + [wind_spec, wind_spec],
        out_specs=(own_spec, pl.BlockSpec((block, width_x, 1, width_y), lambda i: (i, 0, 0, 0))),
        cost_estimate=pl.CostEstimate(flops=80 * cells, bytes_accessed=20 * cells, transcendentals=0),
    )(bin_mass, left, right, *([left] * 4), *([right] * 4), wind_x, wind_y)

def shifted(block, axis, distance):
    devices = range(lax.axis_size(axis))
    route = [(i - distance, i) for i in devices if i - distance in devices]
    return lax.ppermute(block, axis, route)


def tendency(center_cells, left_cells, right_cells, wind_x, wind_y):
    south_cells = jnp.roll(center_cells, 1, axis=3)
    north_cells = jnp.roll(center_cells, -1, axis=3)
    along_x = jnp.maximum(wind_x, 0.0) * (center_cells - left_cells) + jnp.minimum(wind_x, 0.0) * (
        right_cells - center_cells
    )
    along_y = jnp.maximum(wind_y, 0.0) * (center_cells - south_cells) + jnp.minimum(wind_y, 0.0) * (
        north_cells - center_cells
    )
    return -along_x - along_y


def coupling_table(bin_order, kernel_index, collision_kernels):
    class_count = kernel_index.shape[0]
    table_count = collision_kernels.shape[0]
    class_bins = collision_kernels.shape[1]
    bin_class = bin_order // class_bins
    bin_within = bin_order % class_bins
    kernel_pick = (kernel_index[:, :, None] == lax.iota(jnp.int32, table_count)).astype(jnp.float32)
    block_table = jnp.einsum(
        "ack,kmn->acmn", kernel_pick, collision_kernels.astype(jnp.float32), precision=highest
    )
    class_hot = (bin_class[:, None] == lax.iota(jnp.int32, class_count)).astype(jnp.float32)
    within_hot = (bin_within[:, None] == lax.iota(jnp.int32, class_bins)).astype(jnp.float32)
    row_table = jnp.einsum("bm,acmn->bacn", within_hot, block_table, precision=highest)
    row_table = jnp.einsum("ba,bacn->bcn", class_hot, row_table, precision=highest)
    coupling = jnp.einsum("bcn,dc,dn->bd", row_table, class_hot, within_hot, precision=highest)
    same_class = jnp.dot(class_hot, class_hot.T, precision=highest)
    return jnp.concatenate([coupling, same_class], axis=0).astype(jnp.bfloat16)


def collide(table, first, tie=None):
    all_bins = table.shape[1]
    iterate = first
    for substep in range(SUB):
        if tie is not None and substep == SUB // 2:
            iterate, tie = lax.optimization_barrier((iterate, tie))
        products = jnp.dot(table, iterate.astype(jnp.bfloat16), preferred_element_type=jnp.float32)
        iterate = iterate + collision_rate * products[all_bins:] * products[:all_bins]
    change = (iterate - first).astype(jnp.bfloat16)
    return change if tie is None else (change, tie)


def spread_collision(grown, bin_order, kernel_index, collision_kernels):
    local_bins, width_x, width_z, width_y = grown.shape
    table = coupling_table(bin_order, kernel_index, collision_kernels)
    all_bins = table.shape[1]
    start = grown.astype(jnp.bfloat16).reshape(local_bins, width_x, width_z * width_y)
    cell_block = lax.all_to_all(start, "bins", split_axis=2, concat_axis=0, tiled=True)
    block_shape = cell_block.shape
    first = cell_block.reshape(all_bins, -1).astype(jnp.float32)
    change = collide(table, first).reshape(block_shape)
    change = lax.all_to_all(change, "bins", split_axis=0, concat_axis=2, tiled=True)
    return change.reshape(local_bins, width_x, width_z, width_y).astype(jnp.float32)


def paired_table(bin_order, kernel_index, collision_kernels):
    local_bins = bin_order.shape[0] // 2
    me = lax.axis_index("bins")
    order = lax.dynamic_slice_in_dim(
        jnp.concatenate([bin_order, bin_order]), me * local_bins, 2 * local_bins
    )
    return coupling_table(order, kernel_index, collision_kernels)


def paired_collision(grown, table):
    local_bins, width_x, width_z, width_y = grown.shape
    swap = [(0, 1), (1, 0)]
    me = lax.axis_index("bins")
    halves = grown.astype(jnp.bfloat16).reshape(local_bins, 2, width_x // 2, width_z, width_y)
    own = lax.dynamic_index_in_dim(halves, me, axis=1, keepdims=False)
    away = lax.dynamic_index_in_dim(halves, 1 - me, axis=1, keepdims=False)
    kept, returned = [], []
    for chunk in range(width_x // 2):
        arrived = lax.ppermute(away[:, chunk], "bins", swap)
        first = jnp.concatenate([own[:, chunk], arrived], axis=0).reshape(2 * local_bins, -1).astype(jnp.float32)
        if returned:
            change, returned[-1] = collide(table, first, returned[-1])
        else:
            change = collide(table, first)
        change = change.reshape(2 * local_bins, width_z, width_y)
        returned.append(lax.ppermute(change[local_bins:], "bins", swap))
        kept.append(change[:local_bins])
    pair = jnp.stack([jnp.stack(kept, axis=1), jnp.stack(returned, axis=1)], axis=1)
    pair = jnp.where(me == 0, pair, pair[:, ::-1])
    return pair.reshape(local_bins, width_x, width_z, width_y).astype(jnp.float32)


def body(
    bin_mass,
    wind_east,
    wind_north,
    supersaturation,
    potential_temp,
    terrain_height,
    fall_speed,
    growth_rate,
    latent_factor,
    bin_order,
    kernel_index,
    collision_kernels,
):
    local_bins, width_x, width_z, width_y = bin_mass.shape
    levels = lax.axis_index("vert") * width_z + lax.iota(jnp.int32, width_z)
    open_cells = (levels[None, :, None] >= terrain_height[:, None, :]).astype(jnp.float32)
    wind_x = wind_east * open_cells
    wind_y = wind_north * open_cells
    section_weights = (1.0 / 3.0, 0.5, 1.0)
    paired = lax.axis_size("bins") == 2 and width_x % 2 == 0
    table = paired_table(bin_order, kernel_index, collision_kernels) if paired else None
    if width_x >= len(section_weights):
        table, (section_field, bottom) = advect_kernel_call(
            bin_mass, wind_x, wind_y, section_weights, table
        )
    else:
        section_field = bin_mass
        for weight_now in section_weights:
            extended = extended_2(section_field, (("tiles", 1),), 1, jnp.bfloat16)
            section_field = bin_mass + weight_now * tendency(
                extended[:, 1:-1], extended[:, :-2], extended[:, 2:], wind_x, wind_y
            )
        bottom = section_field[:, :, :1, :]
    rim_above = shifted(bottom, "vert", -1)
    from_above = jnp.concatenate([section_field[:, :, 1:], rim_above], axis=2)
    speed = fall_speed[:, None, None, None]
    settled = (1.0 - speed) * section_field + speed * from_above
    growth = growth_rate[:, None, None, None]
    partial = (
        jnp.sum(growth * settled, axis=0),
        jnp.sum(latent_factor[:, None, None, None] * growth * settled, axis=0),
    )
    bin_devices = lax.axis_size("bins")
    if bin_devices == 2:
        swap = [(0, 1), (1, 0)]
        other = lax.ppermute(jnp.stack(partial), "bins", swap)
        uptake, heating = partial[0] + other[0], partial[1] + other[1]
    else:
        uptake, heating = lax.psum(partial, "bins")
    midway = supersaturation * jnp.exp(-0.5 * condense_rate * uptake)
    grown = settled * (1.0 + growth_gain * growth * midway)
    temp_next = potential_temp + heating_gain * midway * heating
    vapor_next = supersaturation * jnp.exp(-condense_rate * uptake)
    if paired:
        change = paired_collision(grown, table)
    else:
        change = spread_collision(grown, bin_order, kernel_index, collision_kernels)
    mass_next = (grown + change) * open_cells
    return (mass_next, temp_next, vapor_next)


def solution(mesh):
    return jax.shard_map(
        body,
        mesh=mesh,
        in_specs=(
            P("bins", ("groups", "tiles"), "vert", None),
            P(("groups", "tiles"), "vert", None),
            P(("groups", "tiles"), "vert", None),
            P(("groups", "tiles"), "vert", None),
            P(("groups", "tiles"), "vert", None),
            P(("groups", "tiles"), None),
            P("bins"),
            P("bins"),
            P("bins"),
            P(),
            P(),
            P(),
        ),
        out_specs=(
            P("bins", ("groups", "tiles"), "vert", None),
            P(("groups", "tiles"), "vert", None),
            P(("groups", "tiles"), "vert", None),
        ),
        check_vma=False,
    )
```

```python
import functools

import jax
import jax.numpy as jnp
from jax import lax
from jax.experimental import pallas as pl
from jax.experimental.pallas import tpu as pltpu
from jax.sharding import PartitionSpec as P

SUB = 8


collision_rate = 0.001
condense_rate = 0.02
heating_gain = 0.03
growth_gain = 0.5
highest = lax.Precision.HIGHEST


def extended_2(array, sides, width, link=jnp.float32):
    for axis, dim in sides:
        size, length = (lax.axis_size(axis), array.shape[dim])
        up = [(i, (i + 1) % size) for i in range(size - 1)]
        down = [(j, i) for i, j in up]
        last = lax.slice_in_dim(array, length - width, length, axis=dim)
        first = lax.slice_in_dim(array, 0, width, axis=dim)
        before = lax.ppermute(last.astype(link), axis, up).astype(array.dtype)
        after = lax.ppermute(first.astype(link), axis, down).astype(array.dtype)
        array = jnp.concatenate([before, array, after], axis=dim)
    return array


def rim_kernel(depth, q_ref, wx_ref, wy_ref, left_ref, right_ref):
    local_bins, width_x = q_ref.shape[:2]
    for out_ref, lo in ((left_ref, width_x - depth), (right_ref, 0)):
        out_ref[0:local_bins] = q_ref[:, lo : lo + depth].astype(out_ref.dtype)
        for k, wind_ref in enumerate((wx_ref, wy_ref)):
            wind = wind_ref[lo : lo + depth]
            high = wind.astype(out_ref.dtype)
            low = (wind - high.astype(jnp.float32)).astype(out_ref.dtype)
            out_ref[local_bins + k] = high
            out_ref[local_bins + 2 + k] = low


def rims(bin_mass, wind_x, wind_y, depth):
    local_bins, width_x, width_z, width_y = bin_mass.shape
    shape = jax.ShapeDtypeStruct((local_bins + 4, depth, width_z, width_y), jnp.bfloat16)
    return pl.pallas_call(
        functools.partial(rim_kernel, depth),
        out_shape=(shape, shape),
    )(bin_mass, wind_x, wind_y)


def advect_kernel(weights, q_ref, left_ref, right_ref, *refs):
    left_winds, right_winds = refs[0:4], refs[4:8]
    wx_ref, wy_ref, out_ref, bottom_ref = refs[8:]
    depth = len(weights)
    width = q_ref.shape[1]

    def widened(ref):
        return ref[...].astype(jnp.float32)

    def winds(rows):
        return [widened(rows[k])[0] + widened(rows[k + 2])[0] for k in (0, 1)]

    (wx_left, wy_left), (wx_right, wy_right) = winds(left_winds), winds(right_winds)
    field = jnp.concatenate([widened(left_ref), q_ref[...], widened(right_ref)], axis=1)
    wx = jnp.concatenate([wx_left, wx_ref[...], wx_right], axis=0)
    wy = jnp.concatenate([wy_left, wy_ref[...], wy_right], axis=0)
    section = field
    for stage, weight_now in enumerate(weights, start=1):
        span = width + 2 * (depth - stage)
        center = section[:, 1 : 1 + span]
        west = section[:, 0:span]
        east = section[:, 2 : 2 + span]
        south = pltpu.roll(center, 1, 3)
        north = pltpu.roll(center, center.shape[3] - 1, 3)
        wind_a = wx[stage : stage + span]
        wind_b = wy[stage : stage + span]
        along_x = jnp.maximum(wind_a, 0.0) * (center - west) + jnp.minimum(wind_a, 0.0) * (east - center)
        along_y = jnp.maximum(wind_b, 0.0) * (center - south) + jnp.minimum(wind_b, 0.0) * (north - center)
        section = field[:, stage : stage + span] + weight_now * (-along_x - along_y)
    out_ref[...] = section
    bottom_ref[...] = section[:, :, :1]


def advect_kernel_call(bin_mass, wind_x, wind_y, section_weights, tie):
    local_bins, width_x, width_z, width_y = bin_mass.shape
    depth = len(section_weights)
    tiles = lax.axis_size("tiles")
    up = [(i, i + 1) for i in range(tiles - 1)]
    down = [(j, i) for i, j in up]

    left, right = (
        lax.ppermute(message, "tiles", pairs)
        for message, pairs in zip(rims(bin_mass, wind_x, wind_y, depth), (up, down))
    )
    left, tie = lax.optimization_barrier((left, tie))
    block = max(d for d in range(1, 67) if local_bins % d == 0)
    rim_spec = pl.BlockSpec((block, depth, width_z, width_y), lambda i: (i, 0, 0, 0))
    row_specs = [
        pl.BlockSpec((1, depth, width_z, width_y), lambda i, row=local_bins + k: (row, 0, 0, 0))
        for k in range(4)
    ]
    own_spec = pl.BlockSpec((block, width_x, width_z, width_y), lambda i: (i, 0, 0, 0))
    wind_spec = pl.BlockSpec(wind_x.shape, lambda i: (0, 0, 0))
    cells = local_bins * width_x * width_z * width_y
    return tie, pl.pallas_call(
        functools.partial(advect_kernel, section_weights),
        out_shape=(
            jax.ShapeDtypeStruct(bin_mass.shape, bin_mass.dtype),
            jax.ShapeDtypeStruct((local_bins, width_x, 1, width_y), bin_mass.dtype),
        ),
        grid=(local_bins // block,),
        in_specs=[own_spec, rim_spec, rim_spec] + row_specs + row_specs + [wind_spec, wind_spec],
        out_specs=(own_spec, pl.BlockSpec((block, width_x, 1, width_y), lambda i: (i, 0, 0, 0))),
        cost_estimate=pl.CostEstimate(flops=80 * cells, bytes_accessed=20 * cells, transcendentals=0),
    )(bin_mass, left, right, *([left] * 4), *([right] * 4), wind_x, wind_y)

def shifted(block, axis, distance):
    devices = range(lax.axis_size(axis))
    route = [(i - distance, i) for i in devices if i - distance in devices]
    return lax.ppermute(block, axis, route)


def tendency(center_cells, left_cells, right_cells, wind_x, wind_y):
    south_cells = jnp.roll(center_cells, 1, axis=3)
    north_cells = jnp.roll(center_cells, -1, axis=3)
    along_x = jnp.maximum(wind_x, 0.0) * (center_cells - left_cells) + jnp.minimum(wind_x, 0.0) * (
        right_cells - center_cells
    )
    along_y = jnp.maximum(wind_y, 0.0) * (center_cells - south_cells) + jnp.minimum(wind_y, 0.0) * (
        north_cells - center_cells
    )
    return -along_x - along_y


def coupling_table(bin_order, kernel_index, collision_kernels):
    class_count = kernel_index.shape[0]
    table_count = collision_kernels.shape[0]
    class_bins = collision_kernels.shape[1]
    bin_class = bin_order // class_bins
    bin_within = bin_order % class_bins
    kernel_pick = (kernel_index[:, :, None] == lax.iota(jnp.int32, table_count)).astype(jnp.float32)
    block_table = jnp.einsum(
        "ack,kmn->acmn", kernel_pick, collision_kernels.astype(jnp.float32), precision=highest
    )
    class_hot = (bin_class[:, None] == lax.iota(jnp.int32, class_count)).astype(jnp.float32)
    within_hot = (bin_within[:, None] == lax.iota(jnp.int32, class_bins)).astype(jnp.float32)
    row_table = jnp.einsum("bm,acmn->bacn", within_hot, block_table, precision=highest)
    row_table = jnp.einsum("ba,bacn->bcn", class_hot, row_table, precision=highest)
    coupling = jnp.einsum("bcn,dc,dn->bd", row_table, class_hot, within_hot, precision=highest)
    same_class = jnp.dot(class_hot, class_hot.T, precision=highest)
    return jnp.concatenate([coupling, same_class], axis=0).astype(jnp.bfloat16)


def collide(table, first, tie=None):
    all_bins = table.shape[1]
    iterate = first
    for substep in range(SUB):
        if tie is not None and substep == SUB // 2:
            iterate, tie = lax.optimization_barrier((iterate, tie))
        products = jnp.dot(table, iterate.astype(jnp.bfloat16), preferred_element_type=jnp.float32)
        iterate = iterate + collision_rate * products[all_bins:] * products[:all_bins]
    change = (iterate - first).astype(jnp.bfloat16)
    return change if tie is None else (change, tie)


def spread_collision(grown, bin_order, kernel_index, collision_kernels):
    local_bins, width_x, width_z, width_y = grown.shape
    table = coupling_table(bin_order, kernel_index, collision_kernels)
    all_bins = table.shape[1]
    start = grown.astype(jnp.bfloat16).reshape(local_bins, width_x, width_z * width_y)
    cell_block = lax.all_to_all(start, "bins", split_axis=2, concat_axis=0, tiled=True)
    block_shape = cell_block.shape
    first = cell_block.reshape(all_bins, -1).astype(jnp.float32)
    change = collide(table, first).reshape(block_shape)
    change = lax.all_to_all(change, "bins", split_axis=0, concat_axis=2, tiled=True)
    return change.reshape(local_bins, width_x, width_z, width_y).astype(jnp.float32)


def paired_table(bin_order, kernel_index, collision_kernels):
    local_bins = bin_order.shape[0] // 2
    me = lax.axis_index("bins")
    order = lax.dynamic_slice_in_dim(
        jnp.concatenate([bin_order, bin_order]), me * local_bins, 2 * local_bins
    )
    return coupling_table(order, kernel_index, collision_kernels)


def paired_collision(grown, table):
    local_bins, width_x, width_z, width_y = grown.shape
    swap = [(0, 1), (1, 0)]
    me = lax.axis_index("bins")
    halves = grown.astype(jnp.bfloat16).reshape(local_bins, 2, width_x // 2, width_z, width_y)
    own = lax.dynamic_index_in_dim(halves, me, axis=1, keepdims=False)
    away = lax.dynamic_index_in_dim(halves, 1 - me, axis=1, keepdims=False)
    kept, returned = [], []
    for chunk in range(width_x // 2):
        arrived = lax.ppermute(away[:, chunk], "bins", swap)
        first = jnp.concatenate([own[:, chunk], arrived], axis=0).reshape(2 * local_bins, -1).astype(jnp.float32)
        if returned:
            change, returned[-1] = collide(table, first, returned[-1])
        else:
            change = collide(table, first)
        change = change.reshape(2 * local_bins, width_z, width_y)
        returned.append(lax.ppermute(change[local_bins:], "bins", swap))
        kept.append(change[:local_bins])
    pair = jnp.stack([jnp.stack(kept, axis=1), jnp.stack(returned, axis=1)], axis=1)
    pair = jnp.where(me == 0, pair, pair[:, ::-1])
    return pair.reshape(local_bins, width_x, width_z, width_y).astype(jnp.float32)


def body(
    bin_mass,
    wind_east,
    wind_north,
    supersaturation,
    potential_temp,
    terrain_height,
    fall_speed,
    growth_rate,
    latent_factor,
    bin_order,
    kernel_index,
    collision_kernels,
):
    local_bins, width_x, width_z, width_y = bin_mass.shape
    levels = lax.axis_index("vert") * width_z + lax.iota(jnp.int32, width_z)
    open_cells = (levels[None, :, None] >= terrain_height[:, None, :]).astype(jnp.float32)
    wind_x = wind_east * open_cells
    wind_y = wind_north * open_cells
    section_weights = (1.0 / 3.0, 0.5, 1.0)
    paired = lax.axis_size("bins") == 2 and width_x % 2 == 0
    table = paired_table(bin_order, kernel_index, collision_kernels) if paired else None
    if width_x >= len(section_weights):
        table, (section_field, bottom) = advect_kernel_call(
            bin_mass, wind_x, wind_y, section_weights, table
        )
    else:
        section_field = bin_mass
        for weight_now in section_weights:
            extended = extended_2(section_field, (("tiles", 1),), 1, jnp.bfloat16)
            section_field = bin_mass + weight_now * tendency(
                extended[:, 1:-1], extended[:, :-2], extended[:, 2:], wind_x, wind_y
            )
        bottom = section_field[:, :, :1, :]
    rim_above = shifted(bottom, "vert", -1)
    from_above = jnp.concatenate([section_field[:, :, 1:], rim_above], axis=2)
    speed = fall_speed[:, None, None, None]
    settled = (1.0 - speed) * section_field + speed * from_above
    growth = growth_rate[:, None, None, None]
    partial = (
        jnp.sum(growth * settled, axis=0),
        jnp.sum(latent_factor[:, None, None, None] * growth * settled, axis=0),
    )
    bin_devices = lax.axis_size("bins")
    if bin_devices == 2:
        swap = [(0, 1), (1, 0)]
        other = lax.ppermute(jnp.stack(partial), "bins", swap)
        uptake, heating = partial[0] + other[0], partial[1] + other[1]
    else:
        uptake, heating = lax.psum(partial, "bins")
    midway = supersaturation * jnp.exp(-0.5 * condense_rate * uptake)
    grown = settled * (1.0 + growth_gain * growth * midway)
    temp_next = potential_temp + heating_gain * midway * heating
    vapor_next = supersaturation * jnp.exp(-condense_rate * uptake)
    if paired:
        change = paired_collision(grown, table)
    else:
        change = spread_collision(grown, bin_order, kernel_index, collision_kernels)
    mass_next = (grown + change) * open_cells
    return (mass_next, temp_next, vapor_next)


def solution(mesh):
    return jax.shard_map(
        body,
        mesh=mesh,
        in_specs=(
            P("bins", ("groups", "tiles"), "vert", None),
            P(("groups", "tiles"), "vert", None),
            P(("groups", "tiles"), "vert", None),
            P(("groups", "tiles"), "vert", None),
            P(("groups", "tiles"), "vert", None),
            P(("groups", "tiles"), None),
            P("bins"),
            P("bins"),
            P("bins"),
            P(),
            P(),
            P(),
        ),
        out_specs=(
            P("bins", ("groups", "tiles"), "vert", None),
            P(("groups", "tiles"), "vert", None),
            P(("groups", "tiles"), "vert", None),
        ),
        check_vma=False,
    )
```

```python
import functools

import jax
import jax.numpy as jnp
from jax import lax
from jax.experimental import pallas as pl
from jax.experimental.pallas import tpu as pltpu
from jax.sharding import PartitionSpec as P

SUB = 8


collision_rate = 0.001
condense_rate = 0.02
heating_gain = 0.03
growth_gain = 0.5
highest = lax.Precision.HIGHEST


def extended_2(array, sides, width, link=jnp.float32):
    for axis, dim in sides:
        size, length = (lax.axis_size(axis), array.shape[dim])
        up = [(i, (i + 1) % size) for i in range(size - 1)]
        down = [(j, i) for i, j in up]
        last = lax.slice_in_dim(array, length - width, length, axis=dim)
        first = lax.slice_in_dim(array, 0, width, axis=dim)
        before = lax.ppermute(last.astype(link), axis, up).astype(array.dtype)
        after = lax.ppermute(first.astype(link), axis, down).astype(array.dtype)
        array = jnp.concatenate([before, array, after], axis=dim)
    return array


def rim_kernel(depth, q_ref, wx_ref, wy_ref, left_ref, right_ref):
    local_bins = q_ref.shape[0]
    plane = pl.program_id(0)
    width_x = pl.num_programs(0)

    def fill(out_ref):
        out_ref[0:local_bins] = q_ref[...].astype(out_ref.dtype)
        for k, wind_ref in enumerate((wx_ref, wy_ref)):
            wind = wind_ref[...]
            high = wind.astype(out_ref.dtype)
            low = (wind - high.astype(jnp.float32)).astype(out_ref.dtype)
            out_ref[local_bins + k] = high
            out_ref[local_bins + 2 + k] = low

    pl.when(plane >= width_x - depth)(lambda: fill(left_ref))
    pl.when(plane < depth)(lambda: fill(right_ref))


def rims(bin_mass, wind_x, wind_y, depth):
    local_bins, width_x, width_z, width_y = bin_mass.shape
    shape = jax.ShapeDtypeStruct((local_bins + 4, depth, width_z, width_y), jnp.bfloat16)
    out_block = (local_bins + 4, 1, width_z, width_y)
    wind_spec = pl.BlockSpec((1, width_z, width_y), lambda x: (x, 0, 0))
    return pl.pallas_call(
        functools.partial(rim_kernel, depth),
        out_shape=(shape, shape),
        grid=(width_x,),
        in_specs=[
            pl.BlockSpec((local_bins, 1, width_z, width_y), lambda x: (0, x, 0, 0)),
            wind_spec,
            wind_spec,
        ],
        out_specs=(
            pl.BlockSpec(out_block, lambda x: (0, jnp.maximum(x - (width_x - depth), 0), 0, 0)),
            pl.BlockSpec(out_block, lambda x: (0, jnp.minimum(x, depth - 1), 0, 0)),
        ),
    )(bin_mass, wind_x, wind_y)


def advect_kernel(weights, q_ref, left_ref, right_ref, *refs):
    left_winds, right_winds = refs[0:4], refs[4:8]
    wx_ref, wy_ref, out_ref, bottom_ref = refs[8:]
    depth = len(weights)
    width = q_ref.shape[1]

    def widened(ref):
        return ref[...].astype(jnp.float32)

    def winds(rows):
        return [widened(rows[k])[0] + widened(rows[k + 2])[0] for k in (0, 1)]

    (wx_left, wy_left), (wx_right, wy_right) = winds(left_winds), winds(right_winds)
    field = jnp.concatenate([widened(left_ref), q_ref[...], widened(right_ref)], axis=1)
    wx = jnp.concatenate([wx_left, wx_ref[...], wx_right], axis=0)
    wy = jnp.concatenate([wy_left, wy_ref[...], wy_right], axis=0)
    section = field
    for stage, weight_now in enumerate(weights, start=1):
        span = width + 2 * (depth - stage)
        center = section[:, 1 : 1 + span]
        west = section[:, 0:span]
        east = section[:, 2 : 2 + span]
        south = pltpu.roll(center, 1, 3)
        north = pltpu.roll(center, center.shape[3] - 1, 3)
        wind_a = wx[stage : stage + span]
        wind_b = wy[stage : stage + span]
        along_x = jnp.maximum(wind_a, 0.0) * (center - west) + jnp.minimum(wind_a, 0.0) * (east - center)
        along_y = jnp.maximum(wind_b, 0.0) * (center - south) + jnp.minimum(wind_b, 0.0) * (north - center)
        section = field[:, stage : stage + span] + weight_now * (-along_x - along_y)
    out_ref[...] = section
    bottom_ref[...] = section[:, :, :1]


def advect_kernel_call(bin_mass, wind_x, wind_y, section_weights, tie):
    local_bins, width_x, width_z, width_y = bin_mass.shape
    depth = len(section_weights)
    tiles = lax.axis_size("tiles")
    up = [(i, i + 1) for i in range(tiles - 1)]
    down = [(j, i) for i, j in up]

    left, right = (
        lax.ppermute(message, "tiles", pairs)
        for message, pairs in zip(rims(bin_mass, wind_x, wind_y, depth), (up, down))
    )
    left, tie = lax.optimization_barrier((left, tie))
    block = max(d for d in range(1, 34) if local_bins % d == 0)
    rim_spec = pl.BlockSpec((block, depth, width_z, width_y), lambda i: (i, 0, 0, 0))
    row_specs = [
        pl.BlockSpec((1, depth, width_z, width_y), lambda i, row=local_bins + k: (row, 0, 0, 0))
        for k in range(4)
    ]
    own_spec = pl.BlockSpec((block, width_x, width_z, width_y), lambda i: (i, 0, 0, 0))
    wind_spec = pl.BlockSpec(wind_x.shape, lambda i: (0, 0, 0))
    cells = local_bins * width_x * width_z * width_y
    return tie, pl.pallas_call(
        functools.partial(advect_kernel, section_weights),
        out_shape=(
            jax.ShapeDtypeStruct(bin_mass.shape, bin_mass.dtype),
            jax.ShapeDtypeStruct((local_bins, width_x, 1, width_y), bin_mass.dtype),
        ),
        grid=(local_bins // block,),
        in_specs=[own_spec, rim_spec, rim_spec] + row_specs + row_specs + [wind_spec, wind_spec],
        out_specs=(own_spec, pl.BlockSpec((block, width_x, 1, width_y), lambda i: (i, 0, 0, 0))),
        cost_estimate=pl.CostEstimate(flops=80 * cells, bytes_accessed=20 * cells, transcendentals=0),
    )(bin_mass, left, right, *([left] * 4), *([right] * 4), wind_x, wind_y)

def shifted(block, axis, distance):
    devices = range(lax.axis_size(axis))
    route = [(i - distance, i) for i in devices if i - distance in devices]
    return lax.ppermute(block, axis, route)


def tendency(center_cells, left_cells, right_cells, wind_x, wind_y):
    south_cells = jnp.roll(center_cells, 1, axis=3)
    north_cells = jnp.roll(center_cells, -1, axis=3)
    along_x = jnp.maximum(wind_x, 0.0) * (center_cells - left_cells) + jnp.minimum(wind_x, 0.0) * (
        right_cells - center_cells
    )
    along_y = jnp.maximum(wind_y, 0.0) * (center_cells - south_cells) + jnp.minimum(wind_y, 0.0) * (
        north_cells - center_cells
    )
    return -along_x - along_y


def coupling_table(bin_order, kernel_index, collision_kernels):
    class_count = kernel_index.shape[0]
    table_count = collision_kernels.shape[0]
    class_bins = collision_kernels.shape[1]
    bin_class = bin_order // class_bins
    bin_within = bin_order % class_bins
    kernel_pick = (kernel_index[:, :, None] == lax.iota(jnp.int32, table_count)).astype(jnp.float32)
    block_table = jnp.einsum(
        "ack,kmn->acmn", kernel_pick, collision_kernels.astype(jnp.float32), precision=highest
    )
    class_hot = (bin_class[:, None] == lax.iota(jnp.int32, class_count)).astype(jnp.float32)
    within_hot = (bin_within[:, None] == lax.iota(jnp.int32, class_bins)).astype(jnp.float32)
    row_table = jnp.einsum("bm,acmn->bacn", within_hot, block_table, precision=highest)
    row_table = jnp.einsum("ba,bacn->bcn", class_hot, row_table, precision=highest)
    coupling = jnp.einsum("bcn,dc,dn->bd", row_table, class_hot, within_hot, precision=highest)
    same_class = jnp.dot(class_hot, class_hot.T, precision=highest)
    return jnp.concatenate([coupling, same_class], axis=0).astype(jnp.bfloat16)


def collide(table, first, tie=None):
    all_bins = table.shape[1]
    iterate = first
    for substep in range(SUB):
        if tie is not None and substep == SUB // 2:
            iterate, tie = lax.optimization_barrier((iterate, tie))
        products = jnp.dot(table, iterate.astype(jnp.bfloat16), preferred_element_type=jnp.float32)
        iterate = iterate + collision_rate * products[all_bins:] * products[:all_bins]
    change = (iterate - first).astype(jnp.bfloat16)
    return change if tie is None else (change, tie)


def spread_collision(grown, bin_order, kernel_index, collision_kernels):
    local_bins, width_x, width_z, width_y = grown.shape
    table = coupling_table(bin_order, kernel_index, collision_kernels)
    all_bins = table.shape[1]
    start = grown.astype(jnp.bfloat16).reshape(local_bins, width_x, width_z * width_y)
    cell_block = lax.all_to_all(start, "bins", split_axis=2, concat_axis=0, tiled=True)
    block_shape = cell_block.shape
    first = cell_block.reshape(all_bins, -1).astype(jnp.float32)
    change = collide(table, first).reshape(block_shape)
    change = lax.all_to_all(change, "bins", split_axis=0, concat_axis=2, tiled=True)
    return change.reshape(local_bins, width_x, width_z, width_y).astype(jnp.float32)


def paired_table(bin_order, kernel_index, collision_kernels):
    local_bins = bin_order.shape[0] // 2
    me = lax.axis_index("bins")
    order = lax.dynamic_slice_in_dim(
        jnp.concatenate([bin_order, bin_order]), me * local_bins, 2 * local_bins
    )
    return coupling_table(order, kernel_index, collision_kernels)


def paired_collision(grown, table):
    local_bins, width_x, width_z, width_y = grown.shape
    swap = [(0, 1), (1, 0)]
    me = lax.axis_index("bins")
    halves = grown.astype(jnp.bfloat16).reshape(local_bins, 2, width_x // 2, width_z, width_y)
    own = lax.dynamic_index_in_dim(halves, me, axis=1, keepdims=False)
    away = lax.dynamic_index_in_dim(halves, 1 - me, axis=1, keepdims=False)
    kept, returned = [], []
    for chunk in range(width_x // 2):
        arrived = lax.ppermute(away[:, chunk], "bins", swap)
        first = jnp.concatenate([own[:, chunk], arrived], axis=0).reshape(2 * local_bins, -1).astype(jnp.float32)
        if returned:
            change, returned[-1] = collide(table, first, returned[-1])
        else:
            change = collide(table, first)
        change = change.reshape(2 * local_bins, width_z, width_y)
        returned.append(lax.ppermute(change[local_bins:], "bins", swap))
        kept.append(change[:local_bins])
    pair = jnp.stack([jnp.stack(kept, axis=1), jnp.stack(returned, axis=1)], axis=1)
    pair = jnp.where(me == 0, pair, pair[:, ::-1])
    return pair.reshape(local_bins, width_x, width_z, width_y).astype(jnp.float32)


def body(
    bin_mass,
    wind_east,
    wind_north,
    supersaturation,
    potential_temp,
    terrain_height,
    fall_speed,
    growth_rate,
    latent_factor,
    bin_order,
    kernel_index,
    collision_kernels,
):
    local_bins, width_x, width_z, width_y = bin_mass.shape
    levels = lax.axis_index("vert") * width_z + lax.iota(jnp.int32, width_z)
    open_cells = (levels[None, :, None] >= terrain_height[:, None, :]).astype(jnp.float32)
    wind_x = wind_east * open_cells
    wind_y = wind_north * open_cells
    section_weights = (1.0 / 3.0, 0.5, 1.0)
    paired = lax.axis_size("bins") == 2 and width_x % 2 == 0
    table = paired_table(bin_order, kernel_index, collision_kernels) if paired else None
    if width_x >= len(section_weights):
        table, (section_field, bottom) = advect_kernel_call(
            bin_mass, wind_x, wind_y, section_weights, table
        )
    else:
        section_field = bin_mass
        for weight_now in section_weights:
            extended = extended_2(section_field, (("tiles", 1),), 1, jnp.bfloat16)
            section_field = bin_mass + weight_now * tendency(
                extended[:, 1:-1], extended[:, :-2], extended[:, 2:], wind_x, wind_y
            )
        bottom = section_field[:, :, :1, :]
    rim_above = shifted(bottom, "vert", -1)
    from_above = jnp.concatenate([section_field[:, :, 1:], rim_above], axis=2)
    speed = fall_speed[:, None, None, None]
    settled = (1.0 - speed) * section_field + speed * from_above
    growth = growth_rate[:, None, None, None]
    partial = (
        jnp.sum(growth * settled, axis=0),
        jnp.sum(latent_factor[:, None, None, None] * growth * settled, axis=0),
    )
    bin_devices = lax.axis_size("bins")
    if bin_devices == 2:
        swap = [(0, 1), (1, 0)]
        other = lax.ppermute(jnp.stack(partial), "bins", swap)
        uptake, heating = partial[0] + other[0], partial[1] + other[1]
    else:
        uptake, heating = lax.psum(partial, "bins")
    midway = supersaturation * jnp.exp(-0.5 * condense_rate * uptake)
    grown = settled * (1.0 + growth_gain * growth * midway)
    temp_next = potential_temp + heating_gain * midway * heating
    vapor_next = supersaturation * jnp.exp(-condense_rate * uptake)
    if paired:
        change = paired_collision(grown, table)
    else:
        change = spread_collision(grown, bin_order, kernel_index, collision_kernels)
    mass_next = (grown + change) * open_cells
    return (mass_next, temp_next, vapor_next)


def solution(mesh):
    return jax.shard_map(
        body,
        mesh=mesh,
        in_specs=(
            P("bins", ("groups", "tiles"), "vert", None),
            P(("groups", "tiles"), "vert", None),
            P(("groups", "tiles"), "vert", None),
            P(("groups", "tiles"), "vert", None),
            P(("groups", "tiles"), "vert", None),
            P(("groups", "tiles"), None),
            P("bins"),
            P("bins"),
            P("bins"),
            P(),
            P(),
            P(),
        ),
        out_specs=(
            P("bins", ("groups", "tiles"), "vert", None),
            P(("groups", "tiles"), "vert", None),
            P(("groups", "tiles"), "vert", None),
        ),
        check_vma=False,
    )
```

```python
import functools

import jax
import jax.numpy as jnp
from jax import lax
from jax.experimental import pallas as pl
from jax.experimental.pallas import tpu as pltpu
from jax.sharding import PartitionSpec as P

SUB = 8


collision_rate = 0.001
condense_rate = 0.02
heating_gain = 0.03
growth_gain = 0.5
highest = lax.Precision.HIGHEST


def extended_2(array, sides, width, link=jnp.float32):
    for axis, dim in sides:
        size, length = (lax.axis_size(axis), array.shape[dim])
        up = [(i, (i + 1) % size) for i in range(size - 1)]
        down = [(j, i) for i, j in up]
        last = lax.slice_in_dim(array, length - width, length, axis=dim)
        first = lax.slice_in_dim(array, 0, width, axis=dim)
        before = lax.ppermute(last.astype(link), axis, up).astype(array.dtype)
        after = lax.ppermute(first.astype(link), axis, down).astype(array.dtype)
        array = jnp.concatenate([before, array, after], axis=dim)
    return array


def rim_kernel(depth, q_ref, east_ref, north_ref, terrain_ref, left_ref, right_ref):
    local_bins, width_x, width_z = q_ref.shape[:3]
    levels = lax.axis_index("vert") * width_z + lax.broadcasted_iota(jnp.int32, east_ref.shape, 1)
    open_cells = (levels >= terrain_ref[...][:, None, :]).astype(jnp.float32)
    winds = (east_ref[...] * open_cells, north_ref[...] * open_cells)
    for out_ref, lo in ((left_ref, width_x - depth), (right_ref, 0)):
        out_ref[0:local_bins] = q_ref[:, lo : lo + depth].astype(out_ref.dtype)
        for k, wind_all in enumerate(winds):
            wind = wind_all[lo : lo + depth]
            high = wind.astype(out_ref.dtype)
            low = (wind - high.astype(jnp.float32)).astype(out_ref.dtype)
            out_ref[local_bins + k] = high
            out_ref[local_bins + 2 + k] = low


def rims(bin_mass, wind_east, wind_north, terrain_height, depth):
    local_bins, width_x, width_z, width_y = bin_mass.shape
    shape = jax.ShapeDtypeStruct((local_bins + 4, depth, width_z, width_y), jnp.bfloat16)
    return pl.pallas_call(
        functools.partial(rim_kernel, depth),
        out_shape=(shape, shape),
    )(bin_mass, wind_east, wind_north, terrain_height)


def advect_kernel(weights, q_ref, left_ref, right_ref, *refs):
    left_winds, right_winds = refs[0:4], refs[4:8]
    wx_ref, wy_ref, out_ref, bottom_ref = refs[8:]
    depth = len(weights)
    width = q_ref.shape[1]

    def widened(ref):
        return ref[...].astype(jnp.float32)

    def winds(rows):
        return [widened(rows[k])[0] + widened(rows[k + 2])[0] for k in (0, 1)]

    (wx_left, wy_left), (wx_right, wy_right) = winds(left_winds), winds(right_winds)
    field = jnp.concatenate([widened(left_ref), q_ref[...], widened(right_ref)], axis=1)
    wx = jnp.concatenate([wx_left, wx_ref[...], wx_right], axis=0)
    wy = jnp.concatenate([wy_left, wy_ref[...], wy_right], axis=0)
    section = field
    for stage, weight_now in enumerate(weights, start=1):
        span = width + 2 * (depth - stage)
        center = section[:, 1 : 1 + span]
        west = section[:, 0:span]
        east = section[:, 2 : 2 + span]
        south = pltpu.roll(center, 1, 3)
        north = pltpu.roll(center, center.shape[3] - 1, 3)
        wind_a = wx[stage : stage + span]
        wind_b = wy[stage : stage + span]
        along_x = jnp.maximum(wind_a, 0.0) * (center - west) + jnp.minimum(wind_a, 0.0) * (east - center)
        along_y = jnp.maximum(wind_b, 0.0) * (center - south) + jnp.minimum(wind_b, 0.0) * (north - center)
        section = field[:, stage : stage + span] + weight_now * (-along_x - along_y)
    out_ref[...] = section
    bottom_ref[...] = section[:, :, :1]


def advect_kernel_call(bin_mass, wind_x, wind_y, section_weights, tie, raw_winds):
    local_bins, width_x, width_z, width_y = bin_mass.shape
    depth = len(section_weights)
    tiles = lax.axis_size("tiles")
    up = [(i, i + 1) for i in range(tiles - 1)]
    down = [(j, i) for i, j in up]

    left, right = (
        lax.ppermute(message, "tiles", pairs)
        for message, pairs in zip(rims(bin_mass, *raw_winds, depth), (up, down))
    )
    left, tie = lax.optimization_barrier((left, tie))
    block = max(d for d in range(1, 34) if local_bins % d == 0)
    rim_spec = pl.BlockSpec((block, depth, width_z, width_y), lambda i: (i, 0, 0, 0))
    row_specs = [
        pl.BlockSpec((1, depth, width_z, width_y), lambda i, row=local_bins + k: (row, 0, 0, 0))
        for k in range(4)
    ]
    own_spec = pl.BlockSpec((block, width_x, width_z, width_y), lambda i: (i, 0, 0, 0))
    wind_spec = pl.BlockSpec(wind_x.shape, lambda i: (0, 0, 0))
    cells = local_bins * width_x * width_z * width_y
    return tie, pl.pallas_call(
        functools.partial(advect_kernel, section_weights),
        out_shape=(
            jax.ShapeDtypeStruct(bin_mass.shape, bin_mass.dtype),
            jax.ShapeDtypeStruct((local_bins, width_x, 1, width_y), bin_mass.dtype),
        ),
        grid=(local_bins // block,),
        in_specs=[own_spec, rim_spec, rim_spec] + row_specs + row_specs + [wind_spec, wind_spec],
        out_specs=(own_spec, pl.BlockSpec((block, width_x, 1, width_y), lambda i: (i, 0, 0, 0))),
        cost_estimate=pl.CostEstimate(flops=80 * cells, bytes_accessed=20 * cells, transcendentals=0),
    )(bin_mass, left, right, *([left] * 4), *([right] * 4), wind_x, wind_y)

def shifted(block, axis, distance):
    devices = range(lax.axis_size(axis))
    route = [(i - distance, i) for i in devices if i - distance in devices]
    return lax.ppermute(block, axis, route)


def tendency(center_cells, left_cells, right_cells, wind_x, wind_y):
    south_cells = jnp.roll(center_cells, 1, axis=3)
    north_cells = jnp.roll(center_cells, -1, axis=3)
    along_x = jnp.maximum(wind_x, 0.0) * (center_cells - left_cells) + jnp.minimum(wind_x, 0.0) * (
        right_cells - center_cells
    )
    along_y = jnp.maximum(wind_y, 0.0) * (center_cells - south_cells) + jnp.minimum(wind_y, 0.0) * (
        north_cells - center_cells
    )
    return -along_x - along_y


def coupling_table(bin_order, kernel_index, collision_kernels):
    class_count = kernel_index.shape[0]
    table_count = collision_kernels.shape[0]
    class_bins = collision_kernels.shape[1]
    bin_class = bin_order // class_bins
    bin_within = bin_order % class_bins
    kernel_pick = (kernel_index[:, :, None] == lax.iota(jnp.int32, table_count)).astype(jnp.float32)
    block_table = jnp.einsum(
        "ack,kmn->acmn", kernel_pick, collision_kernels.astype(jnp.float32), precision=highest
    )
    class_hot = (bin_class[:, None] == lax.iota(jnp.int32, class_count)).astype(jnp.float32)
    within_hot = (bin_within[:, None] == lax.iota(jnp.int32, class_bins)).astype(jnp.float32)
    row_table = jnp.einsum("bm,acmn->bacn", within_hot, block_table, precision=highest)
    row_table = jnp.einsum("ba,bacn->bcn", class_hot, row_table, precision=highest)
    coupling = jnp.einsum("bcn,dc,dn->bd", row_table, class_hot, within_hot, precision=highest)
    same_class = jnp.dot(class_hot, class_hot.T, precision=highest)
    return jnp.concatenate([coupling, same_class], axis=0).astype(jnp.bfloat16)


def collide(table, first, tie=None):
    all_bins = table.shape[1]
    iterate = first
    for substep in range(SUB):
        if tie is not None and substep == SUB // 2:
            iterate, tie = lax.optimization_barrier((iterate, tie))
        products = jnp.dot(table, iterate.astype(jnp.bfloat16), preferred_element_type=jnp.float32)
        iterate = iterate + collision_rate * products[all_bins:] * products[:all_bins]
    change = (iterate - first).astype(jnp.bfloat16)
    return change if tie is None else (change, tie)


def spread_collision(grown, bin_order, kernel_index, collision_kernels):
    local_bins, width_x, width_z, width_y = grown.shape
    table = coupling_table(bin_order, kernel_index, collision_kernels)
    all_bins = table.shape[1]
    start = grown.astype(jnp.bfloat16).reshape(local_bins, width_x, width_z * width_y)
    cell_block = lax.all_to_all(start, "bins", split_axis=2, concat_axis=0, tiled=True)
    block_shape = cell_block.shape
    first = cell_block.reshape(all_bins, -1).astype(jnp.float32)
    change = collide(table, first).reshape(block_shape)
    change = lax.all_to_all(change, "bins", split_axis=0, concat_axis=2, tiled=True)
    return change.reshape(local_bins, width_x, width_z, width_y).astype(jnp.float32)


def paired_table(bin_order, kernel_index, collision_kernels):
    local_bins = bin_order.shape[0] // 2
    me = lax.axis_index("bins")
    order = lax.dynamic_slice_in_dim(
        jnp.concatenate([bin_order, bin_order]), me * local_bins, 2 * local_bins
    )
    return coupling_table(order, kernel_index, collision_kernels)


def paired_collision(grown, table):
    local_bins, width_x, width_z, width_y = grown.shape
    swap = [(0, 1), (1, 0)]
    me = lax.axis_index("bins")
    halves = grown.astype(jnp.bfloat16).reshape(local_bins, 2, width_x // 2, width_z, width_y)
    own = lax.dynamic_index_in_dim(halves, me, axis=1, keepdims=False)
    away = lax.dynamic_index_in_dim(halves, 1 - me, axis=1, keepdims=False)
    kept, returned = [], []
    for chunk in range(width_x // 2):
        arrived = lax.ppermute(away[:, chunk], "bins", swap)
        first = jnp.concatenate([own[:, chunk], arrived], axis=0).reshape(2 * local_bins, -1).astype(jnp.float32)
        if returned:
            change, returned[-1] = collide(table, first, returned[-1])
        else:
            change = collide(table, first)
        change = change.reshape(2 * local_bins, width_z, width_y)
        returned.append(lax.ppermute(change[local_bins:], "bins", swap))
        kept.append(change[:local_bins])
    pair = jnp.stack([jnp.stack(kept, axis=1), jnp.stack(returned, axis=1)], axis=1)
    pair = jnp.where(me == 0, pair, pair[:, ::-1])
    return pair.reshape(local_bins, width_x, width_z, width_y).astype(jnp.float32)


def body(
    bin_mass,
    wind_east,
    wind_north,
    supersaturation,
    potential_temp,
    terrain_height,
    fall_speed,
    growth_rate,
    latent_factor,
    bin_order,
    kernel_index,
    collision_kernels,
):
    local_bins, width_x, width_z, width_y = bin_mass.shape
    levels = lax.axis_index("vert") * width_z + lax.iota(jnp.int32, width_z)
    open_cells = (levels[None, :, None] >= terrain_height[:, None, :]).astype(jnp.float32)
    wind_x = wind_east * open_cells
    wind_y = wind_north * open_cells
    section_weights = (1.0 / 3.0, 0.5, 1.0)
    paired = lax.axis_size("bins") == 2 and width_x % 2 == 0
    table = paired_table(bin_order, kernel_index, collision_kernels) if paired else None
    if width_x >= len(section_weights):
        table, (section_field, bottom) = advect_kernel_call(
            bin_mass, wind_x, wind_y, section_weights, table, (wind_east, wind_north, terrain_height)
        )
    else:
        section_field = bin_mass
        for weight_now in section_weights:
            extended = extended_2(section_field, (("tiles", 1),), 1, jnp.bfloat16)
            section_field = bin_mass + weight_now * tendency(
                extended[:, 1:-1], extended[:, :-2], extended[:, 2:], wind_x, wind_y
            )
        bottom = section_field[:, :, :1, :]
    rim_above = shifted(bottom, "vert", -1)
    from_above = jnp.concatenate([section_field[:, :, 1:], rim_above], axis=2)
    speed = fall_speed[:, None, None, None]
    settled = (1.0 - speed) * section_field + speed * from_above
    growth = growth_rate[:, None, None, None]
    partial = (
        jnp.sum(growth * settled, axis=0),
        jnp.sum(latent_factor[:, None, None, None] * growth * settled, axis=0),
    )
    bin_devices = lax.axis_size("bins")
    if bin_devices == 2:
        swap = [(0, 1), (1, 0)]
        other = lax.ppermute(jnp.stack(partial), "bins", swap)
        uptake, heating = partial[0] + other[0], partial[1] + other[1]
    else:
        uptake, heating = lax.psum(partial, "bins")
    midway = supersaturation * jnp.exp(-0.5 * condense_rate * uptake)
    grown = settled * (1.0 + growth_gain * growth * midway)
    temp_next = potential_temp + heating_gain * midway * heating
    vapor_next = supersaturation * jnp.exp(-condense_rate * uptake)
    if paired:
        change = paired_collision(grown, table)
    else:
        change = spread_collision(grown, bin_order, kernel_index, collision_kernels)
    mass_next = (grown + change) * open_cells
    return (mass_next, temp_next, vapor_next)


def solution(mesh):
    return jax.shard_map(
        body,
        mesh=mesh,
        in_specs=(
            P("bins", ("groups", "tiles"), "vert", None),
            P(("groups", "tiles"), "vert", None),
            P(("groups", "tiles"), "vert", None),
            P(("groups", "tiles"), "vert", None),
            P(("groups", "tiles"), "vert", None),
            P(("groups", "tiles"), None),
            P("bins"),
            P("bins"),
            P("bins"),
            P(),
            P(),
            P(),
        ),
        out_specs=(
            P("bins", ("groups", "tiles"), "vert", None),
            P(("groups", "tiles"), "vert", None),
            P(("groups", "tiles"), "vert", None),
        ),
        check_vma=False,
    )
```

```python
import functools

import jax
import jax.numpy as jnp
from jax import lax
from jax.experimental import pallas as pl
from jax.experimental.pallas import tpu as pltpu
from jax.sharding import PartitionSpec as P

SUB = 8


collision_rate = 0.001
condense_rate = 0.02
heating_gain = 0.03
growth_gain = 0.5
highest = lax.Precision.HIGHEST


def extended_2(array, sides, width, link=jnp.float32):
    for axis, dim in sides:
        size, length = (lax.axis_size(axis), array.shape[dim])
        up = [(i, (i + 1) % size) for i in range(size - 1)]
        down = [(j, i) for i, j in up]
        last = lax.slice_in_dim(array, length - width, length, axis=dim)
        first = lax.slice_in_dim(array, 0, width, axis=dim)
        before = lax.ppermute(last.astype(link), axis, up).astype(array.dtype)
        after = lax.ppermute(first.astype(link), axis, down).astype(array.dtype)
        array = jnp.concatenate([before, array, after], axis=dim)
    return array


def rim_kernel(depth, q_ref, east_ref, north_ref, terrain_ref, left_ref, right_ref):
    local_bins, width_x, width_z = q_ref.shape[:3]
    levels = lax.axis_index("vert") * width_z + lax.broadcasted_iota(jnp.int32, east_ref.shape, 1)
    open_cells = (levels >= terrain_ref[...][:, None, :]).astype(jnp.float32)
    winds = (east_ref[...] * open_cells, north_ref[...] * open_cells)
    for out_ref, lo in ((left_ref, width_x - depth), (right_ref, 0)):
        out_ref[0:local_bins] = q_ref[:, lo : lo + depth].astype(out_ref.dtype)
        for k, wind_all in enumerate(winds):
            wind = wind_all[lo : lo + depth]
            high = wind.astype(out_ref.dtype)
            low = (wind - high.astype(jnp.float32)).astype(out_ref.dtype)
            out_ref[local_bins + k] = high
            out_ref[local_bins + 2 + k] = low


def rims(bin_mass, wind_east, wind_north, terrain_height, depth):
    local_bins, width_x, width_z, width_y = bin_mass.shape
    shape = jax.ShapeDtypeStruct((local_bins + 4, depth, width_z, width_y), jnp.bfloat16)
    return pl.pallas_call(
        functools.partial(rim_kernel, depth),
        out_shape=(shape, shape),
    )(bin_mass, wind_east, wind_north, terrain_height)


def advect_kernel(weights, q_ref, left_ref, right_ref, *refs):
    left_winds, right_winds = refs[0:4], refs[4:8]
    wx_ref, wy_ref, out_ref, bottom_ref = refs[8:]
    depth = len(weights)
    width = q_ref.shape[1]

    def widened(ref):
        return ref[...].astype(jnp.float32)

    def winds(rows):
        return [widened(rows[k])[0] + widened(rows[k + 2])[0] for k in (0, 1)]

    (wx_left, wy_left), (wx_right, wy_right) = winds(left_winds), winds(right_winds)
    field = jnp.concatenate([widened(left_ref), q_ref[...], widened(right_ref)], axis=1)
    wx = jnp.concatenate([wx_left, wx_ref[...], wx_right], axis=0)
    wy = jnp.concatenate([wy_left, wy_ref[...], wy_right], axis=0)
    section = field
    for stage, weight_now in enumerate(weights, start=1):
        span = width + 2 * (depth - stage)
        center = section[:, 1 : 1 + span]
        west = section[:, 0:span]
        east = section[:, 2 : 2 + span]
        south = pltpu.roll(center, 1, 3)
        north = pltpu.roll(center, center.shape[3] - 1, 3)
        wind_a = wx[stage : stage + span]
        wind_b = wy[stage : stage + span]
        along_x = jnp.maximum(wind_a, 0.0) * (center - west) + jnp.minimum(wind_a, 0.0) * (east - center)
        along_y = jnp.maximum(wind_b, 0.0) * (center - south) + jnp.minimum(wind_b, 0.0) * (north - center)
        section = field[:, stage : stage + span] + weight_now * (-along_x - along_y)
    out_ref[...] = section
    bottom_ref[...] = section[:, :, :1]


def advect_kernel_call(bin_mass, wind_x, wind_y, section_weights, tie, raw_winds):
    local_bins, width_x, width_z, width_y = bin_mass.shape
    depth = len(section_weights)
    tiles = lax.axis_size("tiles")
    up = [(i, i + 1) for i in range(tiles - 1)]
    down = [(j, i) for i, j in up]

    left, right = (
        lax.ppermute(message, "tiles", pairs)
        for message, pairs in zip(rims(bin_mass, *raw_winds, depth), (up, down))
    )
    left, tie = lax.optimization_barrier((left, tie))
    block = max(d for d in range(1, 34) if local_bins % d == 0)
    rim_spec = pl.BlockSpec((block, depth, width_z, width_y), lambda i: (i, 0, 0, 0))
    row_specs = [
        pl.BlockSpec((1, depth, width_z, width_y), lambda i, row=local_bins + k: (row, 0, 0, 0))
        for k in range(4)
    ]
    own_spec = pl.BlockSpec((block, width_x, width_z, width_y), lambda i: (i, 0, 0, 0))
    wind_spec = pl.BlockSpec(wind_x.shape, lambda i: (0, 0, 0))
    cells = local_bins * width_x * width_z * width_y
    return tie, pl.pallas_call(
        functools.partial(advect_kernel, section_weights),
        out_shape=(
            jax.ShapeDtypeStruct(bin_mass.shape, bin_mass.dtype),
            jax.ShapeDtypeStruct((local_bins, width_x, 1, width_y), bin_mass.dtype),
        ),
        grid=(local_bins // block,),
        in_specs=[own_spec, rim_spec, rim_spec] + row_specs + row_specs + [wind_spec, wind_spec],
        out_specs=(own_spec, pl.BlockSpec((block, width_x, 1, width_y), lambda i: (i, 0, 0, 0))),
        cost_estimate=pl.CostEstimate(flops=80 * cells, bytes_accessed=20 * cells, transcendentals=0),
    )(bin_mass, left, right, *([left] * 4), *([right] * 4), wind_x, wind_y)

def shifted(block, axis, distance):
    devices = range(lax.axis_size(axis))
    route = [(i - distance, i) for i in devices if i - distance in devices]
    return lax.ppermute(block, axis, route)


def tendency(center_cells, left_cells, right_cells, wind_x, wind_y):
    south_cells = jnp.roll(center_cells, 1, axis=3)
    north_cells = jnp.roll(center_cells, -1, axis=3)
    along_x = jnp.maximum(wind_x, 0.0) * (center_cells - left_cells) + jnp.minimum(wind_x, 0.0) * (
        right_cells - center_cells
    )
    along_y = jnp.maximum(wind_y, 0.0) * (center_cells - south_cells) + jnp.minimum(wind_y, 0.0) * (
        north_cells - center_cells
    )
    return -along_x - along_y


def coupling_table(bin_order, kernel_index, collision_kernels):
    class_count = kernel_index.shape[0]
    table_count = collision_kernels.shape[0]
    class_bins = collision_kernels.shape[1]
    bin_class = bin_order // class_bins
    bin_within = bin_order % class_bins
    kernel_pick = (kernel_index[:, :, None] == lax.iota(jnp.int32, table_count)).astype(jnp.float32)
    block_table = jnp.einsum(
        "ack,kmn->acmn", kernel_pick, collision_kernels.astype(jnp.float32), precision=highest
    )
    class_hot = (bin_class[:, None] == lax.iota(jnp.int32, class_count)).astype(jnp.float32)
    within_hot = (bin_within[:, None] == lax.iota(jnp.int32, class_bins)).astype(jnp.float32)
    row_table = jnp.einsum("bm,acmn->bacn", within_hot, block_table, precision=highest)
    row_table = jnp.einsum("ba,bacn->bcn", class_hot, row_table, precision=highest)
    coupling = jnp.einsum("bcn,dc,dn->bd", row_table, class_hot, within_hot, precision=highest)
    same_class = jnp.dot(class_hot, class_hot.T, precision=highest)
    return jnp.concatenate([coupling, same_class], axis=0).astype(jnp.bfloat16)


def collide(table, first, tie=None):
    all_bins = table.shape[1]
    iterate = first
    for substep in range(SUB):
        if tie is not None and substep == SUB // 2:
            iterate, tie = lax.optimization_barrier((iterate, tie))
        products = jnp.dot(table, iterate.astype(jnp.bfloat16), preferred_element_type=jnp.float32)
        iterate = iterate + collision_rate * products[all_bins:] * products[:all_bins]
    change = (iterate - first).astype(jnp.bfloat16)
    return change if tie is None else (change, tie)


def spread_collision(grown, bin_order, kernel_index, collision_kernels):
    local_bins, width_x, width_z, width_y = grown.shape
    table = coupling_table(bin_order, kernel_index, collision_kernels)
    all_bins = table.shape[1]
    start = grown.astype(jnp.bfloat16).reshape(local_bins, width_x, width_z * width_y)
    cell_block = lax.all_to_all(start, "bins", split_axis=2, concat_axis=0, tiled=True)
    block_shape = cell_block.shape
    first = cell_block.reshape(all_bins, -1).astype(jnp.float32)
    change = collide(table, first).reshape(block_shape)
    change = lax.all_to_all(change, "bins", split_axis=0, concat_axis=2, tiled=True)
    return change.reshape(local_bins, width_x, width_z, width_y).astype(jnp.float32)


def paired_table(bin_order, kernel_index, collision_kernels):
    local_bins = bin_order.shape[0] // 2
    me = lax.axis_index("bins")
    order = lax.dynamic_slice_in_dim(
        jnp.concatenate([bin_order, bin_order]), me * local_bins, 2 * local_bins
    )
    return coupling_table(order, kernel_index, collision_kernels)


def paired_collision(grown, table, open_cells):
    local_bins, width_x, width_z, width_y = grown.shape
    swap = [(0, 1), (1, 0)]
    me = lax.axis_index("bins")
    halves = grown.astype(jnp.bfloat16).reshape(local_bins, 2, width_x // 2, width_z, width_y)
    own = lax.dynamic_index_in_dim(halves, me, axis=1, keepdims=False)
    away = lax.dynamic_index_in_dim(halves, 1 - me, axis=1, keepdims=False)
    kept, returned = [], []
    for chunk in range(width_x // 2):
        arrived = lax.ppermute(away[:, chunk], "bins", swap)
        first = jnp.concatenate([own[:, chunk], arrived], axis=0).reshape(2 * local_bins, -1).astype(jnp.float32)
        if returned:
            change, returned[-1] = collide(table, first, returned[-1])
        else:
            change = collide(table, first)
        change = change.reshape(2 * local_bins, width_z, width_y)
        returned.append(lax.ppermute(change[local_bins:], "bins", swap))
        kept.append(change[:local_bins])
    hx = width_x // 2
    waiting = returned[-1]
    returned[-1] = jnp.zeros_like(waiting)
    pair = jnp.stack([jnp.stack(kept, axis=1), jnp.stack(returned, axis=1)], axis=1)
    pair = jnp.where(me == 0, pair, pair[:, ::-1])
    change = pair.reshape(local_bins, width_x, width_z, width_y).astype(jnp.float32)
    early = (grown + change) * open_cells
    last = (1 - me) * hx + hx - 1
    late = (
        lax.dynamic_index_in_dim(grown, last, axis=1) + waiting[:, None].astype(jnp.float32)
    ) * lax.dynamic_index_in_dim(open_cells, last, axis=0)
    return lax.dynamic_update_slice_in_dim(early, late, last, axis=1)


def body(
    bin_mass,
    wind_east,
    wind_north,
    supersaturation,
    potential_temp,
    terrain_height,
    fall_speed,
    growth_rate,
    latent_factor,
    bin_order,
    kernel_index,
    collision_kernels,
):
    local_bins, width_x, width_z, width_y = bin_mass.shape
    levels = lax.axis_index("vert") * width_z + lax.iota(jnp.int32, width_z)
    open_cells = (levels[None, :, None] >= terrain_height[:, None, :]).astype(jnp.float32)
    wind_x = wind_east * open_cells
    wind_y = wind_north * open_cells
    section_weights = (1.0 / 3.0, 0.5, 1.0)
    paired = lax.axis_size("bins") == 2 and width_x % 2 == 0
    table = paired_table(bin_order, kernel_index, collision_kernels) if paired else None
    if width_x >= len(section_weights):
        table, (section_field, bottom) = advect_kernel_call(
            bin_mass, wind_x, wind_y, section_weights, table, (wind_east, wind_north, terrain_height)
        )
    else:
        section_field = bin_mass
        for weight_now in section_weights:
            extended = extended_2(section_field, (("tiles", 1),), 1, jnp.bfloat16)
            section_field = bin_mass + weight_now * tendency(
                extended[:, 1:-1], extended[:, :-2], extended[:, 2:], wind_x, wind_y
            )
        bottom = section_field[:, :, :1, :]
    rim_above = shifted(bottom, "vert", -1)
    from_above = jnp.concatenate([section_field[:, :, 1:], rim_above], axis=2)
    speed = fall_speed[:, None, None, None]
    settled = (1.0 - speed) * section_field + speed * from_above
    growth = growth_rate[:, None, None, None]
    partial = (
        jnp.sum(growth * settled, axis=0),
        jnp.sum(latent_factor[:, None, None, None] * growth * settled, axis=0),
    )
    bin_devices = lax.axis_size("bins")
    if bin_devices == 2:
        swap = [(0, 1), (1, 0)]
        other = lax.ppermute(jnp.stack(partial), "bins", swap)
        uptake, heating = partial[0] + other[0], partial[1] + other[1]
    else:
        uptake, heating = lax.psum(partial, "bins")
    midway = supersaturation * jnp.exp(-0.5 * condense_rate * uptake)
    grown = settled * (1.0 + growth_gain * growth * midway)
    temp_next = potential_temp + heating_gain * midway * heating
    vapor_next = supersaturation * jnp.exp(-condense_rate * uptake)
    if paired:
        mass_next = paired_collision(grown, table, open_cells)
    else:
        change = spread_collision(grown, bin_order, kernel_index, collision_kernels)
        mass_next = (grown + change) * open_cells
    return (mass_next, temp_next, vapor_next)


def solution(mesh):
    return jax.shard_map(
        body,
        mesh=mesh,
        in_specs=(
            P("bins", ("groups", "tiles"), "vert", None),
            P(("groups", "tiles"), "vert", None),
            P(("groups", "tiles"), "vert", None),
            P(("groups", "tiles"), "vert", None),
            P(("groups", "tiles"), "vert", None),
            P(("groups", "tiles"), None),
            P("bins"),
            P("bins"),
            P("bins"),
            P(),
            P(),
            P(),
        ),
        out_specs=(
            P("bins", ("groups", "tiles"), "vert", None),
            P(("groups", "tiles"), "vert", None),
            P(("groups", "tiles"), "vert", None),
        ),
        check_vma=False,
    )
```
